32 devices in a mesh: seq: 8 (over z, y), tp: 4 (over x, core).
Axes of the slice: x: 2, y: 2, z: 4, core: 2. Of those that a mesh axis runs over, the one named last changes fastest.
Arguments:
- new_query: bfloat16 [8, 3584], P('seq', 'tp'), may hold values from -360 to 360
- new_key: bfloat16 [8, 512], P('seq', 'tp'), may hold values from -6 to 6
- new_value: bfloat16 [8, 512], P('seq', 'tp'), may hold values from -6 to 6
- cache_keys: bfloat16 [8, 4096, 512], P('seq', None, 'tp'), may hold values from -6 to 6
- cache_values: bfloat16 [8, 4096, 512], P('seq', None, 'tp'), may hold values from -6 to 6
- cache_length: int32 [8], P('seq'), may hold values from 1 to 4096, 16384 in all
- dealing: int32 [8], replicated, may hold values from 0 to 7, each once
- out_weight: bfloat16 [3584, 3584], P('tp', 'seq'), may hold values from -0.09375 to 0.09375
- stretch_query: bfloat16 [3, 256, 3584], P(None, 'seq', 'tp'), may hold values from -360 to 360
- stretch_key: bfloat16 [3, 256, 512], P(None, 'seq', 'tp'), may hold values from -6 to 6
- stretch_value: bfloat16 [3, 256, 512], P(None, 'seq', 'tp'), may hold values from -6 to 6
- prior_keys: bfloat16 [3, 8192, 512], P(None, 'seq', 'tp'), may hold values from -6 to 6
- prior_values: bfloat16 [3, 8192, 512], P(None, 'seq', 'tp'), may hold values from -6 to 6
- stretch_start: int32 [3], replicated, may hold values from 1 to 8192, 16384 in all
Outputs:
- decode_mixed: bfloat16 [8, 3584], P('tp', 'seq')
- stretch_out: bfloat16 [3, 256, 3584], P(None, 'seq', 'tp')
The draws below stay inside these ranges and needn't reach their ends.
Inputs may be any that keep to these rules, and one draw needn't show every extreme that they name: dealing[a] is the cache slot of the decode request that arrives a-th; every slot appears once. `cache_length`: cached positions in use of each decode slot; one slot is full. `stretch_start`: cached positions of each stretch's request that precede the stretch; one request's cache is full.
All inputs are finite; a program needn't handle non-finite values. No bound on the sum of `cache_length` on one device may be relied on, other than what follows from the above.
Results may differ from the reference program's by a relative error of at most 0.0051.
Values may be sent and summed in bfloat16 or wider, within the bound.
No kernel may reach another device: no remote copies, remote signals or barrier semaphores. Data moves between devices by JAX's collectives and lax.ppermute only.
A program may use at most 64 MiB of HBM per device.

```python
import math
import jax
import jax.numpy as jnp
import numpy as np
from jax import lax

D = 3584
H = 28
KVH = 4
HD = 128
PRE = 3
STRETCH = 256
MAXLEN_P = 8192
MAXLEN_D = 4096
DEC = 8


def query_draw(key, shape):
    normals = jnp.clip(jax.random.normal(key, shape, jnp.float32), -6.0, 6.0) * 3.0
    return normals.astype(jnp.bfloat16)


def draw_new_query(key, part):
    return query_draw(key, (DEC, H * HD))


def draw_stretch_query(key, part):
    return query_draw(key, (PRE, STRETCH, H * HD))


def block_scale(stream_key, shape, shards, smallest, high):
    loudness, own = 1.0, jax.random.fold_in(stream_key, 6)
    for dim, parts in shards:
        steps = jnp.exp(jax.random.uniform(jax.random.fold_in(own, dim), (parts,), jnp.float32, smallest / len(shards), high / len(shards)))
        loudness = loudness * jnp.repeat(steps, shape[dim] // parts).reshape([-1 if axis == dim else 1 for axis in range(len(shape))])
    return loudness


def profile(number_of, total, bound, slope):
    loads = [(1 << 20) // math.isqrt(rank ** slope) + 1 for rank in range(2, number_of + 1)]
    spare, given = total - bound - (number_of - 1), [1] * (number_of - 1)
    while spare > 0:
        movable = [i for i in range(number_of - 1) if given[i] < bound]
        whole, budget = sum([loads[i] for i in movable]), spare
        for i in movable:
            more = min(bound - given[i], max(1, budget * loads[i] // whole), spare)
            given[i] = given[i] + more
            spare = spare - more
    return np.array([bound] + given)


def ragged_sizes(stream_key, count, total, most, lean):
    if count == 2:
        one = jax.random.randint(stream_key, (), max(1, total - most), min(most, total - 1) + 1)
        return jnp.stack([one, total - one])
    sizes = jnp.asarray(profile(count, total, most, lean), jnp.int32)
    pairs = (count - 1) // 2
    donor, receiver = sizes[1:1 + 2 * pairs:2], sizes[2:2 + 2 * pairs:2]
    slack = jnp.minimum(donor - 1, most - receiver)
    moved = jax.random.randint(jax.random.fold_in(stream_key, 1), (pairs,), 0, 1 << 20) % (slack + 1)
    sizes = sizes.at[1:1 + 2 * pairs:2].set(donor - moved).at[2:2 + 2 * pairs:2].set(receiver + moved)
    return sizes[jax.random.permutation(jax.random.fold_in(stream_key, 2), count)]


def gaussian(rng, extent, spread, most, shards=(), kind=jnp.bfloat16):
    loudness = block_scale(rng, extent, shards, -0.22, 0.18) if shards else 1.0
    drawn = jax.random.normal(rng, extent, jnp.float32) * spread * loudness
    return jnp.minimum(jnp.maximum(drawn, -most), most).astype(kind)


def setup_inputs(seed: int = 0) -> dict:
    splits = jax.random.split(jax.random.key(seed), 15)
    new_query = draw_new_query(jax.random.fold_in(splits[14], 71), 0)
    new_key = gaussian(splits[1], (DEC, KVH * HD), 1.0, 6.0, ((0, 8), (1, 4)))
    new_value = gaussian(splits[2], (DEC, KVH * HD), 1.0, 6.0, ((0, 8), (1, 4)))
    cache_keys = gaussian(splits[3], (DEC, MAXLEN_D, KVH * HD), 1.0, 6.0, ((0, 8), (2, 4)))
    cache_values = gaussian(splits[4], (DEC, MAXLEN_D, KVH * HD), 1.0, 6.0, ((0, 8), (2, 4)))
    cache_length = ragged_sizes(splits[5], DEC, DEC * MAXLEN_D // 2, MAXLEN_D, 2).astype(jnp.int32)
    dealing = jax.random.permutation(splits[6], DEC).astype(jnp.int32)
    out_weight = gaussian(splits[7], (H * HD, D), (H * HD) ** -0.5, 0.09375, ((0, 4), (1, 8)))
    stretch_query = draw_stretch_query(jax.random.fold_in(splits[14], 71), 0)
    stretch_key = gaussian(splits[9], (PRE, STRETCH, KVH * HD), 1.0, 6.0, ((1, 8), (2, 4)))
    stretch_value = gaussian(splits[10], (PRE, STRETCH, KVH * HD), 1.0, 6.0, ((1, 8), (2, 4)))
    prior_keys = gaussian(splits[11], (PRE, MAXLEN_P, KVH * HD), 1.0, 6.0, ((1, 8), (2, 4)))
    prior_values = gaussian(splits[12], (PRE, MAXLEN_P, KVH * HD), 1.0, 6.0, ((1, 8), (2, 4)))
    stretch_start = ragged_sizes(splits[13], PRE, 2 * MAXLEN_P, MAXLEN_P, 2).astype(jnp.int32)
    return dict(new_query=new_query, new_key=new_key, new_value=new_value, cache_keys=cache_keys, cache_values=cache_values, cache_length=cache_length, dealing=dealing, out_weight=out_weight, stretch_query=stretch_query, stretch_key=stretch_key, stretch_value=stretch_value, prior_keys=prior_keys, prior_values=prior_values, stretch_start=stretch_start)


NEG_FILL = -1e+30

def attend(queries, keys, values, visible):
    factor = 1.0 / math.sqrt(queries.shape[-1])
    scores = jnp.dot(queries, keys.T, preferred_element_type=jnp.float32) * factor
    scores = jnp.where(visible, scores, NEG_FILL)
    row_top = lax.optimization_barrier(jnp.max(scores, axis=1, keepdims=True))
    weights = jnp.where(visible, jnp.exp(scores - row_top), 0.0)
    weight_sum = lax.optimization_barrier(jnp.sum(weights, axis=1, keepdims=True))
    numerator = jnp.dot(weights.astype(jnp.bfloat16), values, preferred_element_type=jnp.float32)
    return (numerator / weight_sum).astype(jnp.bfloat16)

def reference(new_query, new_key, new_value, cache_keys, cache_values, cache_length, dealing, out_weight, stretch_query, stretch_key, stretch_value, prior_keys, prior_values, stretch_start):
    group_size = H // KVH
    cache_span = cache_keys.shape[1]
    cache_pos = jnp.arange(cache_span, dtype=jnp.int32)

    def decode_one(request):
        query_row, own_key, own_value, cache_slot = request
        cached_keys = cache_keys[cache_slot]
        cached_values = cache_values[cache_slot]
        length = cache_length[cache_slot]
        visible = jnp.concatenate([cache_pos < length, jnp.ones((1,), dtype=jnp.bool_)])
        visible = jnp.broadcast_to(visible[None, :], (group_size, cache_span + 1))
        per_head = []
        for kv_head in range(KVH):
            offset = kv_head * HD
            key_all = jnp.concatenate([cached_keys[:, offset:offset + HD], own_key[None, offset:offset + HD]], axis=0)
            value_all = jnp.concatenate([cached_values[:, offset:offset + HD], own_value[None, offset:offset + HD]], axis=0)
            query_block = query_row[offset * group_size:(offset + HD) * group_size].reshape(group_size, HD)
            per_head.append(attend(query_block, key_all, value_all, visible).reshape(group_size * HD))
        return jnp.concatenate(per_head)
    attended = lax.map(decode_one, (new_query, new_key, new_value, dealing))
    decode_mixed = jnp.dot(attended, out_weight, preferred_element_type=jnp.float32).astype(jnp.bfloat16)
    stretch_len = stretch_query.shape[1]
    prior_span = prior_keys.shape[1]
    prior_pos = jnp.arange(prior_span, dtype=jnp.int32)
    row_count = stretch_len * group_size
    token_row = jnp.arange(row_count, dtype=jnp.int32) // group_size
    stretch_pos = jnp.arange(stretch_len, dtype=jnp.int32)
    causal = stretch_pos[None, :] <= token_row[:, None]
    outputs = []
    for stretch_index in range(PRE):
        prior_visible = jnp.broadcast_to((prior_pos < stretch_start[stretch_index])[None, :], (row_count, prior_span))
        visible = jnp.concatenate([prior_visible, causal], axis=1)
        per_head = []
        for kv_head in range(KVH):
            offset = kv_head * HD
            key_all = jnp.concatenate([prior_keys[stretch_index][:, offset:offset + HD], stretch_key[stretch_index][:, offset:offset + HD]], axis=0)
            value_all = jnp.concatenate([prior_values[stretch_index][:, offset:offset + HD], stretch_value[stretch_index][:, offset:offset + HD]], axis=0)
            query_block = stretch_query[stretch_index][:, offset * group_size:(offset + HD) * group_size].reshape(row_count, HD)
            per_head.append(attend(query_block, key_all, value_all, visible).reshape(stretch_len, group_size * HD))
        outputs.append(jnp.concatenate(per_head, axis=1))
    stretch_out = jnp.stack(outputs)
    return (decode_mixed, stretch_out)
```

```python
import math

import jax
import jax.numpy as jnp
from jax import lax
from jax.sharding import PartitionSpec as P

NEG_FILL = -1e30


def partial_attend(queries, keys, values, visible):
    factor = 1.0 / math.sqrt(queries.shape[-1])
    scores = jnp.dot(queries, keys.T, preferred_element_type=jnp.float32) * factor
    scores = jnp.where(visible, scores, NEG_FILL)
    row_top = jnp.max(scores, axis=1)
    weights = jnp.where(visible, jnp.exp(scores - row_top[:, None]), 0.0)
    weight_sum = jnp.sum(weights, axis=1)
    numerator = jnp.dot(weights.astype(jnp.bfloat16), values, preferred_element_type=jnp.float32)
    return (row_top, weight_sum, numerator)


def body(
    new_query,
    new_key,
    new_value,
    cache_keys,
    cache_values,
    cache_length,
    dealing,
    out_weight,
    stretch_query,
    stretch_key,
    stretch_value,
    prior_keys,
    prior_values,
    stretch_start,
):
    head_size = cache_keys.shape[2]
    group_size = new_query.shape[1] // head_size
    local_dec = new_query.shape[0]
    seq_rank = lax.axis_index("seq")
    seq_count = lax.axis_size("seq")
    total_dec = local_dec * seq_count
    stretch_count, local_tok, query_width = stretch_query.shape
    key_width = stretch_key.shape[2]
    stretch_rows = stretch_count * local_tok

    stretch_pack = jnp.concatenate([stretch_query, stretch_key, stretch_value], axis=2).reshape(
        stretch_rows, query_width + 2 * key_width
    )
    decode_pack = jnp.concatenate([new_query, new_key, new_value], axis=1)
    gathered = lax.all_gather(
        jnp.concatenate([stretch_pack, decode_pack], axis=0), "seq", axis=0, tiled=False
    )

    decode_part = gathered[:, stretch_rows:, :].reshape(total_dec, query_width + 2 * key_width)
    every_query = decode_part[:, :query_width]
    every_key = decode_part[:, query_width : query_width + key_width]
    every_value = decode_part[:, query_width + key_width :]
    slot_ids = seq_rank * local_dec + jnp.arange(local_dec, dtype=jnp.int32)
    arrival_ids = jnp.arange(total_dec, dtype=jnp.int32)
    sources = jnp.sum(
        jnp.where(dealing[None, :] == slot_ids[:, None], arrival_ids[None, :], 0), axis=1
    )
    home_query = jnp.take(every_query, sources, axis=0)
    home_key = jnp.take(every_key, sources, axis=0)
    home_value = jnp.take(every_value, sources, axis=0)
    cache_span = cache_keys.shape[1]
    cache_pos = jnp.arange(cache_span, dtype=jnp.int32)

    def decode_slot(query_row, own_key, own_value, cached_keys, cached_values, length):
        key_all = jnp.concatenate([cached_keys, own_key[None, :]], axis=0)
        value_all = jnp.concatenate([cached_values, own_value[None, :]], axis=0)
        visible = jnp.concatenate([cache_pos < length, jnp.ones((1,), dtype=jnp.bool_)])
        visible = jnp.broadcast_to(visible[None, :], (group_size, cache_span + 1))
        row_top, weight_sum, numerator = partial_attend(
            query_row.reshape(group_size, head_size), key_all, value_all, visible
        )
        return (
            (numerator / weight_sum[:, None]).astype(jnp.bfloat16).reshape(group_size * head_size)
        )

    home_out = jax.vmap(decode_slot)(
        home_query, home_key, home_value, cache_keys, cache_values, cache_length
    )

    prior_span = prior_keys.shape[1]
    rows_per_src = local_tok * group_size
    row_count = seq_count * rows_per_src
    prior_pos = seq_rank * prior_span + jnp.arange(prior_span, dtype=jnp.int32)
    stretch_part = gathered[:, :stretch_rows, :].reshape(
        seq_count, stretch_count, local_tok, query_width + 2 * key_width
    )
    numer_list, total_list, peak_list = ([], [], [])
    for stretch_index in range(stretch_count):
        queries_all = stretch_part[:, stretch_index, :, :query_width].reshape(row_count, head_size)
        prior_visible = jnp.broadcast_to(
            (prior_pos < stretch_start[stretch_index])[None, :], (row_count, prior_span)
        )

        def work_part():
            return partial_attend(
                queries_all, prior_keys[stretch_index], prior_values[stretch_index], prior_visible
            )

        def skip_part():
            return (
                jnp.full((row_count,), NEG_FILL, jnp.float32),
                jnp.zeros((row_count,), jnp.float32),
                jnp.zeros((row_count, head_size), jnp.float32),
            )

        pieces = lax.cond(
            seq_rank * prior_span < stretch_start[stretch_index], work_part, skip_part
        )
        peak_list.append(pieces[0].reshape(seq_count, rows_per_src))
        total_list.append(pieces[1].reshape(seq_count, rows_per_src))
        numer_list.append(pieces[2].reshape(seq_count, rows_per_src * head_size))

    dec_width = local_dec * group_size * head_size
    payload = jnp.concatenate(
        numer_list
        + total_list
        + peak_list
        + [
            jnp.broadcast_to(
                home_out.reshape(1, dec_width).astype(jnp.float32), (seq_count, dec_width)
            )
        ],
        axis=1,
    )
    received = lax.all_to_all(payload, "seq", 0, 0, tiled=True)
    numer_width = stretch_count * rows_per_src * head_size
    got_num = received[:, :numer_width].reshape(seq_count, stretch_count, local_tok, group_size, head_size)
    got_sum = received[:, numer_width : numer_width + stretch_count * rows_per_src].reshape(
        seq_count, stretch_count, local_tok, group_size
    )
    got_top = received[
        :, numer_width + stretch_count * rows_per_src : numer_width + 2 * stretch_count * rows_per_src
    ].reshape(seq_count, stretch_count, local_tok, group_size)
    all_out = (
        received[:, numer_width + 2 * stretch_count * rows_per_src :]
        .reshape(total_dec, group_size * head_size)
        .astype(jnp.bfloat16)
    )

    arrival_out = jnp.take(all_out, dealing, axis=0)
    arrival_terms = jnp.dot(arrival_out, out_weight, preferred_element_type=jnp.float32)
    decode_mixed = lax.psum_scatter(arrival_terms, "tp", scatter_dimension=0, tiled=True).astype(
        jnp.bfloat16
    )

    stretch_len = local_tok * seq_count
    local_rows = local_tok * group_size
    stretch_pos = jnp.arange(stretch_len, dtype=jnp.int32)
    own_token = seq_rank * local_tok + jnp.arange(local_rows, dtype=jnp.int32) // group_size
    causal = stretch_pos[None, :] <= own_token[:, None]
    self_tops, self_totals, self_numers = ([], [], [])
    for stretch_index in range(stretch_count):
        local_queries = stretch_query[stretch_index].reshape(local_rows, head_size)
        keys_all = stretch_part[:, stretch_index, :, query_width : query_width + key_width].reshape(
            stretch_len, key_width
        )
        values_all = stretch_part[:, stretch_index, :, query_width + key_width :].reshape(
            stretch_len, key_width
        )
        pieces = partial_attend(local_queries, keys_all, values_all, causal)
        self_tops.append(pieces[0].reshape(local_tok, group_size))
        self_totals.append(pieces[1].reshape(local_tok, group_size))
        self_numers.append(pieces[2].reshape(local_tok, group_size, head_size))
    self_top = jnp.stack(self_tops)
    self_sum = jnp.stack(self_totals)
    self_num = jnp.stack(self_numers)
    final_top = jnp.maximum(jnp.max(got_top, axis=0), self_top)
    part_factor = jnp.exp(got_top - final_top[None])
    self_factor = jnp.exp(self_top - final_top)
    total_sum = jnp.sum(got_sum * part_factor, axis=0) + self_sum * self_factor
    total_num = (
        jnp.sum(got_num * part_factor[..., None], axis=0) + self_num * self_factor[..., None]
    )
    stretch_out = (
        (total_num / total_sum[..., None])
        .astype(jnp.bfloat16)
        .reshape(stretch_count, local_tok, group_size * head_size)
    )
    return (decode_mixed, stretch_out)


def solution(mesh):
    return jax.shard_map(
        body,
        mesh=mesh,
        in_specs=(
            P("seq", "tp"),
            P("seq", "tp"),
            P("seq", "tp"),
            P("seq", None, "tp"),
            P("seq", None, "tp"),
            P("seq"),
            P(),
            P("tp", "seq"),
            P(None, "seq", "tp"),
            P(None, "seq", "tp"),
            P(None, "seq", "tp"),
            P(None, "seq", "tp"),
            P(None, "seq", "tp"),
            P(),
        ),
        out_specs=(P("tp", "seq"), P(None, "seq", "tp")),
        check_vma=False,
    )
```

```python
import math

import jax
import jax.numpy as jnp
from jax import lax
from jax.sharding import PartitionSpec as P

NEG_FILL = -1e30


def partial_attend(queries, keys, values, visible):
    factor = 1.0 / math.sqrt(queries.shape[-1])
    scores = jnp.dot(queries, keys.T, preferred_element_type=jnp.float32) * factor
    scores = jnp.where(visible, scores, NEG_FILL)
    row_top = jnp.max(scores, axis=1)
    weights = jnp.where(visible, jnp.exp(scores - row_top[:, None]), 0.0)
    weight_sum = jnp.sum(weights, axis=1)
    numerator = jnp.dot(weights.astype(jnp.bfloat16), values, preferred_element_type=jnp.float32)
    return (row_top, weight_sum, numerator)


def body(
    new_query,
    new_key,
    new_value,
    cache_keys,
    cache_values,
    cache_length,
    dealing,
    out_weight,
    stretch_query,
    stretch_key,
    stretch_value,
    prior_keys,
    prior_values,
    stretch_start,
):
    head_size = cache_keys.shape[2]
    group_size = new_query.shape[1] // head_size
    local_dec = new_query.shape[0]
    seq_rank = lax.axis_index("seq")
    seq_count = lax.axis_size("seq")
    total_dec = local_dec * seq_count
    stretch_count, local_tok, query_width = stretch_query.shape
    key_width = stretch_key.shape[2]
    stretch_rows = stretch_count * local_tok

    stretch_pack = jnp.concatenate([stretch_query, stretch_key, stretch_value], axis=2).reshape(
        stretch_rows, query_width + 2 * key_width
    )
    decode_pack = jnp.concatenate([new_query, new_key, new_value], axis=1)
    gathered = lax.all_gather(
        jnp.concatenate([stretch_pack, decode_pack], axis=0), "seq", axis=0, tiled=False
    )

    decode_part = gathered[:, stretch_rows:, :].reshape(total_dec, query_width + 2 * key_width)
    every_query = decode_part[:, :query_width]
    every_key = decode_part[:, query_width : query_width + key_width]
    every_value = decode_part[:, query_width + key_width :]
    slot_ids = seq_rank * local_dec + jnp.arange(local_dec, dtype=jnp.int32)
    arrival_ids = jnp.arange(total_dec, dtype=jnp.int32)
    sources = jnp.sum(
        jnp.where(dealing[None, :] == slot_ids[:, None], arrival_ids[None, :], 0), axis=1
    )
    home_query = jnp.take(every_query, sources, axis=0)
    home_key = jnp.take(every_key, sources, axis=0)
    home_value = jnp.take(every_value, sources, axis=0)
    cache_span = cache_keys.shape[1]
    cache_pos = jnp.arange(cache_span, dtype=jnp.int32)

    def decode_slot(query_row, own_key, own_value, cached_keys, cached_values, length):
        key_all = jnp.concatenate([cached_keys, own_key[None, :]], axis=0)
        value_all = jnp.concatenate([cached_values, own_value[None, :]], axis=0)
        visible = jnp.concatenate([cache_pos < length, jnp.ones((1,), dtype=jnp.bool_)])
        visible = jnp.broadcast_to(visible[None, :], (group_size, cache_span + 1))
        row_top, weight_sum, numerator = partial_attend(
            query_row.reshape(group_size, head_size), key_all, value_all, visible
        )
        return (
            (numerator / weight_sum[:, None]).astype(jnp.bfloat16).reshape(group_size * head_size)
        )

    home_out = jax.vmap(decode_slot)(
        home_query, home_key, home_value, cache_keys, cache_values, cache_length
    )

    prior_span = prior_keys.shape[1]
    rows_per_src = local_tok * group_size
    row_count = seq_count * rows_per_src
    prior_pos = seq_rank * prior_span + jnp.arange(prior_span, dtype=jnp.int32)
    stretch_part = gathered[:, :stretch_rows, :].reshape(
        seq_count, stretch_count, local_tok, query_width + 2 * key_width
    )
    queries_all = (
        stretch_part[:, :, :, :query_width]
        .transpose(1, 0, 2, 3)
        .reshape(stretch_count, row_count, head_size)
    )
    factor = 1.0 / math.sqrt(head_size)
    scores = (
        jnp.einsum("crd,cpd->crp", queries_all, prior_keys, preferred_element_type=jnp.float32)
        * factor
    )
    prior_visible = (prior_pos[None, :] < stretch_start[:, None])[:, None, :]
    scores = jnp.where(prior_visible, scores, NEG_FILL)
    part_top = jnp.max(scores, axis=2)
    weights = jnp.where(prior_visible, jnp.exp(scores - part_top[..., None]), 0.0)
    part_sum = jnp.sum(weights, axis=2)
    part_num = jnp.einsum(
        "crp,cpd->crd", weights.astype(jnp.bfloat16), prior_values,
        preferred_element_type=jnp.float32,
    )
    safe_sum = jnp.maximum(part_sum, 1.0)
    part_out = (part_num / safe_sum[..., None]).astype(jnp.bfloat16)
    part_lse = part_top + jnp.log(safe_sum)
    lse_hi = lax.reduce_precision(part_lse, exponent_bits=8, mantissa_bits=7)
    lse_rest = part_lse - lse_hi
    lse_mid = lax.reduce_precision(lse_rest, exponent_bits=8, mantissa_bits=7)
    lse_lo = lse_rest - lse_mid
    stat_count = 3 * stretch_count * rows_per_src
    stat_rows = -(-stat_count // head_size)
    stats = (
        jnp.stack([lse_hi, lse_mid, lse_lo])
        .reshape(3, stretch_count, seq_count, rows_per_src)
        .transpose(2, 0, 1, 3)
        .reshape(seq_count, stat_count)
    )
    stats = jnp.pad(stats, ((0, 0), (0, stat_rows * head_size - stat_count))).astype(jnp.bfloat16)

    dec_rows = local_dec * group_size
    out_rows = stretch_count * rows_per_src
    payload = jnp.concatenate(
        [
            part_out.reshape(stretch_count, seq_count, rows_per_src, head_size)
            .transpose(1, 0, 2, 3)
            .reshape(seq_count, out_rows, head_size),
            stats.reshape(seq_count, stat_rows, head_size),
            jnp.broadcast_to(
                home_out.reshape(1, dec_rows, head_size), (seq_count, dec_rows, head_size)
            ),
        ],
        axis=1,
    )
    received = lax.all_to_all(payload, "seq", 0, 0, tiled=True)
    got_out = (
        received[:, :out_rows, :]
        .reshape(seq_count, stretch_count, local_tok, group_size, head_size)
        .astype(jnp.float32)
    )
    got_stats = (
        received[:, out_rows : out_rows + stat_rows, :]
        .reshape(seq_count, stat_rows * head_size)[:, :stat_count]
        .astype(jnp.float32)
        .reshape(seq_count, 3, stretch_count, local_tok, group_size)
    )
    got_lse = (got_stats[:, 0] + got_stats[:, 1]) + got_stats[:, 2]
    all_out = received[:, out_rows + stat_rows :, :].reshape(total_dec, group_size * head_size)

    arrival_out = jnp.take(all_out, dealing, axis=0)
    arrival_terms = jnp.dot(arrival_out, out_weight, preferred_element_type=jnp.float32)
    decode_mixed = lax.psum_scatter(arrival_terms, "tp", scatter_dimension=0, tiled=True).astype(
        jnp.bfloat16
    )

    stretch_len = local_tok * seq_count
    local_rows = local_tok * group_size
    stretch_pos = jnp.arange(stretch_len, dtype=jnp.int32)
    own_token = seq_rank * local_tok + jnp.arange(local_rows, dtype=jnp.int32) // group_size
    causal = stretch_pos[None, :] <= own_token[:, None]
    self_tops, self_totals, self_numers = ([], [], [])
    for stretch_index in range(stretch_count):
        local_queries = stretch_query[stretch_index].reshape(local_rows, head_size)
        keys_all = stretch_part[:, stretch_index, :, query_width : query_width + key_width].reshape(
            stretch_len, key_width
        )
        values_all = stretch_part[:, stretch_index, :, query_width + key_width :].reshape(
            stretch_len, key_width
        )
        pieces = partial_attend(local_queries, keys_all, values_all, causal)
        self_tops.append(pieces[0].reshape(local_tok, group_size))
        self_totals.append(pieces[1].reshape(local_tok, group_size))
        self_numers.append(pieces[2].reshape(local_tok, group_size, head_size))
    self_top = jnp.stack(self_tops)
    self_sum = jnp.stack(self_totals)
    self_num = jnp.stack(self_numers)
    final_top = jnp.maximum(jnp.max(got_lse, axis=0), self_top + jnp.log(self_sum))
    part_factor = jnp.exp(got_lse - final_top[None])
    self_factor = jnp.exp(self_top - final_top)
    total_sum = jnp.sum(part_factor, axis=0) + self_sum * self_factor
    total_num = (
        jnp.sum(got_out * part_factor[..., None], axis=0) + self_num * self_factor[..., None]
    )
    stretch_out = (
        (total_num / total_sum[..., None])
        .astype(jnp.bfloat16)
        .reshape(stretch_count, local_tok, group_size * head_size)
    )
    return (decode_mixed, stretch_out)


def solution(mesh):
    return jax.shard_map(
        body,
        mesh=mesh,
        in_specs=(
            P("seq", "tp"),
            P("seq", "tp"),
            P("seq", "tp"),
            P("seq", None, "tp"),
            P("seq", None, "tp"),
            P("seq"),
            P(),
            P("tp", "seq"),
            P(None, "seq", "tp"),
            P(None, "seq", "tp"),
            P(None, "seq", "tp"),
            P(None, "seq", "tp"),
            P(None, "seq", "tp"),
            P(),
        ),
        out_specs=(P("tp", "seq"), P(None, "seq", "tp")),
        check_vma=False,
    )
```

```python
import functools
import math

import jax
import jax.numpy as jnp
from jax import lax
from jax.experimental import pallas as pl
from jax.experimental.pallas import tpu as pltpu
from jax.sharding import PartitionSpec as P

NEG_FILL = -1e30


def partial_attend(queries, keys, values, visible):
    factor = 1.0 / math.sqrt(queries.shape[-1])
    scores = jnp.dot(queries, keys.T, preferred_element_type=jnp.float32) * factor
    scores = jnp.where(visible, scores, NEG_FILL)
    row_top = jnp.max(scores, axis=1)
    weights = jnp.where(visible, jnp.exp(scores - row_top[:, None]), 0.0)
    weight_sum = jnp.sum(weights, axis=1)
    numerator = jnp.dot(weights.astype(jnp.bfloat16), values, preferred_element_type=jnp.float32)
    return (row_top, weight_sum, numerator)


def _prefill_kernel(limit_ref, q_ref, k_ref, v_ref, o_ref, lse_ref, *, group_size, head_size):
    c = pl.program_id(0)
    limit = limit_ref[c]
    keys = k_ref[0]
    values = v_ref[0]
    factor = 1.0 / math.sqrt(head_size)
    col = lax.broadcasted_iota(jnp.int32, (1, keys.shape[0]), 1)
    visible = col < limit
    for h in range(group_size):
        q = q_ref[0, :, h * head_size:(h + 1) * head_size]
        s = lax.dot_general(q, keys, (((1,), (1,)), ((), ())), preferred_element_type=jnp.float32) * factor
        s = jnp.where(visible, s, NEG_FILL)
        m = jnp.max(s, axis=1, keepdims=True)
        w = jnp.where(visible, jnp.exp(s - m), 0.0)
        l = jnp.sum(w, axis=1, keepdims=True)
        num = jnp.dot(w.astype(jnp.bfloat16), values, preferred_element_type=jnp.float32)
        safe = jnp.maximum(l, 1.0)
        o_ref[0, :, h * head_size:(h + 1) * head_size] = (num / safe).astype(o_ref.dtype)
        lse_ref[0, :, h:h + 1] = m + jnp.log(safe)

def prefill_partial(limits, queries, keys, values, group_size):
    n, t, qw = queries.shape
    p, hd = keys.shape[1], keys.shape[2]
    kern = functools.partial(_prefill_kernel, group_size=group_size, head_size=hd)
    return pl.pallas_call(
        kern,
        grid_spec=pltpu.PrefetchScalarGridSpec(
            num_scalar_prefetch=1,
            grid=(n,),
            in_specs=[
                pl.BlockSpec((1, t, qw), lambda c, lim: (c, 0, 0)),
                pl.BlockSpec((1, p, hd), lambda c, lim: (c, 0, 0)),
                pl.BlockSpec((1, p, hd), lambda c, lim: (c, 0, 0)),
            ],
            out_specs=[
                pl.BlockSpec((1, t, qw), lambda c, lim: (c, 0, 0)),
                pl.BlockSpec((1, t, group_size), lambda c, lim: (c, 0, 0)),
            ],
        ),
        out_shape=[jax.ShapeDtypeStruct((n, t, qw), jnp.bfloat16), jax.ShapeDtypeStruct((n, t, group_size), jnp.float32)],
    )(limits, queries, keys, values)


def body(
    new_query,
    new_key,
    new_value,
    cache_keys,
    cache_values,
    cache_length,
    dealing,
    out_weight,
    stretch_query,
    stretch_key,
    stretch_value,
    prior_keys,
    prior_values,
    stretch_start,
):
    head_size = cache_keys.shape[2]
    group_size = new_query.shape[1] // head_size
    local_dec = new_query.shape[0]
    seq_rank = lax.axis_index("seq")
    seq_count = lax.axis_size("seq")
    total_dec = local_dec * seq_count
    stretch_count, local_tok, query_width = stretch_query.shape
    key_width = stretch_key.shape[2]
    stretch_rows = stretch_count * local_tok

    stretch_pack = jnp.concatenate([stretch_query, stretch_key, stretch_value], axis=2).reshape(
        stretch_rows, query_width + 2 * key_width
    )
    decode_pack = jnp.concatenate([new_query, new_key, new_value], axis=1)
    gathered = lax.all_gather(
        jnp.concatenate([stretch_pack, decode_pack], axis=0), "seq", axis=0, tiled=False
    )

    decode_part = gathered[:, stretch_rows:, :].reshape(total_dec, query_width + 2 * key_width)
    every_query = decode_part[:, :query_width]
    every_key = decode_part[:, query_width : query_width + key_width]
    every_value = decode_part[:, query_width + key_width :]
    slot_ids = seq_rank * local_dec + jnp.arange(local_dec, dtype=jnp.int32)
    arrival_ids = jnp.arange(total_dec, dtype=jnp.int32)
    sources = jnp.sum(
        jnp.where(dealing[None, :] == slot_ids[:, None], arrival_ids[None, :], 0), axis=1
    )
    home_query = jnp.take(every_query, sources, axis=0)
    home_key = jnp.take(every_key, sources, axis=0)
    home_value = jnp.take(every_value, sources, axis=0)
    cache_span = cache_keys.shape[1]
    cache_pos = jnp.arange(cache_span, dtype=jnp.int32)

    def decode_slot(query_row, own_key, own_value, cached_keys, cached_values, length):
        key_all = jnp.concatenate([cached_keys, own_key[None, :]], axis=0)
        value_all = jnp.concatenate([cached_values, own_value[None, :]], axis=0)
        visible = jnp.concatenate([cache_pos < length, jnp.ones((1,), dtype=jnp.bool_)])
        visible = jnp.broadcast_to(visible[None, :], (group_size, cache_span + 1))
        row_top, weight_sum, numerator = partial_attend(
            query_row.reshape(group_size, head_size), key_all, value_all, visible
        )
        return (
            (numerator / weight_sum[:, None]).astype(jnp.bfloat16).reshape(group_size * head_size)
        )

    home_out = jax.vmap(decode_slot)(
        home_query, home_key, home_value, cache_keys, cache_values, cache_length
    )

    prior_span = prior_keys.shape[1]
    rows_per_src = local_tok * group_size
    row_count = seq_count * rows_per_src
    prior_pos = seq_rank * prior_span + jnp.arange(prior_span, dtype=jnp.int32)
    stretch_part = gathered[:, :stretch_rows, :].reshape(
        seq_count, stretch_count, local_tok, query_width + 2 * key_width
    )
    queries_all = (
        stretch_part[:, :, :, :query_width]
        .transpose(1, 0, 2, 3)
        .reshape(stretch_count, seq_count * local_tok, query_width)
    )
    limits = jnp.clip(stretch_start - seq_rank * prior_span, 0, prior_span).astype(jnp.int32)
    part_out, part_lse = prefill_partial(limits, queries_all, prior_keys, prior_values, group_size)
    part_out = part_out.reshape(stretch_count, row_count, head_size)
    part_lse = part_lse.reshape(stretch_count, row_count)
    lse_hi = lax.reduce_precision(part_lse, exponent_bits=8, mantissa_bits=7)
    lse_rest = part_lse - lse_hi
    lse_mid = lax.reduce_precision(lse_rest, exponent_bits=8, mantissa_bits=7)
    lse_lo = lse_rest - lse_mid
    stat_count = 3 * stretch_count * rows_per_src
    stat_rows = -(-stat_count // head_size)
    stats = (
        jnp.stack([lse_hi, lse_mid, lse_lo])
        .reshape(3, stretch_count, seq_count, rows_per_src)
        .transpose(2, 0, 1, 3)
        .reshape(seq_count, stat_count)
    )
    stats = jnp.pad(stats, ((0, 0), (0, stat_rows * head_size - stat_count))).astype(jnp.bfloat16)

    dec_rows = local_dec * group_size
    out_rows = stretch_count * rows_per_src
    payload = jnp.concatenate(
        [
            part_out.reshape(stretch_count, seq_count, rows_per_src, head_size)
            .transpose(1, 0, 2, 3)
            .reshape(seq_count, out_rows, head_size),
            stats.reshape(seq_count, stat_rows, head_size),
            jnp.broadcast_to(
                home_out.reshape(1, dec_rows, head_size), (seq_count, dec_rows, head_size)
            ),
        ],
        axis=1,
    )
    received = lax.all_to_all(payload, "seq", 0, 0, tiled=True)
    got_out = (
        received[:, :out_rows, :]
        .reshape(seq_count, stretch_count, local_tok, group_size, head_size)
        .astype(jnp.float32)
    )
    got_stats = (
        received[:, out_rows : out_rows + stat_rows, :]
        .reshape(seq_count, stat_rows * head_size)[:, :stat_count]
        .astype(jnp.float32)
        .reshape(seq_count, 3, stretch_count, local_tok, group_size)
    )
    got_lse = (got_stats[:, 0] + got_stats[:, 1]) + got_stats[:, 2]
    all_out = received[:, out_rows + stat_rows :, :].reshape(total_dec, group_size * head_size)

    arrival_out = jnp.take(all_out, dealing, axis=0)
    arrival_terms = jnp.dot(arrival_out, out_weight, preferred_element_type=jnp.float32)
    decode_mixed = lax.psum_scatter(arrival_terms, "tp", scatter_dimension=0, tiled=True).astype(
        jnp.bfloat16
    )

    stretch_len = local_tok * seq_count
    local_rows = local_tok * group_size
    stretch_pos = jnp.arange(stretch_len, dtype=jnp.int32)
    own_token = seq_rank * local_tok + jnp.arange(local_rows, dtype=jnp.int32) // group_size
    causal = stretch_pos[None, :] <= own_token[:, None]
    self_tops, self_totals, self_numers = ([], [], [])
    for stretch_index in range(stretch_count):
        local_queries = stretch_query[stretch_index].reshape(local_rows, head_size)
        keys_all = stretch_part[:, stretch_index, :, query_width : query_width + key_width].reshape(
            stretch_len, key_width
        )
        values_all = stretch_part[:, stretch_index, :, query_width + key_width :].reshape(
            stretch_len, key_width
        )
        pieces = partial_attend(local_queries, keys_all, values_all, causal)
        self_tops.append(pieces[0].reshape(local_tok, group_size))
        self_totals.append(pieces[1].reshape(local_tok, group_size))
        self_numers.append(pieces[2].reshape(local_tok, group_size, head_size))
    self_top = jnp.stack(self_tops)
    self_sum = jnp.stack(self_totals)
    self_num = jnp.stack(self_numers)
    final_top = jnp.maximum(jnp.max(got_lse, axis=0), self_top + jnp.log(self_sum))
    part_factor = jnp.exp(got_lse - final_top[None])
    self_factor = jnp.exp(self_top - final_top)
    total_sum = jnp.sum(part_factor, axis=0) + self_sum * self_factor
    total_num = (
        jnp.sum(got_out * part_factor[..., None], axis=0) + self_num * self_factor[..., None]
    )
    stretch_out = (
        (total_num / total_sum[..., None])
        .astype(jnp.bfloat16)
        .reshape(stretch_count, local_tok, group_size * head_size)
    )
    return (decode_mixed, stretch_out)


def solution(mesh):
    return jax.shard_map(
        body,
        mesh=mesh,
        in_specs=(
            P("seq", "tp"),
            P("seq", "tp"),
            P("seq", "tp"),
            P("seq", None, "tp"),
            P("seq", None, "tp"),
            P("seq"),
            P(),
            P("tp", "seq"),
            P(None, "seq", "tp"),
            P(None, "seq", "tp"),
            P(None, "seq", "tp"),
            P(None, "seq", "tp"),
            P(None, "seq", "tp"),
            P(),
        ),
        out_specs=(P("tp", "seq"), P(None, "seq", "tp")),
        check_vma=False,
    )
```

```python
import functools
import math

import jax
import jax.numpy as jnp
from jax import lax
from jax.experimental import pallas as pl
from jax.experimental.pallas import tpu as pltpu
from jax.sharding import PartitionSpec as P

NEG_FILL = -1e30


def partial_attend(queries, keys, values, visible):
    factor = 1.0 / math.sqrt(queries.shape[-1])
    scores = jnp.dot(queries, keys.T, preferred_element_type=jnp.float32) * factor
    scores = jnp.where(visible, scores, NEG_FILL)
    row_top = jnp.max(scores, axis=1)
    weights = jnp.where(visible, jnp.exp(scores - row_top[:, None]), 0.0)
    weight_sum = jnp.sum(weights, axis=1)
    numerator = jnp.dot(weights.astype(jnp.bfloat16), values, preferred_element_type=jnp.float32)
    return (row_top, weight_sum, numerator)


def _prefill_kernel(limit_ref, q_ref, k_ref, v_ref, o_ref, lse_ref, *, group_size, head_size):
    c = pl.program_id(0)
    limit = limit_ref[c]
    keys = k_ref[0]
    values = v_ref[0]
    factor = 1.0 / math.sqrt(head_size)
    col = lax.broadcasted_iota(jnp.int32, (1, keys.shape[0]), 1)
    visible = col < limit
    for h in range(group_size):
        q = q_ref[0, :, h * head_size:(h + 1) * head_size]
        s = lax.dot_general(q, keys, (((1,), (1,)), ((), ())), preferred_element_type=jnp.float32) * factor
        s = jnp.where(visible, s, NEG_FILL)
        m = jnp.max(s, axis=1, keepdims=True)
        w = jnp.where(visible, jnp.exp(s - m), 0.0)
        l = jnp.sum(w, axis=1, keepdims=True)
        num = jnp.dot(w.astype(jnp.bfloat16), values, preferred_element_type=jnp.float32)
        safe = jnp.maximum(l, 1.0)
        o_ref[0, :, h * head_size:(h + 1) * head_size] = (num / safe).astype(o_ref.dtype)
        lse_ref[0, :, h:h + 1] = m + jnp.log(safe)

def prefill_partial(limits, queries, keys, values, group_size):
    n, t, qw = queries.shape
    p, hd = keys.shape[1], keys.shape[2]
    kern = functools.partial(_prefill_kernel, group_size=group_size, head_size=hd)
    return pl.pallas_call(
        kern,
        grid_spec=pltpu.PrefetchScalarGridSpec(
            num_scalar_prefetch=1,
            grid=(n,),
            in_specs=[
                pl.BlockSpec((1, t, qw), lambda c, lim: (c, 0, 0)),
                pl.BlockSpec((1, p, hd), lambda c, lim: (c, 0, 0)),
                pl.BlockSpec((1, p, hd), lambda c, lim: (c, 0, 0)),
            ],
            out_specs=[
                pl.BlockSpec((1, t, qw), lambda c, lim: (c, 0, 0)),
                pl.BlockSpec((1, t, group_size), lambda c, lim: (c, 0, 0)),
            ],
        ),
        out_shape=[jax.ShapeDtypeStruct((n, t, qw), jnp.bfloat16), jax.ShapeDtypeStruct((n, t, group_size), jnp.float32)],
    )(limits, queries, keys, values)


def body(
    new_query,
    new_key,
    new_value,
    cache_keys,
    cache_values,
    cache_length,
    dealing,
    out_weight,
    stretch_query,
    stretch_key,
    stretch_value,
    prior_keys,
    prior_values,
    stretch_start,
):
    head_size = cache_keys.shape[2]
    group_size = new_query.shape[1] // head_size
    local_dec = new_query.shape[0]
    seq_rank = lax.axis_index("seq")
    seq_count = lax.axis_size("seq")
    total_dec = local_dec * seq_count
    stretch_count, local_tok, query_width = stretch_query.shape
    key_width = stretch_key.shape[2]
    stretch_rows = stretch_count * local_tok

    stretch_pack = jnp.concatenate([stretch_query, stretch_key, stretch_value], axis=2).reshape(
        stretch_rows, query_width + 2 * key_width
    )
    decode_pack = jnp.concatenate([new_query, new_key, new_value], axis=1)
    pack = jnp.concatenate([stretch_pack, decode_pack], axis=0)
    gathered = lax.all_to_all(
        jnp.broadcast_to(pack[None], (seq_count,) + pack.shape), "seq", 0, 0, tiled=True
    )

    decode_part = gathered[:, stretch_rows:, :].reshape(total_dec, query_width + 2 * key_width)
    every_query = decode_part[:, :query_width]
    every_key = decode_part[:, query_width : query_width + key_width]
    every_value = decode_part[:, query_width + key_width :]
    slot_ids = seq_rank * local_dec + jnp.arange(local_dec, dtype=jnp.int32)
    arrival_ids = jnp.arange(total_dec, dtype=jnp.int32)
    sources = jnp.sum(
        jnp.where(dealing[None, :] == slot_ids[:, None], arrival_ids[None, :], 0), axis=1
    )
    home_query = jnp.take(every_query, sources, axis=0)
    home_key = jnp.take(every_key, sources, axis=0)
    home_value = jnp.take(every_value, sources, axis=0)
    cache_span = cache_keys.shape[1]
    cache_pos = jnp.arange(cache_span, dtype=jnp.int32)

    def decode_slot(query_row, own_key, own_value, cached_keys, cached_values, length):
        key_all = jnp.concatenate([cached_keys, own_key[None, :]], axis=0)
        value_all = jnp.concatenate([cached_values, own_value[None, :]], axis=0)
        visible = jnp.concatenate([cache_pos < length, jnp.ones((1,), dtype=jnp.bool_)])
        visible = jnp.broadcast_to(visible[None, :], (group_size, cache_span + 1))
        row_top, weight_sum, numerator = partial_attend(
            query_row.reshape(group_size, head_size), key_all, value_all, visible
        )
        return (
            (numerator / weight_sum[:, None]).astype(jnp.bfloat16).reshape(group_size * head_size)
        )

    home_out = jax.vmap(decode_slot)(
        home_query, home_key, home_value, cache_keys, cache_values, cache_length
    )

    prior_span = prior_keys.shape[1]
    rows_per_src = local_tok * group_size
    row_count = seq_count * rows_per_src
    prior_pos = seq_rank * prior_span + jnp.arange(prior_span, dtype=jnp.int32)
    stretch_part = gathered[:, :stretch_rows, :].reshape(
        seq_count, stretch_count, local_tok, query_width + 2 * key_width
    )
    queries_all = (
        stretch_part[:, :, :, :query_width]
        .transpose(1, 0, 2, 3)
        .reshape(stretch_count, seq_count * local_tok, query_width)
    )
    limits = jnp.clip(stretch_start - seq_rank * prior_span, 0, prior_span).astype(jnp.int32)
    part_out, part_lse = prefill_partial(limits, queries_all, prior_keys, prior_values, group_size)
    part_out = part_out.reshape(stretch_count, row_count, head_size)
    part_lse = part_lse.reshape(stretch_count, row_count)
    lse_hi = lax.reduce_precision(part_lse, exponent_bits=8, mantissa_bits=7)
    lse_rest = part_lse - lse_hi
    lse_mid = lax.reduce_precision(lse_rest, exponent_bits=8, mantissa_bits=7)
    lse_lo = lse_rest - lse_mid
    stat_count = 3 * stretch_count * rows_per_src
    stat_rows = -(-stat_count // head_size)
    stats = (
        jnp.stack([lse_hi, lse_mid, lse_lo])
        .reshape(3, stretch_count, seq_count, rows_per_src)
        .transpose(2, 0, 1, 3)
        .reshape(seq_count, stat_count)
    )
    stats = jnp.pad(stats, ((0, 0), (0, stat_rows * head_size - stat_count))).astype(jnp.bfloat16)

    dec_rows = local_dec * group_size
    out_rows = stretch_count * rows_per_src
    payload = jnp.concatenate(
        [
            part_out.reshape(stretch_count, seq_count, rows_per_src, head_size)
            .transpose(1, 0, 2, 3)
            .reshape(seq_count, out_rows, head_size),
            stats.reshape(seq_count, stat_rows, head_size),
            jnp.broadcast_to(
                home_out.reshape(1, dec_rows, head_size), (seq_count, dec_rows, head_size)
            ),
        ],
        axis=1,
    )
    received = lax.all_to_all(payload, "seq", 0, 0, tiled=True)
    got_out = (
        received[:, :out_rows, :]
        .reshape(seq_count, stretch_count, local_tok, group_size, head_size)
        .astype(jnp.float32)
    )
    got_stats = (
        received[:, out_rows : out_rows + stat_rows, :]
        .reshape(seq_count, stat_rows * head_size)[:, :stat_count]
        .astype(jnp.float32)
        .reshape(seq_count, 3, stretch_count, local_tok, group_size)
    )
    got_lse = (got_stats[:, 0] + got_stats[:, 1]) + got_stats[:, 2]
    all_out = received[:, out_rows + stat_rows :, :].reshape(total_dec, group_size * head_size)

    arrival_out = jnp.take(all_out, dealing, axis=0)
    arrival_terms = jnp.dot(arrival_out, out_weight, preferred_element_type=jnp.float32)
    decode_mixed = lax.psum_scatter(arrival_terms, "tp", scatter_dimension=0, tiled=True).astype(
        jnp.bfloat16
    )

    stretch_len = local_tok * seq_count
    local_rows = local_tok * group_size
    stretch_pos = jnp.arange(stretch_len, dtype=jnp.int32)
    own_token = seq_rank * local_tok + jnp.arange(local_rows, dtype=jnp.int32) // group_size
    causal = stretch_pos[None, :] <= own_token[:, None]
    self_tops, self_totals, self_numers = ([], [], [])
    for stretch_index in range(stretch_count):
        local_queries = stretch_query[stretch_index].reshape(local_rows, head_size)
        keys_all = stretch_part[:, stretch_index, :, query_width : query_width + key_width].reshape(
            stretch_len, key_width
        )
        values_all = stretch_part[:, stretch_index, :, query_width + key_width :].reshape(
            stretch_len, key_width
        )
        pieces = partial_attend(local_queries, keys_all, values_all, causal)
        self_tops.append(pieces[0].reshape(local_tok, group_size))
        self_totals.append(pieces[1].reshape(local_tok, group_size))
        self_numers.append(pieces[2].reshape(local_tok, group_size, head_size))
    self_top = jnp.stack(self_tops)
    self_sum = jnp.stack(self_totals)
    self_num = jnp.stack(self_numers)
    final_top = jnp.maximum(jnp.max(got_lse, axis=0), self_top + jnp.log(self_sum))
    part_factor = jnp.exp(got_lse - final_top[None])
    self_factor = jnp.exp(self_top - final_top)
    total_sum = jnp.sum(part_factor, axis=0) + self_sum * self_factor
    total_num = (
        jnp.sum(got_out * part_factor[..., None], axis=0) + self_num * self_factor[..., None]
    )
    stretch_out = (
        (total_num / total_sum[..., None])
        .astype(jnp.bfloat16)
        .reshape(stretch_count, local_tok, group_size * head_size)
    )
    return (decode_mixed, stretch_out)


def solution(mesh):
    return jax.shard_map(
        body,
        mesh=mesh,
        in_specs=(
            P("seq", "tp"),
            P("seq", "tp"),
            P("seq", "tp"),
            P("seq", None, "tp"),
            P("seq", None, "tp"),
            P("seq"),
            P(),
            P("tp", "seq"),
            P(None, "seq", "tp"),
            P(None, "seq", "tp"),
            P(None, "seq", "tp"),
            P(None, "seq", "tp"),
            P(None, "seq", "tp"),
            P(),
        ),
        out_specs=(P("tp", "seq"), P(None, "seq", "tp")),
        check_vma=False,
    )
```

```python
import functools
import math

import jax
import jax.numpy as jnp
from jax import lax
from jax.experimental import pallas as pl
from jax.experimental.pallas import tpu as pltpu
from jax.sharding import PartitionSpec as P

NEG_FILL = -1e30


def partial_attend(queries, keys, values, visible):
    factor = 1.0 / math.sqrt(queries.shape[-1])
    scores = jnp.dot(queries, keys.T, preferred_element_type=jnp.float32) * factor
    scores = jnp.where(visible, scores, NEG_FILL)
    row_top = jnp.max(scores, axis=1)
    weights = jnp.where(visible, jnp.exp(scores - row_top[:, None]), 0.0)
    weight_sum = jnp.sum(weights, axis=1)
    numerator = jnp.dot(weights.astype(jnp.bfloat16), values, preferred_element_type=jnp.float32)
    return (row_top, weight_sum, numerator)


def _prefill_kernel(
    info_ref, q_ref, k_ref, v_ref, sk_ref, sv_ref, o_ref, lse_ref, *, group_size, head_size
):
    c = pl.program_id(0)
    limit = info_ref[c]
    key_offset = info_ref[info_ref.shape[0] - 1]
    keys = k_ref[0]
    values = v_ref[0]
    own_keys = sk_ref[0]
    own_values = sv_ref[0]
    factor = 1.0 / math.sqrt(head_size)
    tokens = q_ref.shape[1]
    col = lax.broadcasted_iota(jnp.int32, (1, keys.shape[0]), 1)
    visible = col < limit
    key_token = key_offset + lax.broadcasted_iota(jnp.int32, (tokens, own_keys.shape[0]), 1)
    query_token = lax.broadcasted_iota(jnp.int32, (tokens, own_keys.shape[0]), 0)
    causal = key_token <= query_token
    dims = (((1,), (1,)), ((), ()))
    for h in range(group_size):
        q = q_ref[0, :, h * head_size : (h + 1) * head_size]
        s = lax.dot_general(q, keys, dims, preferred_element_type=jnp.float32) * factor
        s = jnp.where(visible, s, NEG_FILL)
        s_own = lax.dot_general(q, own_keys, dims, preferred_element_type=jnp.float32) * factor
        s_own = jnp.where(causal, s_own, NEG_FILL)
        m = jnp.maximum(
            jnp.max(s, axis=1, keepdims=True), jnp.max(s_own, axis=1, keepdims=True)
        )
        w = jnp.where(visible, jnp.exp(s - m), 0.0)
        w_own = jnp.where(causal, jnp.exp(s_own - m), 0.0)
        l = jnp.sum(w, axis=1, keepdims=True) + jnp.sum(w_own, axis=1, keepdims=True)
        num = jnp.dot(w.astype(jnp.bfloat16), values, preferred_element_type=jnp.float32)
        num = num + jnp.dot(
            w_own.astype(jnp.bfloat16), own_values, preferred_element_type=jnp.float32
        )
        safe = jnp.maximum(l, 1.0)
        o_ref[0, :, h * head_size : (h + 1) * head_size] = (num / safe).astype(o_ref.dtype)
        lse_ref[0, :, h : h + 1] = m + jnp.log(safe)


def prefill_partial(info, queries, keys, values, own_keys, own_values, group_size):
    n, t, qw = queries.shape
    p, hd = keys.shape[1], keys.shape[2]
    own = own_keys.shape[1]
    kern = functools.partial(_prefill_kernel, group_size=group_size, head_size=hd)
    return pl.pallas_call(
        kern,
        grid_spec=pltpu.PrefetchScalarGridSpec(
            num_scalar_prefetch=1,
            grid=(n,),
            in_specs=[
                pl.BlockSpec((1, t, qw), lambda c, info: (c, 0, 0)),
                pl.BlockSpec((1, p, hd), lambda c, info: (c, 0, 0)),
                pl.BlockSpec((1, p, hd), lambda c, info: (c, 0, 0)),
                pl.BlockSpec((1, own, hd), lambda c, info: (c, 0, 0)),
                pl.BlockSpec((1, own, hd), lambda c, info: (c, 0, 0)),
            ],
            out_specs=[
                pl.BlockSpec((1, t, qw), lambda c, info: (c, 0, 0)),
                pl.BlockSpec((1, t, group_size), lambda c, info: (c, 0, 0)),
            ],
        ),
        out_shape=[
            jax.ShapeDtypeStruct((n, t, qw), jnp.bfloat16),
            jax.ShapeDtypeStruct((n, t, group_size), jnp.float32),
        ],
    )(info, queries, keys, values, own_keys, own_values)


def body(
    new_query,
    new_key,
    new_value,
    cache_keys,
    cache_values,
    cache_length,
    dealing,
    out_weight,
    stretch_query,
    stretch_key,
    stretch_value,
    prior_keys,
    prior_values,
    stretch_start,
):
    head_size = cache_keys.shape[2]
    group_size = new_query.shape[1] // head_size
    local_dec = new_query.shape[0]
    seq_rank = lax.axis_index("seq")
    seq_count = lax.axis_size("seq")
    total_dec = local_dec * seq_count
    stretch_count, local_tok, query_width = stretch_query.shape
    key_width = stretch_key.shape[2]
    stretch_rows = stretch_count * local_tok

    decode_kv = jnp.concatenate([new_key, new_value], axis=1)
    decode_kv = jnp.pad(decode_kv, ((0, 0), (0, query_width - 2 * key_width)))
    pack = jnp.concatenate(
        [stretch_query.reshape(stretch_rows, query_width), new_query, decode_kv], axis=0
    )
    gathered = lax.all_to_all(
        jnp.broadcast_to(pack[None], (seq_count,) + pack.shape), "seq", 0, 0, tiled=True
    )
    every_query = gathered[:, stretch_rows : stretch_rows + local_dec, :].reshape(
        total_dec, query_width
    )
    every_kv = gathered[:, stretch_rows + local_dec :, :].reshape(total_dec, query_width)
    every_key = every_kv[:, :key_width]
    every_value = every_kv[:, key_width : 2 * key_width]
    slot_ids = seq_rank * local_dec + jnp.arange(local_dec, dtype=jnp.int32)
    arrival_ids = jnp.arange(total_dec, dtype=jnp.int32)
    sources = jnp.sum(
        jnp.where(dealing[None, :] == slot_ids[:, None], arrival_ids[None, :], 0), axis=1
    )
    home_query = jnp.take(every_query, sources, axis=0)
    home_key = jnp.take(every_key, sources, axis=0)
    home_value = jnp.take(every_value, sources, axis=0)
    cache_span = cache_keys.shape[1]
    cache_pos = jnp.arange(cache_span, dtype=jnp.int32)

    def decode_slot(query_row, own_key, own_value, cached_keys, cached_values, length):
        key_all = jnp.concatenate([cached_keys, own_key[None, :]], axis=0)
        value_all = jnp.concatenate([cached_values, own_value[None, :]], axis=0)
        visible = jnp.concatenate([cache_pos < length, jnp.ones((1,), dtype=jnp.bool_)])
        visible = jnp.broadcast_to(visible[None, :], (group_size, cache_span + 1))
        row_top, weight_sum, numerator = partial_attend(
            query_row.reshape(group_size, head_size), key_all, value_all, visible
        )
        return (
            (numerator / weight_sum[:, None]).astype(jnp.bfloat16).reshape(group_size * head_size)
        )

    home_out = jax.vmap(decode_slot)(
        home_query, home_key, home_value, cache_keys, cache_values, cache_length
    )

    prior_span = prior_keys.shape[1]
    rows_per_src = local_tok * group_size
    row_count = seq_count * rows_per_src
    prior_pos = seq_rank * prior_span + jnp.arange(prior_span, dtype=jnp.int32)
    queries_all = (
        gathered[:, :stretch_rows, :]
        .reshape(seq_count, stretch_count, local_tok, query_width)
        .transpose(1, 0, 2, 3)
        .reshape(stretch_count, seq_count * local_tok, query_width)
    )
    limits = jnp.clip(stretch_start - seq_rank * prior_span, 0, prior_span).astype(jnp.int32)
    info = jnp.concatenate([limits, (seq_rank * local_tok).astype(jnp.int32)[None]])
    part_out, part_lse = prefill_partial(
        info, queries_all, prior_keys, prior_values, stretch_key, stretch_value, group_size
    )
    part_out = part_out.reshape(stretch_count, row_count, head_size)
    part_lse = part_lse.reshape(stretch_count, row_count)
    lse_hi = lax.reduce_precision(part_lse, exponent_bits=8, mantissa_bits=7)
    lse_rest = part_lse - lse_hi
    lse_mid = lax.reduce_precision(lse_rest, exponent_bits=8, mantissa_bits=7)
    lse_lo = lse_rest - lse_mid
    stat_count = 3 * stretch_count * rows_per_src
    stat_rows = -(-stat_count // head_size)
    stats = (
        jnp.stack([lse_hi, lse_mid, lse_lo])
        .reshape(3, stretch_count, seq_count, rows_per_src)
        .transpose(2, 0, 1, 3)
        .reshape(seq_count, stat_count)
    )
    stats = jnp.pad(stats, ((0, 0), (0, stat_rows * head_size - stat_count))).astype(jnp.bfloat16)

    dec_rows = local_dec * group_size
    out_rows = stretch_count * rows_per_src
    payload = jnp.concatenate(
        [
            part_out.reshape(stretch_count, seq_count, rows_per_src, head_size)
            .transpose(1, 0, 2, 3)
            .reshape(seq_count, out_rows, head_size),
            stats.reshape(seq_count, stat_rows, head_size),
            jnp.broadcast_to(
                home_out.reshape(1, dec_rows, head_size), (seq_count, dec_rows, head_size)
            ),
        ],
        axis=1,
    )
    received = lax.all_to_all(payload, "seq", 0, 0, tiled=True)
    got_out = (
        received[:, :out_rows, :]
        .reshape(seq_count, stretch_count, local_tok, group_size, head_size)
        .astype(jnp.float32)
    )
    got_stats = (
        received[:, out_rows : out_rows + stat_rows, :]
        .reshape(seq_count, stat_rows * head_size)[:, :stat_count]
        .astype(jnp.float32)
        .reshape(seq_count, 3, stretch_count, local_tok, group_size)
    )
    got_lse = (got_stats[:, 0] + got_stats[:, 1]) + got_stats[:, 2]
    all_out = received[:, out_rows + stat_rows :, :].reshape(total_dec, group_size * head_size)

    arrival_out = jnp.take(all_out, dealing, axis=0)
    arrival_terms = jnp.dot(arrival_out, out_weight, preferred_element_type=jnp.float32)
    decode_mixed = lax.psum_scatter(arrival_terms, "tp", scatter_dimension=0, tiled=True).astype(
        jnp.bfloat16
    )

    final_top = jnp.max(got_lse, axis=0)
    part_factor = jnp.exp(got_lse - final_top[None])
    total_sum = jnp.sum(part_factor, axis=0)
    total_num = jnp.sum(got_out * part_factor[..., None], axis=0)
    stretch_out = (
        (total_num / total_sum[..., None])
        .astype(jnp.bfloat16)
        .reshape(stretch_count, local_tok, group_size * head_size)
    )
    return (decode_mixed, stretch_out)


def solution(mesh):
    return jax.shard_map(
        body,
        mesh=mesh,
        in_specs=(
            P("seq", "tp"),
            P("seq", "tp"),
            P("seq", "tp"),
            P("seq", None, "tp"),
            P("seq", None, "tp"),
            P("seq"),
            P(),
            P("tp", "seq"),
            P(None, "seq", "tp"),
            P(None, "seq", "tp"),
            P(None, "seq", "tp"),
            P(None, "seq", "tp"),
            P(None, "seq", "tp"),
            P(),
        ),
        out_specs=(P("tp", "seq"), P(None, "seq", "tp")),
        check_vma=False,
    )
```

```python
import functools
import math

import jax
import jax.numpy as jnp
from jax import lax
from jax.experimental import pallas as pl
from jax.experimental.pallas import tpu as pltpu
from jax.sharding import PartitionSpec as P

NEG_FILL = -1e30


def partial_attend(queries, keys, values, visible):
    factor = 1.0 / math.sqrt(queries.shape[-1])
    scores = jnp.dot(queries, keys.T, preferred_element_type=jnp.float32) * factor
    scores = jnp.where(visible, scores, NEG_FILL)
    row_top = jnp.max(scores, axis=1)
    weights = jnp.where(visible, jnp.exp(scores - row_top[:, None]), 0.0)
    weight_sum = jnp.sum(weights, axis=1)
    numerator = jnp.dot(weights.astype(jnp.bfloat16), values, preferred_element_type=jnp.float32)
    return (row_top, weight_sum, numerator)


def _prefill_kernel(
    info_ref, q_ref, k_ref, v_ref, sk_ref, sv_ref, o_ref, lse_ref, *, group_size, head_size
):
    c = pl.program_id(0)
    limit = info_ref[c]
    key_offset = info_ref[info_ref.shape[0] - 1]
    keys = k_ref[0]
    values = v_ref[0]
    own_keys = sk_ref[0]
    own_values = sv_ref[0]
    factor = 1.0 / math.sqrt(head_size)
    tokens = q_ref.shape[1]
    col = lax.broadcasted_iota(jnp.int32, (1, keys.shape[0]), 1)
    visible = col < limit
    key_token = key_offset + lax.broadcasted_iota(jnp.int32, (tokens, own_keys.shape[0]), 1)
    query_token = lax.broadcasted_iota(jnp.int32, (tokens, own_keys.shape[0]), 0)
    causal = key_token <= query_token
    dims = (((1,), (1,)), ((), ()))
    for h in range(group_size):
        q = q_ref[0, :, h * head_size : (h + 1) * head_size]
        s = lax.dot_general(q, keys, dims, preferred_element_type=jnp.float32) * factor
        s = jnp.where(visible, s, NEG_FILL)
        s_own = lax.dot_general(q, own_keys, dims, preferred_element_type=jnp.float32) * factor
        s_own = jnp.where(causal, s_own, NEG_FILL)
        m = jnp.maximum(
            jnp.max(s, axis=1, keepdims=True), jnp.max(s_own, axis=1, keepdims=True)
        )
        w = jnp.where(visible, jnp.exp(s - m), 0.0)
        w_own = jnp.where(causal, jnp.exp(s_own - m), 0.0)
        l = jnp.sum(w, axis=1, keepdims=True) + jnp.sum(w_own, axis=1, keepdims=True)
        num = jnp.dot(w.astype(jnp.bfloat16), values, preferred_element_type=jnp.float32)
        num = num + jnp.dot(
            w_own.astype(jnp.bfloat16), own_values, preferred_element_type=jnp.float32
        )
        safe = jnp.maximum(l, 1.0)
        o_ref[0, :, h * head_size : (h + 1) * head_size] = (num / safe).astype(o_ref.dtype)
        lse_ref[0, :, h : h + 1] = m + jnp.log(safe)


def prefill_partial(info, queries, keys, values, own_keys, own_values, group_size):
    n, t, qw = queries.shape
    p, hd = keys.shape[1], keys.shape[2]
    own = own_keys.shape[1]
    kern = functools.partial(_prefill_kernel, group_size=group_size, head_size=hd)
    return pl.pallas_call(
        kern,
        grid_spec=pltpu.PrefetchScalarGridSpec(
            num_scalar_prefetch=1,
            grid=(n,),
            in_specs=[
                pl.BlockSpec((1, t, qw), lambda c, info: (c, 0, 0)),
                pl.BlockSpec((1, p, hd), lambda c, info: (c, 0, 0)),
                pl.BlockSpec((1, p, hd), lambda c, info: (c, 0, 0)),
                pl.BlockSpec((1, own, hd), lambda c, info: (c, 0, 0)),
                pl.BlockSpec((1, own, hd), lambda c, info: (c, 0, 0)),
            ],
            out_specs=[
                pl.BlockSpec((1, t, qw), lambda c, info: (c, 0, 0)),
                pl.BlockSpec((1, t, group_size), lambda c, info: (c, 0, 0)),
            ],
        ),
        out_shape=[
            jax.ShapeDtypeStruct((n, t, qw), jnp.bfloat16),
            jax.ShapeDtypeStruct((n, t, group_size), jnp.float32),
        ],
    )(info, queries, keys, values, own_keys, own_values)


def body(
    new_query,
    new_key,
    new_value,
    cache_keys,
    cache_values,
    cache_length,
    dealing,
    out_weight,
    stretch_query,
    stretch_key,
    stretch_value,
    prior_keys,
    prior_values,
    stretch_start,
):
    head_size = cache_keys.shape[2]
    group_size = new_query.shape[1] // head_size
    local_dec = new_query.shape[0]
    seq_rank = lax.axis_index("seq")
    seq_count = lax.axis_size("seq")
    total_dec = local_dec * seq_count
    stretch_count, local_tok, query_width = stretch_query.shape
    key_width = stretch_key.shape[2]
    stretch_rows = stretch_count * local_tok

    decode_kv = jnp.concatenate([new_key, new_value], axis=1)
    decode_kv = jnp.pad(decode_kv, ((0, 0), (0, query_width - 2 * key_width)))
    pack = jnp.concatenate(
        [stretch_query.reshape(stretch_rows, query_width), new_query, decode_kv], axis=0
    )
    gathered = lax.all_to_all(
        jnp.broadcast_to(pack[None], (seq_count,) + pack.shape), "seq", 0, 0, tiled=True
    )
    every_query = gathered[:, stretch_rows : stretch_rows + local_dec, :].reshape(
        total_dec, query_width
    )
    every_kv = gathered[:, stretch_rows + local_dec :, :].reshape(total_dec, query_width)
    every_key = every_kv[:, :key_width]
    every_value = every_kv[:, key_width : 2 * key_width]
    slot_ids = seq_rank * local_dec + jnp.arange(local_dec, dtype=jnp.int32)
    arrival_ids = jnp.arange(total_dec, dtype=jnp.int32)
    sources = jnp.sum(
        jnp.where(dealing[None, :] == slot_ids[:, None], arrival_ids[None, :], 0), axis=1
    )
    home_query = jnp.take(every_query, sources, axis=0)
    home_key = jnp.take(every_key, sources, axis=0)
    home_value = jnp.take(every_value, sources, axis=0)
    cache_span = cache_keys.shape[1]
    cache_pos = jnp.arange(cache_span, dtype=jnp.int32)

    def decode_slot(query_row, own_key, own_value, cached_keys, cached_values, length):
        key_all = jnp.concatenate([cached_keys, own_key[None, :]], axis=0)
        value_all = jnp.concatenate([cached_values, own_value[None, :]], axis=0)
        visible = jnp.concatenate([cache_pos < length, jnp.ones((1,), dtype=jnp.bool_)])
        visible = jnp.broadcast_to(visible[None, :], (group_size, cache_span + 1))
        row_top, weight_sum, numerator = partial_attend(
            query_row.reshape(group_size, head_size), key_all, value_all, visible
        )
        return (
            (numerator / weight_sum[:, None]).astype(jnp.bfloat16).reshape(group_size * head_size)
        )

    home_out = jax.vmap(decode_slot)(
        home_query, home_key, home_value, cache_keys, cache_values, cache_length
    )
    all_out = lax.all_to_all(
        jnp.broadcast_to(home_out[None], (seq_count,) + home_out.shape), "seq", 0, 0, tiled=True
    ).reshape(total_dec, group_size * head_size)
    arrival_out = jnp.take(all_out, dealing, axis=0)
    arrival_terms = jnp.dot(arrival_out, out_weight, preferred_element_type=jnp.float32)
    decode_mixed = lax.psum_scatter(arrival_terms, "tp", scatter_dimension=0, tiled=True).astype(
        jnp.bfloat16
    )

    prior_span = prior_keys.shape[1]
    rows_per_src = local_tok * group_size
    row_count = seq_count * rows_per_src
    prior_pos = seq_rank * prior_span + jnp.arange(prior_span, dtype=jnp.int32)
    queries_all = (
        gathered[:, :stretch_rows, :]
        .reshape(seq_count, stretch_count, local_tok, query_width)
        .transpose(1, 0, 2, 3)
        .reshape(stretch_count, seq_count * local_tok, query_width)
    )
    limits = jnp.clip(stretch_start - seq_rank * prior_span, 0, prior_span).astype(jnp.int32)
    info = jnp.concatenate([limits, (seq_rank * local_tok).astype(jnp.int32)[None]])
    part_out, part_lse = prefill_partial(
        info, queries_all, prior_keys, prior_values, stretch_key, stretch_value, group_size
    )
    part_out = part_out.reshape(stretch_count, row_count, head_size)
    part_lse = part_lse.reshape(stretch_count, row_count)
    lse_hi = lax.reduce_precision(part_lse, exponent_bits=8, mantissa_bits=7)
    lse_rest = part_lse - lse_hi
    lse_mid = lax.reduce_precision(lse_rest, exponent_bits=8, mantissa_bits=7)
    lse_lo = lse_rest - lse_mid
    stat_count = 3 * stretch_count * rows_per_src
    stat_rows = -(-stat_count // head_size)
    stats = (
        jnp.stack([lse_hi, lse_mid, lse_lo])
        .reshape(3, stretch_count, seq_count, rows_per_src)
        .transpose(2, 0, 1, 3)
        .reshape(seq_count, stat_count)
    )
    stats = jnp.pad(stats, ((0, 0), (0, stat_rows * head_size - stat_count))).astype(jnp.bfloat16)

    dec_rows = local_dec * group_size
    out_rows = stretch_count * rows_per_src
    payload = jnp.concatenate(
        [
            part_out.reshape(stretch_count, seq_count, rows_per_src, head_size)
            .transpose(1, 0, 2, 3)
            .reshape(seq_count, out_rows, head_size),
            stats.reshape(seq_count, stat_rows, head_size),
        ],
        axis=1,
    )
    received = lax.all_to_all(payload, "seq", 0, 0, tiled=True)
    got_out = (
        received[:, :out_rows, :]
        .reshape(seq_count, stretch_count, local_tok, group_size, head_size)
        .astype(jnp.float32)
    )
    got_stats = (
        received[:, out_rows : out_rows + stat_rows, :]
        .reshape(seq_count, stat_rows * head_size)[:, :stat_count]
        .astype(jnp.float32)
        .reshape(seq_count, 3, stretch_count, local_tok, group_size)
    )
    got_lse = (got_stats[:, 0] + got_stats[:, 1]) + got_stats[:, 2]

    final_top = jnp.max(got_lse, axis=0)
    part_factor = jnp.exp(got_lse - final_top[None])
    total_sum = jnp.sum(part_factor, axis=0)
    total_num = jnp.sum(got_out * part_factor[..., None], axis=0)
    stretch_out = (
        (total_num / total_sum[..., None])
        .astype(jnp.bfloat16)
        .reshape(stretch_count, local_tok, group_size * head_size)
    )
    return (decode_mixed, stretch_out)


def solution(mesh):
    return jax.shard_map(
        body,
        mesh=mesh,
        in_specs=(
            P("seq", "tp"),
            P("seq", "tp"),
            P("seq", "tp"),
            P("seq", None, "tp"),
            P("seq", None, "tp"),
            P("seq"),
            P(),
            P("tp", "seq"),
            P(None, "seq", "tp"),
            P(None, "seq", "tp"),
            P(None, "seq", "tp"),
            P(None, "seq", "tp"),
            P(None, "seq", "tp"),
            P(),
        ),
        out_specs=(P("tp", "seq"), P(None, "seq", "tp")),
        check_vma=False,
    )
```

```python
import functools
import math

import jax
import jax.numpy as jnp
from jax import lax
from jax.experimental import pallas as pl
from jax.experimental.pallas import tpu as pltpu
from jax.sharding import PartitionSpec as P

NEG_FILL = -1e30


def partial_attend(queries, keys, values, visible):
    factor = 1.0 / math.sqrt(queries.shape[-1])
    scores = jnp.dot(queries, keys.T, preferred_element_type=jnp.float32) * factor
    scores = jnp.where(visible, scores, NEG_FILL)
    row_top = jnp.max(scores, axis=1)
    weights = jnp.where(visible, jnp.exp(scores - row_top[:, None]), 0.0)
    weight_sum = jnp.sum(weights, axis=1)
    numerator = jnp.dot(weights.astype(jnp.bfloat16), values, preferred_element_type=jnp.float32)
    return (row_top, weight_sum, numerator)


def _prefill_kernel(
    info_ref, q_ref, k_ref, v_ref, sk_ref, sv_ref, o_ref, lse_ref, *, group_size, head_size, local_tok
):
    c = pl.program_id(0)
    limit = info_ref[c]
    key_offset = info_ref[info_ref.shape[0] - 1]
    keys = k_ref[0]
    values = v_ref[0]
    own_keys = sk_ref[0]
    own_values = sv_ref[0]
    factor = 1.0 / math.sqrt(head_size)
    src_count, tok_block, _ = q_ref.shape
    tokens = src_count * tok_block
    col = lax.broadcasted_iota(jnp.int32, (1, keys.shape[0]), 1)
    visible = col < limit
    key_token = key_offset + lax.broadcasted_iota(jnp.int32, (tokens, own_keys.shape[0]), 1)
    row = lax.broadcasted_iota(jnp.int32, (tokens, own_keys.shape[0]), 0)
    query_token = (row // tok_block) * local_tok + row % tok_block
    causal = key_token <= query_token
    dims = (((1,), (1,)), ((), ()))
    for h in range(group_size):
        q = q_ref[:, :, h * head_size : (h + 1) * head_size].reshape(tokens, head_size)
        s = lax.dot_general(q, keys, dims, preferred_element_type=jnp.float32) * factor
        s = jnp.where(visible, s, NEG_FILL)
        s_own = lax.dot_general(q, own_keys, dims, preferred_element_type=jnp.float32) * factor
        s_own = jnp.where(causal, s_own, NEG_FILL)
        m = jnp.maximum(
            jnp.max(s, axis=1, keepdims=True), jnp.max(s_own, axis=1, keepdims=True)
        )
        w = jnp.exp(s - m)
        w_own = jnp.exp(s_own - m)
        empty = m < 0.5 * NEG_FILL
        l = jnp.sum(w, axis=1, keepdims=True) + jnp.sum(w_own, axis=1, keepdims=True)
        num = jnp.dot(w.astype(jnp.bfloat16), values, preferred_element_type=jnp.float32)
        num = num + jnp.dot(
            w_own.astype(jnp.bfloat16), own_values, preferred_element_type=jnp.float32
        )
        l = jnp.where(empty, 0.0, l)
        num = jnp.where(empty, 0.0, num)
        safe = jnp.maximum(l, 1.0)
        o_ref[:, :, h * head_size : (h + 1) * head_size] = (
            (num / safe).astype(o_ref.dtype).reshape(src_count, tok_block, head_size)
        )
        lse_ref[0, :, h : h + 1] = m + jnp.log(safe)


def prefill_partial(
    info, queries, keys, values, own_keys, own_values, group_size, tok_block, local_tok, out_rows
):
    src_count, _, qw = queries.shape
    n, p, hd = keys.shape
    own = own_keys.shape[1]
    tokens = src_count * tok_block
    kern = functools.partial(
        _prefill_kernel, group_size=group_size, head_size=hd, local_tok=local_tok
    )
    return pl.pallas_call(
        kern,
        grid_spec=pltpu.PrefetchScalarGridSpec(
            num_scalar_prefetch=1,
            grid=(n,),
            in_specs=[
                pl.BlockSpec((src_count, tok_block, qw), lambda c, info: (0, c, 0)),
                pl.BlockSpec((1, p, hd), lambda c, info: (c, 0, 0)),
                pl.BlockSpec((1, p, hd), lambda c, info: (c, 0, 0)),
                pl.BlockSpec((1, own, hd), lambda c, info: (c, 0, 0)),
                pl.BlockSpec((1, own, hd), lambda c, info: (c, 0, 0)),
            ],
            out_specs=[
                pl.BlockSpec((src_count, tok_block, qw), lambda c, info: (0, c, 0)),
                pl.BlockSpec((1, tokens, group_size), lambda c, info: (c, 0, 0)),
            ],
        ),
        out_shape=[
            jax.ShapeDtypeStruct((src_count, out_rows, qw), jnp.bfloat16),
            jax.ShapeDtypeStruct((n, tokens, group_size), jnp.float32),
        ],
    )(info, queries, keys, values, own_keys, own_values)


def body(
    new_query,
    new_key,
    new_value,
    cache_keys,
    cache_values,
    cache_length,
    dealing,
    out_weight,
    stretch_query,
    stretch_key,
    stretch_value,
    prior_keys,
    prior_values,
    stretch_start,
):
    head_size = cache_keys.shape[2]
    group_size = new_query.shape[1] // head_size
    local_dec = new_query.shape[0]
    seq_rank = lax.axis_index("seq")
    seq_count = lax.axis_size("seq")
    total_dec = local_dec * seq_count
    stretch_count, local_tok, query_width = stretch_query.shape
    key_width = stretch_key.shape[2]
    stretch_rows = stretch_count * local_tok

    decode_kv = jnp.concatenate([new_key, new_value], axis=1)
    decode_kv = jnp.pad(decode_kv, ((0, 0), (0, query_width - 2 * key_width)))
    pack = jnp.concatenate(
        [stretch_query.reshape(stretch_rows, query_width), new_query, decode_kv], axis=0
    )
    gathered = lax.all_to_all(
        jnp.broadcast_to(pack[None], (seq_count,) + pack.shape), "seq", 0, 0, tiled=True
    )
    every_query = gathered[:, stretch_rows : stretch_rows + local_dec, :].reshape(
        total_dec, query_width
    )
    every_kv = gathered[:, stretch_rows + local_dec :, :].reshape(total_dec, query_width)
    every_key = every_kv[:, :key_width]
    every_value = every_kv[:, key_width : 2 * key_width]
    slot_ids = seq_rank * local_dec + jnp.arange(local_dec, dtype=jnp.int32)
    arrival_ids = jnp.arange(total_dec, dtype=jnp.int32)
    sources = jnp.sum(
        jnp.where(dealing[None, :] == slot_ids[:, None], arrival_ids[None, :], 0), axis=1
    )
    home_query = jnp.take(every_query, sources, axis=0)
    home_key = jnp.take(every_key, sources, axis=0)
    home_value = jnp.take(every_value, sources, axis=0)
    cache_span = cache_keys.shape[1]
    cache_pos = jnp.arange(cache_span, dtype=jnp.int32)

    def decode_slot(query_row, own_key, own_value, cached_keys, cached_values, length):
        key_all = jnp.concatenate([cached_keys, own_key[None, :]], axis=0)
        value_all = jnp.concatenate([cached_values, own_value[None, :]], axis=0)
        visible = jnp.concatenate([cache_pos < length, jnp.ones((1,), dtype=jnp.bool_)])
        visible = jnp.broadcast_to(visible[None, :], (group_size, cache_span + 1))
        row_top, weight_sum, numerator = partial_attend(
            query_row.reshape(group_size, head_size), key_all, value_all, visible
        )
        return (
            (numerator / weight_sum[:, None]).astype(jnp.bfloat16).reshape(group_size * head_size)
        )

    home_out = jax.vmap(decode_slot)(
        home_query, home_key, home_value, cache_keys, cache_values, cache_length
    )
    all_out = lax.all_to_all(
        jnp.broadcast_to(home_out[None], (seq_count,) + home_out.shape), "seq", 0, 0, tiled=True
    ).reshape(total_dec, group_size * head_size)
    arrival_out = jnp.take(all_out, dealing, axis=0)
    arrival_terms = jnp.dot(arrival_out, out_weight, preferred_element_type=jnp.float32)
    decode_mixed = lax.psum_scatter(arrival_terms, "tp", scatter_dimension=0, tiled=True).astype(
        jnp.bfloat16
    )

    prior_span = prior_keys.shape[1]
    direct = local_tok % 16 == 0
    stat_count = 3 * stretch_count * local_tok * group_size
    stat_rows = -(-stat_count // query_width)
    out_rows = stretch_rows
    limits = jnp.clip(stretch_start - seq_rank * prior_span, 0, prior_span).astype(jnp.int32)
    info = jnp.concatenate([limits, (seq_rank * local_tok).astype(jnp.int32)[None]])
    if direct:
        payload, part_lse = prefill_partial(
            info, gathered, prior_keys, prior_values, stretch_key, stretch_value, group_size,
            local_tok, local_tok, out_rows + stat_rows,
        )
    else:
        token_count = seq_count * local_tok
        queries_all = (
            gathered[:, :stretch_rows, :]
            .reshape(seq_count, stretch_count, local_tok, query_width)
            .transpose(1, 0, 2, 3)
            .reshape(1, stretch_rows * seq_count, query_width)
        )
        flat_out, part_lse = prefill_partial(
            info, queries_all, prior_keys, prior_values, stretch_key, stretch_value, group_size,
            token_count, token_count, stretch_rows * seq_count,
        )
        payload = jnp.pad(
            flat_out.reshape(stretch_count, seq_count, local_tok, query_width)
            .transpose(1, 0, 2, 3)
            .reshape(seq_count, out_rows, query_width),
            ((0, 0), (0, stat_rows), (0, 0)),
        )
    part_lse = part_lse.reshape(stretch_count, seq_count, local_tok, group_size)
    lse_hi = lax.reduce_precision(part_lse, exponent_bits=8, mantissa_bits=7)
    lse_rest = part_lse - lse_hi
    lse_mid = lax.reduce_precision(lse_rest, exponent_bits=8, mantissa_bits=7)
    lse_lo = lse_rest - lse_mid
    stats = (
        jnp.stack([lse_hi, lse_mid, lse_lo])
        .transpose(2, 0, 1, 3, 4)
        .reshape(seq_count, stat_count)
    )
    stats = jnp.pad(stats, ((0, 0), (0, stat_rows * query_width - stat_count)))
    payload = lax.dynamic_update_slice(
        payload,
        stats.astype(jnp.bfloat16).reshape(seq_count, stat_rows, query_width),
        (0, out_rows, 0),
    )

    received = lax.all_to_all(payload, "seq", 0, 0, tiled=True)
    got_out = received[:, :out_rows, :].reshape(
        seq_count, stretch_count, local_tok, group_size, head_size
    )
    got_stats = (
        received[:, out_rows:, :]
        .reshape(seq_count, stat_rows * query_width)[:, :stat_count]
        .astype(jnp.float32)
        .reshape(seq_count, 3, stretch_count, local_tok, group_size)
    )
    got_lse = (got_stats[:, 0] + got_stats[:, 1]) + got_stats[:, 2]
    final_top = jnp.max(got_lse, axis=0)
    part_factor = jnp.exp(got_lse - final_top[None])
    total_sum = jnp.sum(part_factor, axis=0)
    total_num = jnp.sum(got_out.astype(jnp.float32) * part_factor[..., None], axis=0)
    stretch_out = (
        (total_num / total_sum[..., None])
        .astype(jnp.bfloat16)
        .reshape(stretch_count, local_tok, group_size * head_size)
    )
    return (decode_mixed, stretch_out)


def solution(mesh):
    return jax.shard_map(
        body,
        mesh=mesh,
        in_specs=(
            P("seq", "tp"),
            P("seq", "tp"),
            P("seq", "tp"),
            P("seq", None, "tp"),
            P("seq", None, "tp"),
            P("seq"),
            P(),
            P("tp", "seq"),
            P(None, "seq", "tp"),
            P(None, "seq", "tp"),
            P(None, "seq", "tp"),
            P(None, "seq", "tp"),
            P(None, "seq", "tp"),
            P(),
        ),
        out_specs=(P("tp", "seq"), P(None, "seq", "tp")),
        check_vma=False,
    )
```

```python
import functools
import math

import jax
import jax.numpy as jnp
from jax import lax
from jax.experimental import pallas as pl
from jax.experimental.pallas import tpu as pltpu
from jax.sharding import PartitionSpec as P

NEG_FILL = -1e30


def partial_attend(queries, keys, values, visible):
    factor = 1.0 / math.sqrt(queries.shape[-1])
    scores = jnp.dot(queries, keys.T, preferred_element_type=jnp.float32) * factor
    scores = jnp.where(visible, scores, NEG_FILL)
    row_top = jnp.max(scores, axis=1)
    weights = jnp.where(visible, jnp.exp(scores - row_top[:, None]), 0.0)
    weight_sum = jnp.sum(weights, axis=1)
    numerator = jnp.dot(weights.astype(jnp.bfloat16), values, preferred_element_type=jnp.float32)
    return (row_top, weight_sum, numerator)


def _prefill_kernel(
    info_ref, q_ref, k_ref, v_ref, sk_ref, sv_ref, o_ref, lse_ref, *, group_size, head_size, local_tok
):
    c = pl.program_id(0)
    limit = info_ref[c]
    key_offset = info_ref[info_ref.shape[0] - 1]
    keys = k_ref[0]
    values = v_ref[0]
    own_keys = sk_ref[0]
    own_values = sv_ref[0]
    factor = 1.0 / math.sqrt(head_size)
    src_count, tok_block, _ = q_ref.shape
    tokens = src_count * tok_block
    col = lax.broadcasted_iota(jnp.int32, (1, keys.shape[0]), 1)
    visible = col < limit
    key_token = key_offset + lax.broadcasted_iota(jnp.int32, (tokens, own_keys.shape[0]), 1)
    row = lax.broadcasted_iota(jnp.int32, (tokens, own_keys.shape[0]), 0)
    query_token = (row // tok_block) * local_tok + row % tok_block
    causal = key_token <= query_token
    dims = (((1,), (1,)), ((), ()))
    for h in range(group_size):
        q = q_ref[:, :, h * head_size : (h + 1) * head_size].reshape(tokens, head_size)
        s = lax.dot_general(q, keys, dims, preferred_element_type=jnp.float32) * factor
        s = jnp.where(visible, s, NEG_FILL)
        s_own = lax.dot_general(q, own_keys, dims, preferred_element_type=jnp.float32) * factor
        s_own = jnp.where(causal, s_own, NEG_FILL)
        m = jnp.maximum(
            jnp.max(s, axis=1, keepdims=True), jnp.max(s_own, axis=1, keepdims=True)
        )
        w = jnp.exp(s - m)
        w_own = jnp.exp(s_own - m)
        empty = m < 0.5 * NEG_FILL
        l = jnp.sum(w, axis=1, keepdims=True) + jnp.sum(w_own, axis=1, keepdims=True)
        num = jnp.dot(w.astype(jnp.bfloat16), values, preferred_element_type=jnp.float32)
        num = num + jnp.dot(
            w_own.astype(jnp.bfloat16), own_values, preferred_element_type=jnp.float32
        )
        l = jnp.where(empty, 0.0, l)
        num = jnp.where(empty, 0.0, num)
        safe = jnp.maximum(l, 1.0)
        o_ref[:, :, h * head_size : (h + 1) * head_size] = (
            (num / safe).astype(o_ref.dtype).reshape(src_count, tok_block, head_size)
        )
        lse_ref[0, :, h : h + 1] = m + jnp.log(safe)


def prefill_partial(
    info, queries, keys, values, own_keys, own_values, group_size, tok_block, local_tok, out_rows
):
    src_count, _, qw = queries.shape
    n, p, hd = keys.shape
    own = own_keys.shape[1]
    tokens = src_count * tok_block
    kern = functools.partial(
        _prefill_kernel, group_size=group_size, head_size=hd, local_tok=local_tok
    )
    return pl.pallas_call(
        kern,
        grid_spec=pltpu.PrefetchScalarGridSpec(
            num_scalar_prefetch=1,
            grid=(n,),
            in_specs=[
                pl.BlockSpec((src_count, tok_block, qw), lambda c, info: (0, c, 0)),
                pl.BlockSpec((1, p, hd), lambda c, info: (c, 0, 0)),
                pl.BlockSpec((1, p, hd), lambda c, info: (c, 0, 0)),
                pl.BlockSpec((1, own, hd), lambda c, info: (c, 0, 0)),
                pl.BlockSpec((1, own, hd), lambda c, info: (c, 0, 0)),
            ],
            out_specs=[
                pl.BlockSpec((src_count, tok_block, qw), lambda c, info: (0, c, 0)),
                pl.BlockSpec((1, tokens, group_size), lambda c, info: (c, 0, 0)),
            ],
        ),
        out_shape=[
            jax.ShapeDtypeStruct((src_count, out_rows, qw), jnp.bfloat16),
            jax.ShapeDtypeStruct((n, tokens, group_size), jnp.float32),
        ],
    )(info, queries, keys, values, own_keys, own_values)


def _combine_kernel(o_ref, lse_ref, out_ref, *, group_size, head_size):
    stretch_count, local_tok, _ = out_ref.shape
    for c in range(stretch_count):
        lse = lse_ref[:, c]
        top = jnp.max(lse, axis=0, keepdims=True)
        weights = jnp.exp(lse - top)
        total = jnp.sum(weights, axis=0)
        for h in range(group_size):
            part = o_ref[
                :, c * local_tok : (c + 1) * local_tok, h * head_size : (h + 1) * head_size
            ].astype(jnp.float32)
            num = jnp.sum(part * weights[:, :, h : h + 1], axis=0)
            out_ref[c, :, h * head_size : (h + 1) * head_size] = (
                num / total[:, h : h + 1]
            ).astype(out_ref.dtype)


def combine_partials(received, lse, group_size, head_size):
    _, stretch_count, local_tok, _ = lse.shape
    kern = functools.partial(_combine_kernel, group_size=group_size, head_size=head_size)
    return pl.pallas_call(
        kern,
        out_shape=jax.ShapeDtypeStruct(
            (stretch_count, local_tok, group_size * head_size), jnp.bfloat16
        ),
    )(received, lse)


def body(
    new_query,
    new_key,
    new_value,
    cache_keys,
    cache_values,
    cache_length,
    dealing,
    out_weight,
    stretch_query,
    stretch_key,
    stretch_value,
    prior_keys,
    prior_values,
    stretch_start,
):
    head_size = cache_keys.shape[2]
    group_size = new_query.shape[1] // head_size
    local_dec = new_query.shape[0]
    seq_rank = lax.axis_index("seq")
    seq_count = lax.axis_size("seq")
    total_dec = local_dec * seq_count
    stretch_count, local_tok, query_width = stretch_query.shape
    key_width = stretch_key.shape[2]
    stretch_rows = stretch_count * local_tok

    decode_kv = jnp.concatenate([new_key, new_value], axis=1)
    decode_kv = jnp.pad(decode_kv, ((0, 0), (0, query_width - 2 * key_width)))
    pack = jnp.concatenate(
        [stretch_query.reshape(stretch_rows, query_width), new_query, decode_kv], axis=0
    )
    gathered = lax.all_to_all(
        jnp.broadcast_to(pack[None], (seq_count,) + pack.shape), "seq", 0, 0, tiled=True
    )
    every_query = gathered[:, stretch_rows : stretch_rows + local_dec, :].reshape(
        total_dec, query_width
    )
    every_kv = gathered[:, stretch_rows + local_dec :, :].reshape(total_dec, query_width)
    every_key = every_kv[:, :key_width]
    every_value = every_kv[:, key_width : 2 * key_width]
    slot_ids = seq_rank * local_dec + jnp.arange(local_dec, dtype=jnp.int32)
    arrival_ids = jnp.arange(total_dec, dtype=jnp.int32)
    sources = jnp.sum(
        jnp.where(dealing[None, :] == slot_ids[:, None], arrival_ids[None, :], 0), axis=1
    )
    home_query = jnp.take(every_query, sources, axis=0)
    home_key = jnp.take(every_key, sources, axis=0)
    home_value = jnp.take(every_value, sources, axis=0)
    cache_span = cache_keys.shape[1]
    cache_pos = jnp.arange(cache_span, dtype=jnp.int32)

    def decode_slot(query_row, own_key, own_value, cached_keys, cached_values, length):
        key_all = jnp.concatenate([cached_keys, own_key[None, :]], axis=0)
        value_all = jnp.concatenate([cached_values, own_value[None, :]], axis=0)
        visible = jnp.concatenate([cache_pos < length, jnp.ones((1,), dtype=jnp.bool_)])
        visible = jnp.broadcast_to(visible[None, :], (group_size, cache_span + 1))
        row_top, weight_sum, numerator = partial_attend(
            query_row.reshape(group_size, head_size), key_all, value_all, visible
        )
        return (
            (numerator / weight_sum[:, None]).astype(jnp.bfloat16).reshape(group_size * head_size)
        )

    home_out = jax.vmap(decode_slot)(
        home_query, home_key, home_value, cache_keys, cache_values, cache_length
    )
    all_out = lax.all_to_all(
        jnp.broadcast_to(home_out[None], (seq_count,) + home_out.shape), "seq", 0, 0, tiled=True
    ).reshape(total_dec, group_size * head_size)
    arrival_out = jnp.take(all_out, dealing, axis=0)
    arrival_terms = jnp.dot(arrival_out, out_weight, preferred_element_type=jnp.float32)
    decode_mixed = lax.psum_scatter(arrival_terms, "tp", scatter_dimension=0, tiled=True).astype(
        jnp.bfloat16
    )

    prior_span = prior_keys.shape[1]
    direct = local_tok % 16 == 0
    stat_count = 3 * stretch_count * local_tok * group_size
    stat_rows = -(-stat_count // query_width)
    out_rows = stretch_rows
    limits = jnp.clip(stretch_start - seq_rank * prior_span, 0, prior_span).astype(jnp.int32)
    info = jnp.concatenate([limits, (seq_rank * local_tok).astype(jnp.int32)[None]])
    if direct:
        payload, part_lse = prefill_partial(
            info, gathered, prior_keys, prior_values, stretch_key, stretch_value, group_size,
            local_tok, local_tok, out_rows + stat_rows,
        )
    else:
        token_count = seq_count * local_tok
        queries_all = (
            gathered[:, :stretch_rows, :]
            .reshape(seq_count, stretch_count, local_tok, query_width)
            .transpose(1, 0, 2, 3)
            .reshape(1, stretch_rows * seq_count, query_width)
        )
        flat_out, part_lse = prefill_partial(
            info, queries_all, prior_keys, prior_values, stretch_key, stretch_value, group_size,
            token_count, token_count, stretch_rows * seq_count,
        )
        payload = jnp.pad(
            flat_out.reshape(stretch_count, seq_count, local_tok, query_width)
            .transpose(1, 0, 2, 3)
            .reshape(seq_count, out_rows, query_width),
            ((0, 0), (0, stat_rows), (0, 0)),
        )
    part_lse = part_lse.reshape(stretch_count, seq_count, local_tok, group_size)
    lse_hi = lax.reduce_precision(part_lse, exponent_bits=8, mantissa_bits=7)
    lse_rest = part_lse - lse_hi
    lse_mid = lax.reduce_precision(lse_rest, exponent_bits=8, mantissa_bits=7)
    lse_lo = lse_rest - lse_mid
    stats = (
        jnp.stack([lse_hi, lse_mid, lse_lo])
        .transpose(2, 0, 1, 3, 4)
        .reshape(seq_count, stat_count)
    )
    stats = jnp.pad(stats, ((0, 0), (0, stat_rows * query_width - stat_count)))
    payload = lax.dynamic_update_slice(
        payload,
        stats.astype(jnp.bfloat16).reshape(seq_count, stat_rows, query_width),
        (0, out_rows, 0),
    )

    received = lax.all_to_all(payload, "seq", 0, 0, tiled=True)
    got_stats = (
        received[:, out_rows:, :]
        .reshape(seq_count, stat_rows * query_width)[:, :stat_count]
        .astype(jnp.float32)
        .reshape(seq_count, 3, stretch_count, local_tok, group_size)
    )
    got_lse = (got_stats[:, 0] + got_stats[:, 1]) + got_stats[:, 2]
    stretch_out = combine_partials(received, got_lse, group_size, head_size)
    return (decode_mixed, stretch_out)


def solution(mesh):
    return jax.shard_map(
        body,
        mesh=mesh,
        in_specs=(
            P("seq", "tp"),
            P("seq", "tp"),
            P("seq", "tp"),
            P("seq", None, "tp"),
            P("seq", None, "tp"),
            P("seq"),
            P(),
            P("tp", "seq"),
            P(None, "seq", "tp"),
            P(None, "seq", "tp"),
            P(None, "seq", "tp"),
            P(None, "seq", "tp"),
            P(None, "seq", "tp"),
            P(),
        ),
        out_specs=(P("tp", "seq"), P(None, "seq", "tp")),
        check_vma=False,
    )
```

```python
import functools
import math

import jax
import jax.numpy as jnp
from jax import lax
from jax.experimental import pallas as pl
from jax.experimental.pallas import tpu as pltpu
from jax.sharding import PartitionSpec as P

NEG_FILL = -1e30


def partial_attend(queries, keys, values, visible):
    factor = 1.0 / math.sqrt(queries.shape[-1])
    scores = jnp.dot(queries, keys.T, preferred_element_type=jnp.float32) * factor
    scores = jnp.where(visible, scores, NEG_FILL)
    row_top = jnp.max(scores, axis=1)
    weights = jnp.where(visible, jnp.exp(scores - row_top[:, None]), 0.0)
    weight_sum = jnp.sum(weights, axis=1)
    numerator = jnp.dot(weights.astype(jnp.bfloat16), values, preferred_element_type=jnp.float32)
    return (row_top, weight_sum, numerator)


def _prefill_kernel(
    info_ref, q_ref, k_ref, v_ref, sk_ref, sv_ref, o_ref, lse_ref, *, group_size, head_size, local_tok
):
    c = pl.program_id(0)
    limit = info_ref[c]
    key_offset = info_ref[info_ref.shape[0] - 1]
    keys = k_ref[0]
    values = v_ref[0]
    own_keys = sk_ref[0]
    own_values = sv_ref[0]
    factor = 1.0 / math.sqrt(head_size)
    src_count, tok_block, _ = q_ref.shape
    tokens = src_count * tok_block
    col = lax.broadcasted_iota(jnp.int32, (1, keys.shape[0]), 1)
    visible = col < limit
    key_token = key_offset + lax.broadcasted_iota(jnp.int32, (tokens, own_keys.shape[0]), 1)
    row = lax.broadcasted_iota(jnp.int32, (tokens, own_keys.shape[0]), 0)
    query_token = (row // tok_block) * local_tok + row % tok_block
    causal = key_token <= query_token
    dims = (((1,), (1,)), ((), ()))

    def heads(masked):
        for h in range(group_size):
            q = q_ref[:, :, h * head_size : (h + 1) * head_size].reshape(tokens, head_size)
            s = lax.dot_general(q, keys, dims, preferred_element_type=jnp.float32) * factor
            if masked:
                s = jnp.where(visible, s, NEG_FILL)
            s_own = lax.dot_general(q, own_keys, dims, preferred_element_type=jnp.float32) * factor
            s_own = jnp.where(causal, s_own, NEG_FILL)
            m = jnp.maximum(
                jnp.max(s, axis=1, keepdims=True), jnp.max(s_own, axis=1, keepdims=True)
            )
            w = jnp.exp(s - m)
            w_own = jnp.exp(s_own - m)
            empty = m < 0.5 * NEG_FILL
            l = jnp.sum(w, axis=1, keepdims=True) + jnp.sum(w_own, axis=1, keepdims=True)
            num = jnp.dot(w.astype(jnp.bfloat16), values, preferred_element_type=jnp.float32)
            num = num + jnp.dot(
                w_own.astype(jnp.bfloat16), own_values, preferred_element_type=jnp.float32
            )
            l = jnp.where(empty, 0.0, l)
            num = jnp.where(empty, 0.0, num)
            safe = jnp.maximum(l, 1.0)
            o_ref[:, :, h * head_size : (h + 1) * head_size] = (
                (num / safe).astype(o_ref.dtype).reshape(src_count, tok_block, head_size)
            )
            lse_ref[0, :, h : h + 1] = m + jnp.log(safe)

    whole_block = limit >= keys.shape[0]

    @pl.when(whole_block)
    def _():
        heads(False)

    @pl.when(jnp.logical_not(whole_block))
    def _():
        heads(True)


def prefill_partial(
    info, queries, keys, values, own_keys, own_values, group_size, tok_block, local_tok, out_rows
):
    src_count, _, qw = queries.shape
    n, p, hd = keys.shape
    own = own_keys.shape[1]
    tokens = src_count * tok_block
    kern = functools.partial(
        _prefill_kernel, group_size=group_size, head_size=hd, local_tok=local_tok
    )
    return pl.pallas_call(
        kern,
        grid_spec=pltpu.PrefetchScalarGridSpec(
            num_scalar_prefetch=1,
            grid=(n,),
            in_specs=[
                pl.BlockSpec((src_count, tok_block, qw), lambda c, info: (0, c, 0)),
                pl.BlockSpec((1, p, hd), lambda c, info: (c, 0, 0)),
                pl.BlockSpec((1, p, hd), lambda c, info: (c, 0, 0)),
                pl.BlockSpec((1, own, hd), lambda c, info: (c, 0, 0)),
                pl.BlockSpec((1, own, hd), lambda c, info: (c, 0, 0)),
            ],
            out_specs=[
                pl.BlockSpec((src_count, tok_block, qw), lambda c, info: (0, c, 0)),
                pl.BlockSpec((1, tokens, group_size), lambda c, info: (c, 0, 0)),
            ],
        ),
        out_shape=[
            jax.ShapeDtypeStruct((src_count, out_rows, qw), jnp.bfloat16),
            jax.ShapeDtypeStruct((n, tokens, group_size), jnp.float32),
        ],
    )(info, queries, keys, values, own_keys, own_values)


def _combine_kernel(o_ref, lse_ref, out_ref, *, group_size, head_size):
    stretch_count, local_tok, _ = out_ref.shape
    for c in range(stretch_count):
        lse = lse_ref[:, c]
        top = jnp.max(lse, axis=0, keepdims=True)
        weights = jnp.exp(lse - top)
        total = jnp.sum(weights, axis=0)
        for h in range(group_size):
            part = o_ref[
                :, c * local_tok : (c + 1) * local_tok, h * head_size : (h + 1) * head_size
            ].astype(jnp.float32)
            num = jnp.sum(part * weights[:, :, h : h + 1], axis=0)
            out_ref[c, :, h * head_size : (h + 1) * head_size] = (
                num / total[:, h : h + 1]
            ).astype(out_ref.dtype)


def combine_partials(received, lse, group_size, head_size):
    _, stretch_count, local_tok, _ = lse.shape
    kern = functools.partial(_combine_kernel, group_size=group_size, head_size=head_size)
    return pl.pallas_call(
        kern,
        out_shape=jax.ShapeDtypeStruct(
            (stretch_count, local_tok, group_size * head_size), jnp.bfloat16
        ),
    )(received, lse)


def body(
    new_query,
    new_key,
    new_value,
    cache_keys,
    cache_values,
    cache_length,
    dealing,
    out_weight,
    stretch_query,
    stretch_key,
    stretch_value,
    prior_keys,
    prior_values,
    stretch_start,
):
    head_size = cache_keys.shape[2]
    group_size = new_query.shape[1] // head_size
    local_dec = new_query.shape[0]
    seq_rank = lax.axis_index("seq")
    seq_count = lax.axis_size("seq")
    total_dec = local_dec * seq_count
    stretch_count, local_tok, query_width = stretch_query.shape
    key_width = stretch_key.shape[2]
    stretch_rows = stretch_count * local_tok

    decode_kv = jnp.concatenate([new_key, new_value], axis=1)
    decode_kv = jnp.pad(decode_kv, ((0, 0), (0, query_width - 2 * key_width)))
    pack = jnp.concatenate(
        [stretch_query.reshape(stretch_rows, query_width), new_query, decode_kv], axis=0
    )
    gathered = lax.all_to_all(
        jnp.broadcast_to(pack[None], (seq_count,) + pack.shape), "seq", 0, 0, tiled=True
    )
    every_query = gathered[:, stretch_rows : stretch_rows + local_dec, :].reshape(
        total_dec, query_width
    )
    every_kv = gathered[:, stretch_rows + local_dec :, :].reshape(total_dec, query_width)
    every_key = every_kv[:, :key_width]
    every_value = every_kv[:, key_width : 2 * key_width]
    slot_ids = seq_rank * local_dec + jnp.arange(local_dec, dtype=jnp.int32)
    arrival_ids = jnp.arange(total_dec, dtype=jnp.int32)
    sources = jnp.sum(
        jnp.where(dealing[None, :] == slot_ids[:, None], arrival_ids[None, :], 0), axis=1
    )
    home_query = jnp.take(every_query, sources, axis=0)
    home_key = jnp.take(every_key, sources, axis=0)
    home_value = jnp.take(every_value, sources, axis=0)
    cache_span = cache_keys.shape[1]
    cache_pos = jnp.arange(cache_span, dtype=jnp.int32)

    def decode_slot(query_row, own_key, own_value, cached_keys, cached_values, length):
        key_all = jnp.concatenate([cached_keys, own_key[None, :]], axis=0)
        value_all = jnp.concatenate([cached_values, own_value[None, :]], axis=0)
        visible = jnp.concatenate([cache_pos < length, jnp.ones((1,), dtype=jnp.bool_)])
        visible = jnp.broadcast_to(visible[None, :], (group_size, cache_span + 1))
        row_top, weight_sum, numerator = partial_attend(
            query_row.reshape(group_size, head_size), key_all, value_all, visible
        )
        return (
            (numerator / weight_sum[:, None]).astype(jnp.bfloat16).reshape(group_size * head_size)
        )

    home_out = jax.vmap(decode_slot)(
        home_query, home_key, home_value, cache_keys, cache_values, cache_length
    )
    all_out = lax.all_to_all(
        jnp.broadcast_to(home_out[None], (seq_count,) + home_out.shape), "seq", 0, 0, tiled=True
    ).reshape(total_dec, group_size * head_size)
    arrival_out = jnp.take(all_out, dealing, axis=0)
    arrival_terms = jnp.dot(arrival_out, out_weight, preferred_element_type=jnp.float32)
    decode_mixed = lax.psum_scatter(arrival_terms, "tp", scatter_dimension=0, tiled=True).astype(
        jnp.bfloat16
    )

    prior_span = prior_keys.shape[1]
    direct = local_tok % 16 == 0
    stat_count = 3 * stretch_count * local_tok * group_size
    stat_rows = -(-stat_count // query_width)
    out_rows = stretch_rows
    limits = jnp.clip(stretch_start - seq_rank * prior_span, 0, prior_span).astype(jnp.int32)
    info = jnp.concatenate([limits, (seq_rank * local_tok).astype(jnp.int32)[None]])
    if direct:
        payload, part_lse = prefill_partial(
            info, gathered, prior_keys, prior_values, stretch_key, stretch_value, group_size,
            local_tok, local_tok, out_rows + stat_rows,
        )
    else:
        token_count = seq_count * local_tok
        queries_all = (
            gathered[:, :stretch_rows, :]
            .reshape(seq_count, stretch_count, local_tok, query_width)
            .transpose(1, 0, 2, 3)
            .reshape(1, stretch_rows * seq_count, query_width)
        )
        flat_out, part_lse = prefill_partial(
            info, queries_all, prior_keys, prior_values, stretch_key, stretch_value, group_size,
            token_count, token_count, stretch_rows * seq_count,
        )
        payload = jnp.pad(
            flat_out.reshape(stretch_count, seq_count, local_tok, query_width)
            .transpose(1, 0, 2, 3)
            .reshape(seq_count, out_rows, query_width),
            ((0, 0), (0, stat_rows), (0, 0)),
        )
    part_lse = part_lse.reshape(stretch_count, seq_count, local_tok, group_size)
    lse_hi = lax.reduce_precision(part_lse, exponent_bits=8, mantissa_bits=7)
    lse_rest = part_lse - lse_hi
    lse_mid = lax.reduce_precision(lse_rest, exponent_bits=8, mantissa_bits=7)
    lse_lo = lse_rest - lse_mid
    stats = (
        jnp.stack([lse_hi, lse_mid, lse_lo])
        .transpose(2, 0, 1, 3, 4)
        .reshape(seq_count, stat_count)
    )
    stats = jnp.pad(stats, ((0, 0), (0, stat_rows * query_width - stat_count)))
    payload = lax.dynamic_update_slice(
        payload,
        stats.astype(jnp.bfloat16).reshape(seq_count, stat_rows, query_width),
        (0, out_rows, 0),
    )

    received = lax.all_to_all(payload, "seq", 0, 0, tiled=True)
    got_stats = (
        received[:, out_rows:, :]
        .reshape(seq_count, stat_rows * query_width)[:, :stat_count]
        .astype(jnp.float32)
        .reshape(seq_count, 3, stretch_count, local_tok, group_size)
    )
    got_lse = (got_stats[:, 0] + got_stats[:, 1]) + got_stats[:, 2]
    stretch_out = combine_partials(received, got_lse, group_size, head_size)
    return (decode_mixed, stretch_out)


def solution(mesh):
    return jax.shard_map(
        body,
        mesh=mesh,
        in_specs=(
            P("seq", "tp"),
            P("seq", "tp"),
            P("seq", "tp"),
            P("seq", None, "tp"),
            P("seq", None, "tp"),
            P("seq"),
            P(),
            P("tp", "seq"),
            P(None, "seq", "tp"),
            P(None, "seq", "tp"),
            P(None, "seq", "tp"),
            P(None, "seq", "tp"),
            P(None, "seq", "tp"),
            P(),
        ),
        out_specs=(P("tp", "seq"), P(None, "seq", "tp")),
        check_vma=False,
    )
```

```python
import functools
import math

import jax
import jax.numpy as jnp
from jax import lax
from jax.experimental import pallas as pl
from jax.experimental.pallas import tpu as pltpu
from jax.sharding import PartitionSpec as P

NEG_FILL = -1e30


def partial_attend(queries, keys, values, visible):
    factor = 1.0 / math.sqrt(queries.shape[-1])
    scores = jnp.dot(queries, keys.T, preferred_element_type=jnp.float32) * factor
    scores = jnp.where(visible, scores, NEG_FILL)
    row_top = jnp.max(scores, axis=1)
    weights = jnp.where(visible, jnp.exp(scores - row_top[:, None]), 0.0)
    weight_sum = jnp.sum(weights, axis=1)
    numerator = jnp.dot(weights.astype(jnp.bfloat16), values, preferred_element_type=jnp.float32)
    return (row_top, weight_sum, numerator)


def _prefill_kernel(
    info_ref, q_ref, k_ref, v_ref, sk_ref, sv_ref, o_ref, lse_ref, *, group_size, head_size, local_tok
):
    c = pl.program_id(0)
    limit = info_ref[c]
    key_offset = info_ref[info_ref.shape[0] - 1]
    keys = k_ref[0]
    values = v_ref[0]
    own_keys = sk_ref[0]
    own_values = sv_ref[0]
    factor = 1.0 / math.sqrt(head_size)
    src_count, tok_block, _ = q_ref.shape
    tokens = src_count * tok_block
    col = lax.broadcasted_iota(jnp.int32, (1, keys.shape[0]), 1)
    visible = col < limit
    key_token = key_offset + lax.broadcasted_iota(jnp.int32, (tokens, own_keys.shape[0]), 1)
    row = lax.broadcasted_iota(jnp.int32, (tokens, own_keys.shape[0]), 0)
    query_token = (row // tok_block) * local_tok + row % tok_block
    causal = key_token <= query_token
    dims = (((1,), (1,)), ((), ()))
    for h in range(group_size):
        q = q_ref[:, :, h * head_size : (h + 1) * head_size].reshape(tokens, head_size)
        s = lax.dot_general(q, keys, dims, preferred_element_type=jnp.float32) * factor
        s = jnp.where(visible, s, NEG_FILL)
        s_own = lax.dot_general(q, own_keys, dims, preferred_element_type=jnp.float32) * factor
        s_own = jnp.where(causal, s_own, NEG_FILL)
        m = jnp.maximum(
            jnp.max(s, axis=1, keepdims=True), jnp.max(s_own, axis=1, keepdims=True)
        )
        w = jnp.exp(s - m)
        w_own = jnp.exp(s_own - m)
        empty = m < 0.5 * NEG_FILL
        l = jnp.sum(w, axis=1, keepdims=True) + jnp.sum(w_own, axis=1, keepdims=True)
        num = jnp.dot(w.astype(jnp.bfloat16), values, preferred_element_type=jnp.float32)
        num = num + jnp.dot(
            w_own.astype(jnp.bfloat16), own_values, preferred_element_type=jnp.float32
        )
        l = jnp.where(empty, 0.0, l)
        num = jnp.where(empty, 0.0, num)
        safe = jnp.maximum(l, 1.0)
        o_ref[:, :, h * head_size : (h + 1) * head_size] = (
            (num / safe).astype(o_ref.dtype).reshape(src_count, tok_block, head_size)
        )
        lse_ref[0, :, h : h + 1] = m + jnp.log(safe)


def prefill_partial(
    info, queries, keys, values, own_keys, own_values, group_size, tok_block, local_tok, out_rows
):
    src_count, _, qw = queries.shape
    n, p, hd = keys.shape
    own = own_keys.shape[1]
    tokens = src_count * tok_block
    kern = functools.partial(
        _prefill_kernel, group_size=group_size, head_size=hd, local_tok=local_tok
    )
    return pl.pallas_call(
        kern,
        grid_spec=pltpu.PrefetchScalarGridSpec(
            num_scalar_prefetch=1,
            grid=(n,),
            in_specs=[
                pl.BlockSpec((src_count, tok_block, qw), lambda c, info: (0, c, 0)),
                pl.BlockSpec((1, p, hd), lambda c, info: (c, 0, 0)),
                pl.BlockSpec((1, p, hd), lambda c, info: (c, 0, 0)),
                pl.BlockSpec((1, own, hd), lambda c, info: (c, 0, 0)),
                pl.BlockSpec((1, own, hd), lambda c, info: (c, 0, 0)),
            ],
            out_specs=[
                pl.BlockSpec((src_count, tok_block, qw), lambda c, info: (0, c, 0)),
                pl.BlockSpec((1, tokens, group_size), lambda c, info: (c, 0, 0)),
            ],
        ),
        out_shape=[
            jax.ShapeDtypeStruct((src_count, out_rows, qw), jnp.bfloat16),
            jax.ShapeDtypeStruct((n, tokens, group_size), jnp.float32),
        ],
    )(info, queries, keys, values, own_keys, own_values)


def _combine_kernel(o_ref, lse_ref, out_ref, *, group_size, head_size):
    stretch_count, local_tok, _ = out_ref.shape
    for c in range(stretch_count):
        lse = lse_ref[:, c]
        top = jnp.max(lse, axis=0, keepdims=True)
        weights = jnp.exp(lse - top)
        total = jnp.sum(weights, axis=0)
        for h in range(group_size):
            part = o_ref[
                :, c * local_tok : (c + 1) * local_tok, h * head_size : (h + 1) * head_size
            ].astype(jnp.float32)
            num = jnp.sum(part * weights[:, :, h : h + 1], axis=0)
            out_ref[c, :, h * head_size : (h + 1) * head_size] = (
                num / total[:, h : h + 1]
            ).astype(out_ref.dtype)


def combine_partials(received, lse, group_size, head_size):
    _, stretch_count, local_tok, _ = lse.shape
    kern = functools.partial(_combine_kernel, group_size=group_size, head_size=head_size)
    return pl.pallas_call(
        kern,
        out_shape=jax.ShapeDtypeStruct(
            (stretch_count, local_tok, group_size * head_size), jnp.bfloat16
        ),
    )(received, lse)


def broadcast_over_seq(pack, seq_rank, seq_count):
    if seq_count > 16 or seq_count % 2:
        return lax.all_to_all(
            jnp.broadcast_to(pack[None], (seq_count,) + pack.shape), "seq", 0, 0, tiled=True
        )
    half = seq_count // 2
    partner = lax.ppermute(pack, "seq", [(i, (i + half) % seq_count) for i in range(seq_count)])
    pair = jnp.stack([pack, partner])
    pieces = [pair]
    for shift in range(1, half):
        perm = [(i, (i // half) * half + (i % half + shift) % half) for i in range(seq_count)]
        pieces.append(lax.ppermute(pair, "seq", perm))
    every = jnp.stack(pieces).reshape((2 * half,) + pack.shape)
    sources = jnp.arange(seq_count, dtype=jnp.int32)
    far = (sources // half) != (seq_rank // half)
    near = jnp.where(far, (sources + half) % seq_count, sources)
    shift_of = (seq_rank % half - near % half) % half
    return jnp.take(every, shift_of * 2 + far.astype(jnp.int32), axis=0)


def body(
    new_query,
    new_key,
    new_value,
    cache_keys,
    cache_values,
    cache_length,
    dealing,
    out_weight,
    stretch_query,
    stretch_key,
    stretch_value,
    prior_keys,
    prior_values,
    stretch_start,
):
    head_size = cache_keys.shape[2]
    group_size = new_query.shape[1] // head_size
    local_dec = new_query.shape[0]
    seq_rank = lax.axis_index("seq")
    seq_count = lax.axis_size("seq")
    total_dec = local_dec * seq_count
    stretch_count, local_tok, query_width = stretch_query.shape
    key_width = stretch_key.shape[2]
    stretch_rows = stretch_count * local_tok

    decode_kv = jnp.concatenate([new_key, new_value], axis=1)
    decode_kv = jnp.pad(decode_kv, ((0, 0), (0, query_width - 2 * key_width)))
    pack = jnp.concatenate(
        [stretch_query.reshape(stretch_rows, query_width), new_query, decode_kv], axis=0
    )
    gathered = broadcast_over_seq(pack, seq_rank, seq_count)
    every_query = gathered[:, stretch_rows : stretch_rows + local_dec, :].reshape(
        total_dec, query_width
    )
    every_kv = gathered[:, stretch_rows + local_dec :, :].reshape(total_dec, query_width)
    every_key = every_kv[:, :key_width]
    every_value = every_kv[:, key_width : 2 * key_width]
    slot_ids = seq_rank * local_dec + jnp.arange(local_dec, dtype=jnp.int32)
    arrival_ids = jnp.arange(total_dec, dtype=jnp.int32)
    sources = jnp.sum(
        jnp.where(dealing[None, :] == slot_ids[:, None], arrival_ids[None, :], 0), axis=1
    )
    home_query = jnp.take(every_query, sources, axis=0)
    home_key = jnp.take(every_key, sources, axis=0)
    home_value = jnp.take(every_value, sources, axis=0)
    cache_span = cache_keys.shape[1]
    cache_pos = jnp.arange(cache_span, dtype=jnp.int32)

    def decode_slot(query_row, own_key, own_value, cached_keys, cached_values, length):
        key_all = jnp.concatenate([cached_keys, own_key[None, :]], axis=0)
        value_all = jnp.concatenate([cached_values, own_value[None, :]], axis=0)
        visible = jnp.concatenate([cache_pos < length, jnp.ones((1,), dtype=jnp.bool_)])
        visible = jnp.broadcast_to(visible[None, :], (group_size, cache_span + 1))
        row_top, weight_sum, numerator = partial_attend(
            query_row.reshape(group_size, head_size), key_all, value_all, visible
        )
        return (
            (numerator / weight_sum[:, None]).astype(jnp.bfloat16).reshape(group_size * head_size)
        )

    home_out = jax.vmap(decode_slot)(
        home_query, home_key, home_value, cache_keys, cache_values, cache_length
    )
    all_out = lax.all_to_all(
        jnp.broadcast_to(home_out[None], (seq_count,) + home_out.shape), "seq", 0, 0, tiled=True
    ).reshape(total_dec, group_size * head_size)
    arrival_out = jnp.take(all_out, dealing, axis=0)
    arrival_terms = jnp.dot(arrival_out, out_weight, preferred_element_type=jnp.float32)
    decode_mixed = lax.psum_scatter(arrival_terms, "tp", scatter_dimension=0, tiled=True).astype(
        jnp.bfloat16
    )

    prior_span = prior_keys.shape[1]
    direct = local_tok % 16 == 0
    stat_count = 3 * stretch_count * local_tok * group_size
    stat_rows = -(-stat_count // query_width)
    out_rows = stretch_rows
    limits = jnp.clip(stretch_start - seq_rank * prior_span, 0, prior_span).astype(jnp.int32)
    info = jnp.concatenate([limits, (seq_rank * local_tok).astype(jnp.int32)[None]])
    if direct:
        payload, part_lse = prefill_partial(
            info, gathered, prior_keys, prior_values, stretch_key, stretch_value, group_size,
            local_tok, local_tok, out_rows + stat_rows,
        )
    else:
        token_count = seq_count * local_tok
        queries_all = (
            gathered[:, :stretch_rows, :]
            .reshape(seq_count, stretch_count, local_tok, query_width)
            .transpose(1, 0, 2, 3)
            .reshape(1, stretch_rows * seq_count, query_width)
        )
        flat_out, part_lse = prefill_partial(
            info, queries_all, prior_keys, prior_values, stretch_key, stretch_value, group_size,
            token_count, token_count, stretch_rows * seq_count,
        )
        payload = jnp.pad(
            flat_out.reshape(stretch_count, seq_count, local_tok, query_width)
            .transpose(1, 0, 2, 3)
            .reshape(seq_count, out_rows, query_width),
            ((0, 0), (0, stat_rows), (0, 0)),
        )
    part_lse = part_lse.reshape(stretch_count, seq_count, local_tok, group_size)
    lse_hi = lax.reduce_precision(part_lse, exponent_bits=8, mantissa_bits=7)
    lse_rest = part_lse - lse_hi
    lse_mid = lax.reduce_precision(lse_rest, exponent_bits=8, mantissa_bits=7)
    lse_lo = lse_rest - lse_mid
    stats = (
        jnp.stack([lse_hi, lse_mid, lse_lo])
        .transpose(2, 0, 1, 3, 4)
        .reshape(seq_count, stat_count)
    )
    stats = jnp.pad(stats, ((0, 0), (0, stat_rows * query_width - stat_count)))
    payload = lax.dynamic_update_slice(
        payload,
        stats.astype(jnp.bfloat16).reshape(seq_count, stat_rows, query_width),
        (0, out_rows, 0),
    )

    received = lax.all_to_all(payload, "seq", 0, 0, tiled=True)
    got_stats = (
        received[:, out_rows:, :]
        .reshape(seq_count, stat_rows * query_width)[:, :stat_count]
        .astype(jnp.float32)
        .reshape(seq_count, 3, stretch_count, local_tok, group_size)
    )
    got_lse = (got_stats[:, 0] + got_stats[:, 1]) + got_stats[:, 2]
    stretch_out = combine_partials(received, got_lse, group_size, head_size)
    return (decode_mixed, stretch_out)


def solution(mesh):
    return jax.shard_map(
        body,
        mesh=mesh,
        in_specs=(
            P("seq", "tp"),
            P("seq", "tp"),
            P("seq", "tp"),
            P("seq", None, "tp"),
            P("seq", None, "tp"),
            P("seq"),
            P(),
            P("tp", "seq"),
            P(None, "seq", "tp"),
            P(None, "seq", "tp"),
            P(None, "seq", "tp"),
            P(None, "seq", "tp"),
            P(None, "seq", "tp"),
            P(),
        ),
        out_specs=(P("tp", "seq"), P(None, "seq", "tp")),
        check_vma=False,
    )
```

```python
import functools
import math

import jax
import jax.numpy as jnp
from jax import lax
from jax.experimental import pallas as pl
from jax.experimental.pallas import tpu as pltpu
from jax.sharding import PartitionSpec as P

NEG_FILL = -1e30


def partial_attend(queries, keys, values, visible):
    factor = 1.0 / math.sqrt(queries.shape[-1])
    scores = jnp.dot(queries, keys.T, preferred_element_type=jnp.float32) * factor
    scores = jnp.where(visible, scores, NEG_FILL)
    row_top = jnp.max(scores, axis=1)
    weights = jnp.where(visible, jnp.exp(scores - row_top[:, None]), 0.0)
    weight_sum = jnp.sum(weights, axis=1)
    numerator = jnp.dot(weights.astype(jnp.bfloat16), values, preferred_element_type=jnp.float32)
    return (row_top, weight_sum, numerator)


def _prefill_kernel(
    info_ref, q_ref, k_ref, v_ref, sk_ref, sv_ref, o_ref, lse_ref, *, group_size, head_size, local_tok
):
    c = pl.program_id(0)
    limit = info_ref[c]
    key_offset = info_ref[info_ref.shape[0] - 1]
    keys = k_ref[0]
    values = v_ref[0]
    own_keys = sk_ref[0]
    own_values = sv_ref[0]
    factor = 1.0 / math.sqrt(head_size)
    src_count, tok_block, _ = q_ref.shape
    tokens = src_count * tok_block
    col = lax.broadcasted_iota(jnp.int32, (1, keys.shape[0]), 1)
    visible = col < limit
    key_token = key_offset + lax.broadcasted_iota(jnp.int32, (tokens, own_keys.shape[0]), 1)
    row = lax.broadcasted_iota(jnp.int32, (tokens, own_keys.shape[0]), 0)
    query_token = (row // tok_block) * local_tok + row % tok_block
    causal = key_token <= query_token
    dims = (((1,), (1,)), ((), ()))
    for h in range(group_size):
        q = q_ref[:, :, h * head_size : (h + 1) * head_size].reshape(tokens, head_size)
        s = lax.dot_general(q, keys, dims, preferred_element_type=jnp.float32) * factor
        s = jnp.where(visible, s, NEG_FILL)
        s_own = lax.dot_general(q, own_keys, dims, preferred_element_type=jnp.float32) * factor
        s_own = jnp.where(causal, s_own, NEG_FILL)
        m = jnp.maximum(
            jnp.max(s, axis=1, keepdims=True), jnp.max(s_own, axis=1, keepdims=True)
        )
        w = jnp.exp(s - m)
        w_own = jnp.exp(s_own - m)
        empty = m < 0.5 * NEG_FILL
        l = jnp.sum(w, axis=1, keepdims=True) + jnp.sum(w_own, axis=1, keepdims=True)
        num = jnp.dot(w.astype(jnp.bfloat16), values, preferred_element_type=jnp.float32)
        num = num + jnp.dot(
            w_own.astype(jnp.bfloat16), own_values, preferred_element_type=jnp.float32
        )
        l = jnp.where(empty, 0.0, l)
        num = jnp.where(empty, 0.0, num)
        safe = jnp.maximum(l, 1.0)
        o_ref[:, :, h * head_size : (h + 1) * head_size] = (
            (num / safe).astype(o_ref.dtype).reshape(src_count, tok_block, head_size)
        )
        lse_ref[0, :, h : h + 1] = m + jnp.log(safe)


def prefill_partial(
    info, queries, keys, values, own_keys, own_values, group_size, tok_block, local_tok, out_rows
):
    src_count, _, qw = queries.shape
    n, p, hd = keys.shape
    own = own_keys.shape[1]
    tokens = src_count * tok_block
    kern = functools.partial(
        _prefill_kernel, group_size=group_size, head_size=hd, local_tok=local_tok
    )
    return pl.pallas_call(
        kern,
        grid_spec=pltpu.PrefetchScalarGridSpec(
            num_scalar_prefetch=1,
            grid=(n,),
            in_specs=[
                pl.BlockSpec((src_count, tok_block, qw), lambda c, info: (0, c, 0)),
                pl.BlockSpec((1, p, hd), lambda c, info: (c, 0, 0)),
                pl.BlockSpec((1, p, hd), lambda c, info: (c, 0, 0)),
                pl.BlockSpec((1, own, hd), lambda c, info: (c, 0, 0)),
                pl.BlockSpec((1, own, hd), lambda c, info: (c, 0, 0)),
            ],
            out_specs=[
                pl.BlockSpec((src_count, tok_block, qw), lambda c, info: (0, c, 0)),
                pl.BlockSpec((1, tokens, group_size), lambda c, info: (c, 0, 0)),
            ],
        ),
        out_shape=[
            jax.ShapeDtypeStruct((src_count, out_rows, qw), jnp.bfloat16),
            jax.ShapeDtypeStruct((n, tokens, group_size), jnp.float32),
        ],
    )(info, queries, keys, values, own_keys, own_values)


def _combine_kernel(o_ref, lse_ref, out_ref, *, group_size, head_size):
    stretch_count, local_tok, _ = out_ref.shape
    for c in range(stretch_count):
        lse = lse_ref[:, c]
        top = jnp.max(lse, axis=0, keepdims=True)
        weights = jnp.exp(lse - top)
        total = jnp.sum(weights, axis=0)
        for h in range(group_size):
            part = o_ref[
                :, c * local_tok : (c + 1) * local_tok, h * head_size : (h + 1) * head_size
            ].astype(jnp.float32)
            num = jnp.sum(part * weights[:, :, h : h + 1], axis=0)
            out_ref[c, :, h * head_size : (h + 1) * head_size] = (
                num / total[:, h : h + 1]
            ).astype(out_ref.dtype)


def combine_partials(received, lse, group_size, head_size):
    _, stretch_count, local_tok, _ = lse.shape
    kern = functools.partial(_combine_kernel, group_size=group_size, head_size=head_size)
    return pl.pallas_call(
        kern,
        out_shape=jax.ShapeDtypeStruct(
            (stretch_count, local_tok, group_size * head_size), jnp.bfloat16
        ),
    )(received, lse)


def broadcast_over_seq(pack, seq_rank, seq_count):
    if seq_count > 16 or seq_count % 2:
        return lax.all_to_all(
            jnp.broadcast_to(pack[None], (seq_count,) + pack.shape), "seq", 0, 0, tiled=True
        )
    half = seq_count // 2
    partner = lax.ppermute(pack, "seq", [(i, (i + half) % seq_count) for i in range(seq_count)])
    pair = jnp.stack([pack, partner])
    pieces = [pair]
    for shift in range(1, half):
        perm = [(i, (i // half) * half + (i % half + shift) % half) for i in range(seq_count)]
        pieces.append(lax.ppermute(pair, "seq", perm))
    every = jnp.stack(pieces).reshape((2 * half,) + pack.shape)
    sources = jnp.arange(seq_count, dtype=jnp.int32)
    far = (sources // half) != (seq_rank // half)
    near = jnp.where(far, (sources + half) % seq_count, sources)
    shift_of = (seq_rank % half - near % half) % half
    return jnp.take(every, shift_of * 2 + far.astype(jnp.int32), axis=0)


def body(
    new_query,
    new_key,
    new_value,
    cache_keys,
    cache_values,
    cache_length,
    dealing,
    out_weight,
    stretch_query,
    stretch_key,
    stretch_value,
    prior_keys,
    prior_values,
    stretch_start,
):
    head_size = cache_keys.shape[2]
    group_size = new_query.shape[1] // head_size
    local_dec = new_query.shape[0]
    seq_rank = lax.axis_index("seq")
    seq_count = lax.axis_size("seq")
    total_dec = local_dec * seq_count
    stretch_count, local_tok, query_width = stretch_query.shape
    key_width = stretch_key.shape[2]
    stretch_rows = stretch_count * local_tok

    decode_kv = jnp.concatenate([new_key, new_value], axis=1)
    decode_kv = jnp.pad(decode_kv, ((0, 0), (0, query_width - 2 * key_width)))
    pack = jnp.concatenate(
        [stretch_query.reshape(stretch_rows, query_width), new_query, decode_kv], axis=0
    )
    gathered = broadcast_over_seq(pack, seq_rank, seq_count)
    every_query = gathered[:, stretch_rows : stretch_rows + local_dec, :].reshape(
        total_dec, query_width
    )
    every_kv = gathered[:, stretch_rows + local_dec :, :].reshape(total_dec, query_width)
    every_key = every_kv[:, :key_width]
    every_value = every_kv[:, key_width : 2 * key_width]
    slot_ids = seq_rank * local_dec + jnp.arange(local_dec, dtype=jnp.int32)
    arrival_ids = jnp.arange(total_dec, dtype=jnp.int32)
    sources = jnp.sum(
        jnp.where(dealing[None, :] == slot_ids[:, None], arrival_ids[None, :], 0), axis=1
    )
    home_query = jnp.take(every_query, sources, axis=0)
    home_key = jnp.take(every_key, sources, axis=0)
    home_value = jnp.take(every_value, sources, axis=0)
    cache_span = cache_keys.shape[1]
    cache_pos = jnp.arange(cache_span, dtype=jnp.int32)

    def decode_slot(query_row, own_key, own_value, cached_keys, cached_values, length):
        key_all = jnp.concatenate([cached_keys, own_key[None, :]], axis=0)
        value_all = jnp.concatenate([cached_values, own_value[None, :]], axis=0)
        visible = jnp.concatenate([cache_pos < length, jnp.ones((1,), dtype=jnp.bool_)])
        visible = jnp.broadcast_to(visible[None, :], (group_size, cache_span + 1))
        row_top, weight_sum, numerator = partial_attend(
            query_row.reshape(group_size, head_size), key_all, value_all, visible
        )
        return (
            (numerator / weight_sum[:, None]).astype(jnp.bfloat16).reshape(group_size * head_size)
        )

    home_out = jax.vmap(decode_slot)(
        home_query, home_key, home_value, cache_keys, cache_values, cache_length
    )
    all_out = broadcast_over_seq(home_out, seq_rank, seq_count).reshape(
        total_dec, group_size * head_size
    )
    arrival_out = jnp.take(all_out, dealing, axis=0)
    arrival_terms = jnp.dot(arrival_out, out_weight, preferred_element_type=jnp.float32)
    decode_mixed = lax.psum_scatter(arrival_terms, "tp", scatter_dimension=0, tiled=True).astype(
        jnp.bfloat16
    )

    prior_span = prior_keys.shape[1]
    direct = local_tok % 16 == 0
    stat_count = 3 * stretch_count * local_tok * group_size
    stat_rows = -(-stat_count // query_width)
    out_rows = stretch_rows
    limits = jnp.clip(stretch_start - seq_rank * prior_span, 0, prior_span).astype(jnp.int32)
    info = jnp.concatenate([limits, (seq_rank * local_tok).astype(jnp.int32)[None]])
    if direct:
        payload, part_lse = prefill_partial(
            info, gathered, prior_keys, prior_values, stretch_key, stretch_value, group_size,
            local_tok, local_tok, out_rows + stat_rows,
        )
    else:
        token_count = seq_count * local_tok
        queries_all = (
            gathered[:, :stretch_rows, :]
            .reshape(seq_count, stretch_count, local_tok, query_width)
            .transpose(1, 0, 2, 3)
            .reshape(1, stretch_rows * seq_count, query_width)
        )
        flat_out, part_lse = prefill_partial(
            info, queries_all, prior_keys, prior_values, stretch_key, stretch_value, group_size,
            token_count, token_count, stretch_rows * seq_count,
        )
        payload = jnp.pad(
            flat_out.reshape(stretch_count, seq_count, local_tok, query_width)
            .transpose(1, 0, 2, 3)
            .reshape(seq_count, out_rows, query_width),
            ((0, 0), (0, stat_rows), (0, 0)),
        )
    part_lse = part_lse.reshape(stretch_count, seq_count, local_tok, group_size)
    lse_hi = lax.reduce_precision(part_lse, exponent_bits=8, mantissa_bits=7)
    lse_rest = part_lse - lse_hi
    lse_mid = lax.reduce_precision(lse_rest, exponent_bits=8, mantissa_bits=7)
    lse_lo = lse_rest - lse_mid
    stats = (
        jnp.stack([lse_hi, lse_mid, lse_lo])
        .transpose(2, 0, 1, 3, 4)
        .reshape(seq_count, stat_count)
    )
    stats = jnp.pad(stats, ((0, 0), (0, stat_rows * query_width - stat_count)))
    payload = lax.dynamic_update_slice(
        payload,
        stats.astype(jnp.bfloat16).reshape(seq_count, stat_rows, query_width),
        (0, out_rows, 0),
    )

    received = lax.all_to_all(payload, "seq", 0, 0, tiled=True)
    got_stats = (
        received[:, out_rows:, :]
        .reshape(seq_count, stat_rows * query_width)[:, :stat_count]
        .astype(jnp.float32)
        .reshape(seq_count, 3, stretch_count, local_tok, group_size)
    )
    got_lse = (got_stats[:, 0] + got_stats[:, 1]) + got_stats[:, 2]
    stretch_out = combine_partials(received, got_lse, group_size, head_size)
    return (decode_mixed, stretch_out)


def solution(mesh):
    return jax.shard_map(
        body,
        mesh=mesh,
        in_specs=(
            P("seq", "tp"),
            P("seq", "tp"),
            P("seq", "tp"),
            P("seq", None, "tp"),
            P("seq", None, "tp"),
            P("seq"),
            P(),
            P("tp", "seq"),
            P(None, "seq", "tp"),
            P(None, "seq", "tp"),
            P(None, "seq", "tp"),
            P(None, "seq", "tp"),
            P(None, "seq", "tp"),
            P(),
        ),
        out_specs=(P("tp", "seq"), P(None, "seq", "tp")),
        check_vma=False,
    )
```

```python
import functools
import math

import jax
import jax.numpy as jnp
from jax import lax
from jax.experimental import pallas as pl
from jax.experimental.pallas import tpu as pltpu
from jax.sharding import PartitionSpec as P

NEG_FILL = -1e30


def partial_attend(queries, keys, values, visible):
    factor = 1.0 / math.sqrt(queries.shape[-1])
    scores = jnp.dot(queries, keys.T, preferred_element_type=jnp.float32) * factor
    scores = jnp.where(visible, scores, NEG_FILL)
    row_top = jnp.max(scores, axis=1)
    weights = jnp.where(visible, jnp.exp(scores - row_top[:, None]), 0.0)
    weight_sum = jnp.sum(weights, axis=1)
    numerator = jnp.dot(weights.astype(jnp.bfloat16), values, preferred_element_type=jnp.float32)
    return (row_top, weight_sum, numerator)


def _prefill_kernel(
    info_ref, q_ref, k_ref, v_ref, sk_ref, sv_ref, o_ref, lse_ref, *, group_size, head_size, local_tok
):
    c = pl.program_id(0)
    limit = info_ref[c]
    key_offset = info_ref[info_ref.shape[0] - 1]
    keys = k_ref[0]
    values = v_ref[0]
    own_keys = sk_ref[0]
    own_values = sv_ref[0]
    factor = 1.0 / math.sqrt(head_size)
    src_count, tok_block, _ = q_ref.shape
    tokens = src_count * tok_block
    col = lax.broadcasted_iota(jnp.int32, (1, keys.shape[0]), 1)
    visible = col < limit
    key_token = key_offset + lax.broadcasted_iota(jnp.int32, (tokens, own_keys.shape[0]), 1)
    row = lax.broadcasted_iota(jnp.int32, (tokens, own_keys.shape[0]), 0)
    query_token = (row // tok_block) * local_tok + row % tok_block
    causal = key_token <= query_token
    dims = (((1,), (1,)), ((), ()))
    for h in range(group_size):
        q = q_ref[:, :, h * head_size : (h + 1) * head_size].reshape(tokens, head_size)
        s = lax.dot_general(q, keys, dims, preferred_element_type=jnp.float32) * factor
        s = jnp.where(visible, s, NEG_FILL)
        s_own = lax.dot_general(q, own_keys, dims, preferred_element_type=jnp.float32) * factor
        s_own = jnp.where(causal, s_own, NEG_FILL)
        m = jnp.maximum(
            jnp.max(s, axis=1, keepdims=True), jnp.max(s_own, axis=1, keepdims=True)
        )
        w = jnp.exp(s - m)
        w_own = jnp.exp(s_own - m)
        empty = m < 0.5 * NEG_FILL
        l = jnp.sum(w, axis=1, keepdims=True) + jnp.sum(w_own, axis=1, keepdims=True)
        num = jnp.dot(w.astype(jnp.bfloat16), values, preferred_element_type=jnp.float32)
        num = num + jnp.dot(
            w_own.astype(jnp.bfloat16), own_values, preferred_element_type=jnp.float32
        )
        l = jnp.where(empty, 0.0, l)
        num = jnp.where(empty, 0.0, num)
        safe = jnp.maximum(l, 1.0)
        o_ref[:, :, h * head_size : (h + 1) * head_size] = (
            (num / safe).astype(o_ref.dtype).reshape(src_count, tok_block, head_size)
        )
        lse_ref[0, :, h : h + 1] = m + jnp.log(safe)


def prefill_partial(
    info, queries, keys, values, own_keys, own_values, group_size, tok_block, local_tok, out_rows
):
    src_count, _, qw = queries.shape
    n, p, hd = keys.shape
    own = own_keys.shape[1]
    tokens = src_count * tok_block
    kern = functools.partial(
        _prefill_kernel, group_size=group_size, head_size=hd, local_tok=local_tok
    )
    return pl.pallas_call(
        kern,
        grid_spec=pltpu.PrefetchScalarGridSpec(
            num_scalar_prefetch=1,
            grid=(n,),
            in_specs=[
                pl.BlockSpec((src_count, tok_block, qw), lambda c, info: (0, c, 0)),
                pl.BlockSpec((1, p, hd), lambda c, info: (c, 0, 0)),
                pl.BlockSpec((1, p, hd), lambda c, info: (c, 0, 0)),
                pl.BlockSpec((1, own, hd), lambda c, info: (c, 0, 0)),
                pl.BlockSpec((1, own, hd), lambda c, info: (c, 0, 0)),
            ],
            out_specs=[
                pl.BlockSpec((src_count, tok_block, qw), lambda c, info: (0, c, 0)),
                pl.BlockSpec((1, tokens, group_size), lambda c, info: (c, 0, 0)),
            ],
        ),
        out_shape=[
            jax.ShapeDtypeStruct((src_count, out_rows, qw), jnp.bfloat16),
            jax.ShapeDtypeStruct((n, tokens, group_size), jnp.float32),
        ],
    )(info, queries, keys, values, own_keys, own_values)


def _combine_kernel(o_ref, lse_ref, out_ref, *, group_size, head_size):
    stretch_count, local_tok, _ = out_ref.shape
    for c in range(stretch_count):
        lse = lse_ref[:, c]
        top = jnp.max(lse, axis=0, keepdims=True)
        weights = jnp.exp(lse - top)
        total = jnp.sum(weights, axis=0)
        for h in range(group_size):
            part = o_ref[
                :, c * local_tok : (c + 1) * local_tok, h * head_size : (h + 1) * head_size
            ].astype(jnp.float32)
            num = jnp.sum(part * weights[:, :, h : h + 1], axis=0)
            out_ref[c, :, h * head_size : (h + 1) * head_size] = (
                num / total[:, h : h + 1]
            ).astype(out_ref.dtype)


def combine_partials(received, lse, group_size, head_size):
    _, stretch_count, local_tok, _ = lse.shape
    kern = functools.partial(_combine_kernel, group_size=group_size, head_size=head_size)
    return pl.pallas_call(
        kern,
        out_shape=jax.ShapeDtypeStruct(
            (stretch_count, local_tok, group_size * head_size), jnp.bfloat16
        ),
    )(received, lse)


def broadcast_over_seq(pack, seq_rank, seq_count):
    if seq_count > 16 or seq_count % 2:
        return lax.all_to_all(
            jnp.broadcast_to(pack[None], (seq_count,) + pack.shape), "seq", 0, 0, tiled=True
        )
    half = seq_count // 2
    partner = lax.ppermute(pack, "seq", [(i, (i + half) % seq_count) for i in range(seq_count)])
    pair = jnp.stack([pack, partner])
    pieces = [pair]
    for shift in range(1, half):
        perm = [(i, (i // half) * half + (i % half + shift) % half) for i in range(seq_count)]
        pieces.append(lax.ppermute(pair, "seq", perm))
    every = jnp.stack(pieces).reshape((2 * half,) + pack.shape)
    sources = jnp.arange(seq_count, dtype=jnp.int32)
    far = (sources // half) != (seq_rank // half)
    near = jnp.where(far, (sources + half) % seq_count, sources)
    shift_of = (seq_rank % half - near % half) % half
    return jnp.take(every, shift_of * 2 + far.astype(jnp.int32), axis=0, mode="clip")


def body(
    new_query,
    new_key,
    new_value,
    cache_keys,
    cache_values,
    cache_length,
    dealing,
    out_weight,
    stretch_query,
    stretch_key,
    stretch_value,
    prior_keys,
    prior_values,
    stretch_start,
):
    head_size = cache_keys.shape[2]
    group_size = new_query.shape[1] // head_size
    local_dec = new_query.shape[0]
    seq_rank = lax.axis_index("seq")
    seq_count = lax.axis_size("seq")
    total_dec = local_dec * seq_count
    stretch_count, local_tok, query_width = stretch_query.shape
    key_width = stretch_key.shape[2]
    stretch_rows = stretch_count * local_tok

    decode_kv = jnp.concatenate([new_key, new_value], axis=1)
    decode_kv = jnp.pad(decode_kv, ((0, 0), (0, query_width - 2 * key_width)))
    pack = jnp.concatenate(
        [stretch_query.reshape(stretch_rows, query_width), new_query, decode_kv], axis=0
    )
    gathered = broadcast_over_seq(pack, seq_rank, seq_count)
    every_query = gathered[:, stretch_rows : stretch_rows + local_dec, :].reshape(
        total_dec, query_width
    )
    every_kv = gathered[:, stretch_rows + local_dec :, :].reshape(total_dec, query_width)
    every_key = every_kv[:, :key_width]
    every_value = every_kv[:, key_width : 2 * key_width]
    slot_ids = seq_rank * local_dec + jnp.arange(local_dec, dtype=jnp.int32)
    arrival_ids = jnp.arange(total_dec, dtype=jnp.int32)
    sources = jnp.sum(
        jnp.where(dealing[None, :] == slot_ids[:, None], arrival_ids[None, :], 0), axis=1
    )
    home_query = jnp.take(every_query, sources, axis=0)
    home_key = jnp.take(every_key, sources, axis=0)
    home_value = jnp.take(every_value, sources, axis=0)
    cache_span = cache_keys.shape[1]
    cache_pos = jnp.arange(cache_span, dtype=jnp.int32)

    def decode_slot(query_row, own_key, own_value, cached_keys, cached_values, length):
        key_all = jnp.concatenate([cached_keys, own_key[None, :]], axis=0)
        value_all = jnp.concatenate([cached_values, own_value[None, :]], axis=0)
        visible = jnp.concatenate([cache_pos < length, jnp.ones((1,), dtype=jnp.bool_)])
        visible = jnp.broadcast_to(visible[None, :], (group_size, cache_span + 1))
        row_top, weight_sum, numerator = partial_attend(
            query_row.reshape(group_size, head_size), key_all, value_all, visible
        )
        return (
            (numerator / weight_sum[:, None]).astype(jnp.bfloat16).reshape(group_size * head_size)
        )

    home_out = jax.vmap(decode_slot)(
        home_query, home_key, home_value, cache_keys, cache_values, cache_length
    )
    all_out = lax.all_to_all(
        jnp.broadcast_to(home_out[None], (seq_count,) + home_out.shape), "seq", 0, 0, tiled=True
    ).reshape(total_dec, group_size * head_size)
    arrival_out = jnp.take(all_out, dealing, axis=0)
    arrival_terms = jnp.dot(arrival_out, out_weight, preferred_element_type=jnp.float32)
    decode_mixed = lax.psum_scatter(arrival_terms, "tp", scatter_dimension=0, tiled=True).astype(
        jnp.bfloat16
    )

    prior_span = prior_keys.shape[1]
    direct = local_tok % 16 == 0
    stat_count = 3 * stretch_count * local_tok * group_size
    stat_rows = -(-stat_count // query_width)
    out_rows = stretch_rows
    limits = jnp.clip(stretch_start - seq_rank * prior_span, 0, prior_span).astype(jnp.int32)
    info = jnp.concatenate([limits, (seq_rank * local_tok).astype(jnp.int32)[None]])
    if direct:
        payload, part_lse = prefill_partial(
            info, gathered, prior_keys, prior_values, stretch_key, stretch_value, group_size,
            local_tok, local_tok, out_rows + stat_rows,
        )
    else:
        token_count = seq_count * local_tok
        queries_all = (
            gathered[:, :stretch_rows, :]
            .reshape(seq_count, stretch_count, local_tok, query_width)
            .transpose(1, 0, 2, 3)
            .reshape(1, stretch_rows * seq_count, query_width)
        )
        flat_out, part_lse = prefill_partial(
            info, queries_all, prior_keys, prior_values, stretch_key, stretch_value, group_size,
            token_count, token_count, stretch_rows * seq_count,
        )
        payload = jnp.pad(
            flat_out.reshape(stretch_count, seq_count, local_tok, query_width)
            .transpose(1, 0, 2, 3)
            .reshape(seq_count, out_rows, query_width),
            ((0, 0), (0, stat_rows), (0, 0)),
        )
    part_lse = part_lse.reshape(stretch_count, seq_count, local_tok, group_size)
    lse_hi = lax.reduce_precision(part_lse, exponent_bits=8, mantissa_bits=7)
    lse_rest = part_lse - lse_hi
    lse_mid = lax.reduce_precision(lse_rest, exponent_bits=8, mantissa_bits=7)
    lse_lo = lse_rest - lse_mid
    stats = (
        jnp.stack([lse_hi, lse_mid, lse_lo])
        .transpose(2, 0, 1, 3, 4)
        .reshape(seq_count, stat_count)
    )
    stats = jnp.pad(stats, ((0, 0), (0, stat_rows * query_width - stat_count)))
    payload = lax.dynamic_update_slice(
        payload,
        stats.astype(jnp.bfloat16).reshape(seq_count, stat_rows, query_width),
        (0, out_rows, 0),
    )

    received = lax.all_to_all(payload, "seq", 0, 0, tiled=True)
    got_stats = (
        received[:, out_rows:, :]
        .reshape(seq_count, stat_rows * query_width)[:, :stat_count]
        .astype(jnp.float32)
        .reshape(seq_count, 3, stretch_count, local_tok, group_size)
    )
    got_lse = (got_stats[:, 0] + got_stats[:, 1]) + got_stats[:, 2]
    stretch_out = combine_partials(received, got_lse, group_size, head_size)
    return (decode_mixed, stretch_out)


def solution(mesh):
    return jax.shard_map(
        body,
        mesh=mesh,
        in_specs=(
            P("seq", "tp"),
            P("seq", "tp"),
            P("seq", "tp"),
            P("seq", None, "tp"),
            P("seq", None, "tp"),
            P("seq"),
            P(),
            P("tp", "seq"),
            P(None, "seq", "tp"),
            P(None, "seq", "tp"),
            P(None, "seq", "tp"),
            P(None, "seq", "tp"),
            P(None, "seq", "tp"),
            P(),
        ),
        out_specs=(P("tp", "seq"), P(None, "seq", "tp")),
        check_vma=False,
    )
```

```python
import functools
import math

import jax
import jax.numpy as jnp
from jax import lax
from jax.experimental import pallas as pl
from jax.experimental.pallas import tpu as pltpu
from jax.sharding import PartitionSpec as P

NEG_FILL = -1e30


def partial_attend(queries, keys, values, visible):
    factor = 1.0 / math.sqrt(queries.shape[-1])
    scores = jnp.dot(queries, keys.T, preferred_element_type=jnp.float32) * factor
    scores = jnp.where(visible, scores, NEG_FILL)
    row_top = jnp.max(scores, axis=1)
    weights = jnp.where(visible, jnp.exp(scores - row_top[:, None]), 0.0)
    weight_sum = jnp.sum(weights, axis=1)
    numerator = jnp.dot(weights.astype(jnp.bfloat16), values, preferred_element_type=jnp.float32)
    return (row_top, weight_sum, numerator)


def _prefill_kernel(
    info_ref, order_ref, q_hbm, k_ref, v_ref, sk_ref, sv_ref, o_ref, lse_ref, q_ref, sems,
    *, group_size, head_size, local_tok
):
    c = pl.program_id(0)
    stretch_count, src_count, tok_block, _ = q_ref.shape

    def query_copy(stretch, src):
        return pltpu.make_async_copy(
            q_hbm.at[order_ref[src], pl.ds(stretch * tok_block, tok_block)],
            q_ref.at[stretch, src],
            sems.at[stretch, src],
        )

    @pl.when(c == 0)
    def _():
        for stretch in range(stretch_count):
            for src in range(src_count):
                query_copy(stretch, src).start()

    for src in range(src_count):
        query_copy(c, src).wait()
    limit = info_ref[c]
    key_offset = info_ref[info_ref.shape[0] - 1]
    keys = k_ref[0]
    values = v_ref[0]
    own_keys = sk_ref[0]
    own_values = sv_ref[0]
    factor = 1.0 / math.sqrt(head_size)
    tokens = src_count * tok_block
    col = lax.broadcasted_iota(jnp.int32, (1, keys.shape[0]), 1)
    visible = col < limit
    key_token = key_offset + lax.broadcasted_iota(jnp.int32, (tokens, own_keys.shape[0]), 1)
    row = lax.broadcasted_iota(jnp.int32, (tokens, own_keys.shape[0]), 0)
    query_token = (row // tok_block) * local_tok + row % tok_block
    causal = key_token <= query_token
    dims = (((1,), (1,)), ((), ()))
    for h in range(group_size):
        q = q_ref[c, :, :, h * head_size : (h + 1) * head_size].reshape(tokens, head_size)
        s = lax.dot_general(q, keys, dims, preferred_element_type=jnp.float32) * factor
        s = jnp.where(visible, s, NEG_FILL)
        s_own = lax.dot_general(q, own_keys, dims, preferred_element_type=jnp.float32) * factor
        s_own = jnp.where(causal, s_own, NEG_FILL)
        m = jnp.maximum(
            jnp.max(s, axis=1, keepdims=True), jnp.max(s_own, axis=1, keepdims=True)
        )
        w = jnp.exp(s - m)
        w_own = jnp.exp(s_own - m)
        empty = m < 0.5 * NEG_FILL
        l = jnp.sum(w, axis=1, keepdims=True) + jnp.sum(w_own, axis=1, keepdims=True)
        num = jnp.dot(w.astype(jnp.bfloat16), values, preferred_element_type=jnp.float32)
        num = num + jnp.dot(
            w_own.astype(jnp.bfloat16), own_values, preferred_element_type=jnp.float32
        )
        l = jnp.where(empty, 0.0, l)
        num = jnp.where(empty, 0.0, num)
        safe = jnp.maximum(l, 1.0)
        o_ref[:, :, h * head_size : (h + 1) * head_size] = (
            (num / safe).astype(o_ref.dtype).reshape(src_count, tok_block, head_size)
        )
        lse_ref[0, :, h : h + 1] = m + jnp.log(safe)


def prefill_partial(
    info, order, queries, keys, values, own_keys, own_values, group_size, tok_block, local_tok,
    out_rows,
):
    src_count = order.shape[0]
    qw = queries.shape[2]
    n, p, hd = keys.shape
    own = own_keys.shape[1]
    tokens = src_count * tok_block
    kern = functools.partial(
        _prefill_kernel, group_size=group_size, head_size=hd, local_tok=local_tok
    )
    return pl.pallas_call(
        kern,
        grid_spec=pltpu.PrefetchScalarGridSpec(
            num_scalar_prefetch=2,
            grid=(n,),
            in_specs=[
                pl.BlockSpec(memory_space=pl.ANY),
                pl.BlockSpec((1, p, hd), lambda c, info, order: (c, 0, 0)),
                pl.BlockSpec((1, p, hd), lambda c, info, order: (c, 0, 0)),
                pl.BlockSpec((1, own, hd), lambda c, info, order: (c, 0, 0)),
                pl.BlockSpec((1, own, hd), lambda c, info, order: (c, 0, 0)),
            ],
            out_specs=[
                pl.BlockSpec((src_count, tok_block, qw), lambda c, info, order: (0, c, 0)),
                pl.BlockSpec((1, tokens, group_size), lambda c, info, order: (c, 0, 0)),
            ],
            scratch_shapes=[
                pltpu.VMEM((n, src_count, tok_block, qw), jnp.bfloat16),
                pltpu.SemaphoreType.DMA((n, src_count)),
            ],
        ),
        out_shape=[
            jax.ShapeDtypeStruct((src_count, out_rows, qw), jnp.bfloat16),
            jax.ShapeDtypeStruct((n, tokens, group_size), jnp.float32),
        ],
    )(info, order, queries, keys, values, own_keys, own_values)


def _combine_kernel(o_ref, lse_ref, out_ref, *, group_size, head_size):
    stretch_count, local_tok, _ = out_ref.shape
    for c in range(stretch_count):
        lse = lse_ref[:, c]
        top = jnp.max(lse, axis=0, keepdims=True)
        weights = jnp.exp(lse - top)
        total = jnp.sum(weights, axis=0)
        for h in range(group_size):
            part = o_ref[
                :, c * local_tok : (c + 1) * local_tok, h * head_size : (h + 1) * head_size
            ].astype(jnp.float32)
            num = jnp.sum(part * weights[:, :, h : h + 1], axis=0)
            out_ref[c, :, h * head_size : (h + 1) * head_size] = (
                num / total[:, h : h + 1]
            ).astype(out_ref.dtype)


def combine_partials(received, lse, group_size, head_size):
    _, stretch_count, local_tok, _ = lse.shape
    kern = functools.partial(_combine_kernel, group_size=group_size, head_size=head_size)
    return pl.pallas_call(
        kern,
        out_shape=jax.ShapeDtypeStruct(
            (stretch_count, local_tok, group_size * head_size), jnp.bfloat16
        ),
    )(received, lse)


def broadcast_over_seq(pack, seq_rank, seq_count):
    if seq_count > 16 or seq_count % 2:
        every = lax.all_to_all(
            jnp.broadcast_to(pack[None], (seq_count,) + pack.shape), "seq", 0, 0, tiled=True
        )
        return every, jnp.arange(seq_count, dtype=jnp.int32)
    half = seq_count // 2
    partner = lax.ppermute(pack, "seq", [(i, (i + half) % seq_count) for i in range(seq_count)])
    pair = jnp.stack([pack, partner])
    pieces = [pair]
    for shift in range(1, half):
        perm = [(i, (i // half) * half + (i % half + shift) % half) for i in range(seq_count)]
        pieces.append(lax.ppermute(pair, "seq", perm))
    every = jnp.stack(pieces).reshape((2 * half,) + pack.shape)
    sources = jnp.arange(seq_count, dtype=jnp.int32)
    far = (sources // half) != (seq_rank // half)
    near = jnp.where(far, (sources + half) % seq_count, sources)
    shift_of = (seq_rank % half - near % half) % half
    return every, (shift_of * 2 + far.astype(jnp.int32)).astype(jnp.int32)


def body(
    new_query,
    new_key,
    new_value,
    cache_keys,
    cache_values,
    cache_length,
    dealing,
    out_weight,
    stretch_query,
    stretch_key,
    stretch_value,
    prior_keys,
    prior_values,
    stretch_start,
):
    head_size = cache_keys.shape[2]
    group_size = new_query.shape[1] // head_size
    local_dec = new_query.shape[0]
    seq_rank = lax.axis_index("seq")
    seq_count = lax.axis_size("seq")
    total_dec = local_dec * seq_count
    stretch_count, local_tok, query_width = stretch_query.shape
    key_width = stretch_key.shape[2]
    stretch_rows = stretch_count * local_tok

    decode_kv = jnp.concatenate([new_key, new_value], axis=1)
    decode_kv = jnp.pad(decode_kv, ((0, 0), (0, query_width - 2 * key_width)))
    pack = jnp.concatenate(
        [stretch_query.reshape(stretch_rows, query_width), new_query, decode_kv], axis=0
    )
    every, order = broadcast_over_seq(pack, seq_rank, seq_count)
    decode_rows = jnp.take(every[:, stretch_rows:, :], order, axis=0)
    every_query = decode_rows[:, :local_dec, :].reshape(total_dec, query_width)
    every_kv = decode_rows[:, local_dec:, :].reshape(total_dec, query_width)
    every_key = every_kv[:, :key_width]
    every_value = every_kv[:, key_width : 2 * key_width]
    slot_ids = seq_rank * local_dec + jnp.arange(local_dec, dtype=jnp.int32)
    arrival_ids = jnp.arange(total_dec, dtype=jnp.int32)
    sources = jnp.sum(
        jnp.where(dealing[None, :] == slot_ids[:, None], arrival_ids[None, :], 0), axis=1
    )
    home_query = jnp.take(every_query, sources, axis=0)
    home_key = jnp.take(every_key, sources, axis=0)
    home_value = jnp.take(every_value, sources, axis=0)
    cache_span = cache_keys.shape[1]
    cache_pos = jnp.arange(cache_span, dtype=jnp.int32)

    def decode_slot(query_row, own_key, own_value, cached_keys, cached_values, length):
        key_all = jnp.concatenate([cached_keys, own_key[None, :]], axis=0)
        value_all = jnp.concatenate([cached_values, own_value[None, :]], axis=0)
        visible = jnp.concatenate([cache_pos < length, jnp.ones((1,), dtype=jnp.bool_)])
        visible = jnp.broadcast_to(visible[None, :], (group_size, cache_span + 1))
        row_top, weight_sum, numerator = partial_attend(
            query_row.reshape(group_size, head_size), key_all, value_all, visible
        )
        return (
            (numerator / weight_sum[:, None]).astype(jnp.bfloat16).reshape(group_size * head_size)
        )

    home_out = jax.vmap(decode_slot)(
        home_query, home_key, home_value, cache_keys, cache_values, cache_length
    )
    all_out = lax.all_to_all(
        jnp.broadcast_to(home_out[None], (seq_count,) + home_out.shape), "seq", 0, 0, tiled=True
    ).reshape(total_dec, group_size * head_size)
    arrival_out = jnp.take(all_out, dealing, axis=0)
    arrival_terms = jnp.dot(arrival_out, out_weight, preferred_element_type=jnp.float32)
    decode_mixed = lax.psum_scatter(arrival_terms, "tp", scatter_dimension=0, tiled=True).astype(
        jnp.bfloat16
    )

    prior_span = prior_keys.shape[1]
    direct = local_tok % 16 == 0
    stat_count = 3 * stretch_count * local_tok * group_size
    stat_rows = -(-stat_count // query_width)
    out_rows = stretch_rows
    limits = jnp.clip(stretch_start - seq_rank * prior_span, 0, prior_span).astype(jnp.int32)
    info = jnp.concatenate([limits, (seq_rank * local_tok).astype(jnp.int32)[None]])
    if direct:
        payload, part_lse = prefill_partial(
            info, order, every, prior_keys, prior_values, stretch_key, stretch_value, group_size,
            local_tok, local_tok, out_rows + stat_rows,
        )
    else:
        token_count = seq_count * local_tok
        queries_all = (
            jnp.take(every, order, axis=0)[:, :stretch_rows, :]
            .reshape(seq_count, stretch_count, local_tok, query_width)
            .transpose(1, 0, 2, 3)
            .reshape(1, stretch_rows * seq_count, query_width)
        )
        flat_out, part_lse = prefill_partial(
            info, jnp.zeros((1,), jnp.int32), queries_all, prior_keys, prior_values, stretch_key, stretch_value, group_size,
            token_count, token_count, stretch_rows * seq_count,
        )
        payload = jnp.pad(
            flat_out.reshape(stretch_count, seq_count, local_tok, query_width)
            .transpose(1, 0, 2, 3)
            .reshape(seq_count, out_rows, query_width),
            ((0, 0), (0, stat_rows), (0, 0)),
        )
    part_lse = part_lse.reshape(stretch_count, seq_count, local_tok, group_size)
    lse_hi = lax.reduce_precision(part_lse, exponent_bits=8, mantissa_bits=7)
    lse_rest = part_lse - lse_hi
    lse_mid = lax.reduce_precision(lse_rest, exponent_bits=8, mantissa_bits=7)
    lse_lo = lse_rest - lse_mid
    stats = (
        jnp.stack([lse_hi, lse_mid, lse_lo])
        .transpose(2, 0, 1, 3, 4)
        .reshape(seq_count, stat_count)
    )
    stats = jnp.pad(stats, ((0, 0), (0, stat_rows * query_width - stat_count)))
    payload = lax.dynamic_update_slice(
        payload,
        stats.astype(jnp.bfloat16).reshape(seq_count, stat_rows, query_width),
        (0, out_rows, 0),
    )

    received = lax.all_to_all(payload, "seq", 0, 0, tiled=True)
    got_stats = (
        received[:, out_rows:, :]
        .reshape(seq_count, stat_rows * query_width)[:, :stat_count]
        .astype(jnp.float32)
        .reshape(seq_count, 3, stretch_count, local_tok, group_size)
    )
    got_lse = (got_stats[:, 0] + got_stats[:, 1]) + got_stats[:, 2]
    stretch_out = combine_partials(received, got_lse, group_size, head_size)
    return (decode_mixed, stretch_out)


def solution(mesh):
    return jax.shard_map(
        body,
        mesh=mesh,
        in_specs=(
            P("seq", "tp"),
            P("seq", "tp"),
            P("seq", "tp"),
            P("seq", None, "tp"),
            P("seq", None, "tp"),
            P("seq"),
            P(),
            P("tp", "seq"),
            P(None, "seq", "tp"),
            P(None, "seq", "tp"),
            P(None, "seq", "tp"),
            P(None, "seq", "tp"),
            P(None, "seq", "tp"),
            P(),
        ),
        out_specs=(P("tp", "seq"), P(None, "seq", "tp")),
        check_vma=False,
    )
```

```python
import functools
import math

import jax
import jax.numpy as jnp
from jax import lax
from jax.experimental import pallas as pl
from jax.experimental.pallas import tpu as pltpu
from jax.sharding import PartitionSpec as P

NEG_FILL = -1e30


def partial_attend(queries, keys, values, visible):
    factor = 1.0 / math.sqrt(queries.shape[-1])
    scores = jnp.dot(queries, keys.T, preferred_element_type=jnp.float32) * factor
    scores = jnp.where(visible, scores, NEG_FILL)
    row_top = jnp.max(scores, axis=1)
    weights = jnp.where(visible, jnp.exp(scores - row_top[:, None]), 0.0)
    weight_sum = jnp.sum(weights, axis=1)
    numerator = jnp.dot(weights.astype(jnp.bfloat16), values, preferred_element_type=jnp.float32)
    return (row_top, weight_sum, numerator)


def _prefill_kernel(
    info_ref, order_ref, q_hbm, k_ref, v_ref, sk_ref, sv_ref, o_ref, lse_ref, q_ref, sems,
    *, group_size, head_size, local_tok
):
    c = pl.program_id(0)
    stretch_count, src_count, tok_block, _ = q_ref.shape

    def query_copy(stretch, src):
        return pltpu.make_async_copy(
            q_hbm.at[order_ref[src], pl.ds(stretch * tok_block, tok_block)],
            q_ref.at[stretch, src],
            sems.at[stretch, src],
        )

    @pl.when(c == 0)
    def _():
        for stretch in range(stretch_count):
            for src in range(src_count):
                query_copy(stretch, src).start()

    for src in range(src_count):
        query_copy(c, src).wait()
    limit = info_ref[c]
    key_offset = info_ref[info_ref.shape[0] - 1]
    keys = k_ref[0]
    values = v_ref[0]
    own_keys = sk_ref[0]
    own_values = sv_ref[0]
    factor = 1.0 / math.sqrt(head_size)
    tokens = src_count * tok_block
    col = lax.broadcasted_iota(jnp.int32, (1, keys.shape[0]), 1)
    visible = col < limit
    key_token = key_offset + lax.broadcasted_iota(jnp.int32, (tokens, own_keys.shape[0]), 1)
    row = lax.broadcasted_iota(jnp.int32, (tokens, own_keys.shape[0]), 0)
    query_token = (row // tok_block) * local_tok + row % tok_block
    causal = key_token <= query_token
    dims = (((1,), (1,)), ((), ()))
    for h in range(group_size):
        q = q_ref[c, :, :, h * head_size : (h + 1) * head_size].reshape(tokens, head_size)
        s = lax.dot_general(q, keys, dims, preferred_element_type=jnp.float32) * factor
        s = jnp.where(visible, s, NEG_FILL)
        s_own = lax.dot_general(q, own_keys, dims, preferred_element_type=jnp.float32) * factor
        s_own = jnp.where(causal, s_own, NEG_FILL)
        m = jnp.maximum(
            jnp.max(s, axis=1, keepdims=True), jnp.max(s_own, axis=1, keepdims=True)
        )
        w = jnp.exp(s - m)
        w_own = jnp.exp(s_own - m)
        empty = m < 0.5 * NEG_FILL
        l = jnp.sum(w, axis=1, keepdims=True) + jnp.sum(w_own, axis=1, keepdims=True)
        num = jnp.dot(w.astype(jnp.bfloat16), values, preferred_element_type=jnp.float32)
        num = num + jnp.dot(
            w_own.astype(jnp.bfloat16), own_values, preferred_element_type=jnp.float32
        )
        l = jnp.where(empty, 0.0, l)
        num = jnp.where(empty, 0.0, num)
        safe = jnp.maximum(l, 1.0)
        o_ref[:, :, h * head_size : (h + 1) * head_size] = (
            (num / safe).astype(o_ref.dtype).reshape(src_count, tok_block, head_size)
        )
        lse_ref[0, :, h : h + 1] = m + jnp.log(safe)


def prefill_partial(
    info, order, queries, keys, values, own_keys, own_values, group_size, tok_block, local_tok,
    out_rows,
):
    src_count = order.shape[0]
    qw = queries.shape[2]
    n, p, hd = keys.shape
    own = own_keys.shape[1]
    tokens = src_count * tok_block
    kern = functools.partial(
        _prefill_kernel, group_size=group_size, head_size=hd, local_tok=local_tok
    )
    return pl.pallas_call(
        kern,
        grid_spec=pltpu.PrefetchScalarGridSpec(
            num_scalar_prefetch=2,
            grid=(n,),
            in_specs=[
                pl.BlockSpec(memory_space=pl.ANY),
                pl.BlockSpec((1, p, hd), lambda c, info, order: (c, 0, 0)),
                pl.BlockSpec((1, p, hd), lambda c, info, order: (c, 0, 0)),
                pl.BlockSpec((1, own, hd), lambda c, info, order: (c, 0, 0)),
                pl.BlockSpec((1, own, hd), lambda c, info, order: (c, 0, 0)),
            ],
            out_specs=[
                pl.BlockSpec((src_count, tok_block, qw), lambda c, info, order: (0, c, 0)),
                pl.BlockSpec((1, tokens, group_size), lambda c, info, order: (c, 0, 0)),
            ],
            scratch_shapes=[
                pltpu.VMEM((n, src_count, tok_block, qw), jnp.bfloat16),
                pltpu.SemaphoreType.DMA((n, src_count)),
            ],
        ),
        out_shape=[
            jax.ShapeDtypeStruct((src_count, out_rows, qw), jnp.bfloat16),
            jax.ShapeDtypeStruct((n, tokens, group_size), jnp.float32),
        ],
    )(info, order, queries, keys, values, own_keys, own_values)


def _combine_kernel(o_ref, lse_ref, out_ref, *, group_size, head_size):
    stretch_count, local_tok, _ = out_ref.shape
    for c in range(stretch_count):
        lse = lse_ref[:, c]
        top = jnp.max(lse, axis=0, keepdims=True)
        weights = jnp.exp(lse - top)
        total = jnp.sum(weights, axis=0)
        for h in range(group_size):
            part = o_ref[
                :, c * local_tok : (c + 1) * local_tok, h * head_size : (h + 1) * head_size
            ].astype(jnp.float32)
            num = jnp.sum(part * weights[:, :, h : h + 1], axis=0)
            out_ref[c, :, h * head_size : (h + 1) * head_size] = (
                num / total[:, h : h + 1]
            ).astype(out_ref.dtype)


def combine_partials(received, lse, group_size, head_size):
    _, stretch_count, local_tok, _ = lse.shape
    kern = functools.partial(_combine_kernel, group_size=group_size, head_size=head_size)
    return pl.pallas_call(
        kern,
        out_shape=jax.ShapeDtypeStruct(
            (stretch_count, local_tok, group_size * head_size), jnp.bfloat16
        ),
    )(received, lse)


def broadcast_over_seq(pack, seq_rank, seq_count):
    if seq_count > 16 or seq_count % 2:
        every = lax.all_to_all(
            jnp.broadcast_to(pack[None], (seq_count,) + pack.shape), "seq", 0, 0, tiled=True
        )
        return every, jnp.arange(seq_count, dtype=jnp.int32)
    half = seq_count // 2
    partner = lax.ppermute(pack, "seq", [(i, (i + half) % seq_count) for i in range(seq_count)])
    perms = [
        [(i, (i // half) * half + (i % half + shift) % half) for i in range(seq_count)]
        for shift in range(1, half)
    ]
    near_pieces = [lax.ppermute(pack, "seq", perm) for perm in perms]
    far_pieces = [lax.ppermute(partner, "seq", perm) for perm in perms]
    every = jnp.stack([pack, partner] + near_pieces + far_pieces)
    sources = jnp.arange(seq_count, dtype=jnp.int32)
    far = (sources // half) != (seq_rank // half)
    near = jnp.where(far, (sources + half) % seq_count, sources)
    shift_of = (seq_rank % half - near % half) % half
    order = jnp.where(
        far,
        jnp.where(shift_of == 0, 1, half + shift_of),
        jnp.where(shift_of == 0, 0, 1 + shift_of),
    )
    return every, order.astype(jnp.int32)


def body(
    new_query,
    new_key,
    new_value,
    cache_keys,
    cache_values,
    cache_length,
    dealing,
    out_weight,
    stretch_query,
    stretch_key,
    stretch_value,
    prior_keys,
    prior_values,
    stretch_start,
):
    head_size = cache_keys.shape[2]
    group_size = new_query.shape[1] // head_size
    local_dec = new_query.shape[0]
    seq_rank = lax.axis_index("seq")
    seq_count = lax.axis_size("seq")
    total_dec = local_dec * seq_count
    stretch_count, local_tok, query_width = stretch_query.shape
    key_width = stretch_key.shape[2]
    stretch_rows = stretch_count * local_tok

    decode_kv = jnp.concatenate([new_key, new_value], axis=1)
    decode_kv = jnp.pad(decode_kv, ((0, 0), (0, query_width - 2 * key_width)))
    pack = jnp.concatenate(
        [stretch_query.reshape(stretch_rows, query_width), new_query, decode_kv], axis=0
    )
    every, order = broadcast_over_seq(pack, seq_rank, seq_count)
    decode_rows = jnp.take(every[:, stretch_rows:, :], order, axis=0)
    every_query = decode_rows[:, :local_dec, :].reshape(total_dec, query_width)
    every_kv = decode_rows[:, local_dec:, :].reshape(total_dec, query_width)
    every_key = every_kv[:, :key_width]
    every_value = every_kv[:, key_width : 2 * key_width]
    slot_ids = seq_rank * local_dec + jnp.arange(local_dec, dtype=jnp.int32)
    arrival_ids = jnp.arange(total_dec, dtype=jnp.int32)
    sources = jnp.sum(
        jnp.where(dealing[None, :] == slot_ids[:, None], arrival_ids[None, :], 0), axis=1
    )
    home_query = jnp.take(every_query, sources, axis=0)
    home_key = jnp.take(every_key, sources, axis=0)
    home_value = jnp.take(every_value, sources, axis=0)
    cache_span = cache_keys.shape[1]
    cache_pos = jnp.arange(cache_span, dtype=jnp.int32)

    def decode_slot(query_row, own_key, own_value, cached_keys, cached_values, length):
        key_all = jnp.concatenate([cached_keys, own_key[None, :]], axis=0)
        value_all = jnp.concatenate([cached_values, own_value[None, :]], axis=0)
        visible = jnp.concatenate([cache_pos < length, jnp.ones((1,), dtype=jnp.bool_)])
        visible = jnp.broadcast_to(visible[None, :], (group_size, cache_span + 1))
        row_top, weight_sum, numerator = partial_attend(
            query_row.reshape(group_size, head_size), key_all, value_all, visible
        )
        return (
            (numerator / weight_sum[:, None]).astype(jnp.bfloat16).reshape(group_size * head_size)
        )

    home_out = jax.vmap(decode_slot)(
        home_query, home_key, home_value, cache_keys, cache_values, cache_length
    )
    all_out = lax.all_to_all(
        jnp.broadcast_to(home_out[None], (seq_count,) + home_out.shape), "seq", 0, 0, tiled=True
    ).reshape(total_dec, group_size * head_size)
    arrival_out = jnp.take(all_out, dealing, axis=0)
    arrival_terms = jnp.dot(arrival_out, out_weight, preferred_element_type=jnp.float32)
    decode_mixed = lax.psum_scatter(arrival_terms, "tp", scatter_dimension=0, tiled=True).astype(
        jnp.bfloat16
    )

    prior_span = prior_keys.shape[1]
    direct = local_tok % 16 == 0
    stat_count = 3 * stretch_count * local_tok * group_size
    stat_rows = -(-stat_count // query_width)
    out_rows = stretch_rows
    limits = jnp.clip(stretch_start - seq_rank * prior_span, 0, prior_span).astype(jnp.int32)
    info = jnp.concatenate([limits, (seq_rank * local_tok).astype(jnp.int32)[None]])
    if direct:
        payload, part_lse = prefill_partial(
            info, order, every, prior_keys, prior_values, stretch_key, stretch_value, group_size,
            local_tok, local_tok, out_rows + stat_rows,
        )
    else:
        token_count = seq_count * local_tok
        queries_all = (
            jnp.take(every, order, axis=0)[:, :stretch_rows, :]
            .reshape(seq_count, stretch_count, local_tok, query_width)
            .transpose(1, 0, 2, 3)
            .reshape(1, stretch_rows * seq_count, query_width)
        )
        flat_out, part_lse = prefill_partial(
            info, jnp.zeros((1,), jnp.int32), queries_all, prior_keys, prior_values, stretch_key, stretch_value, group_size,
            token_count, token_count, stretch_rows * seq_count,
        )
        payload = jnp.pad(
            flat_out.reshape(stretch_count, seq_count, local_tok, query_width)
            .transpose(1, 0, 2, 3)
            .reshape(seq_count, out_rows, query_width),
            ((0, 0), (0, stat_rows), (0, 0)),
        )
    part_lse = part_lse.reshape(stretch_count, seq_count, local_tok, group_size)
    lse_hi = lax.reduce_precision(part_lse, exponent_bits=8, mantissa_bits=7)
    lse_rest = part_lse - lse_hi
    lse_mid = lax.reduce_precision(lse_rest, exponent_bits=8, mantissa_bits=7)
    lse_lo = lse_rest - lse_mid
    stats = (
        jnp.stack([lse_hi, lse_mid, lse_lo])
        .transpose(2, 0, 1, 3, 4)
        .reshape(seq_count, stat_count)
    )
    stats = jnp.pad(stats, ((0, 0), (0, stat_rows * query_width - stat_count)))
    payload = lax.dynamic_update_slice(
        payload,
        stats.astype(jnp.bfloat16).reshape(seq_count, stat_rows, query_width),
        (0, out_rows, 0),
    )

    received = lax.all_to_all(payload, "seq", 0, 0, tiled=True)
    got_stats = (
        received[:, out_rows:, :]
        .reshape(seq_count, stat_rows * query_width)[:, :stat_count]
        .astype(jnp.float32)
        .reshape(seq_count, 3, stretch_count, local_tok, group_size)
    )
    got_lse = (got_stats[:, 0] + got_stats[:, 1]) + got_stats[:, 2]
    stretch_out = combine_partials(received, got_lse, group_size, head_size)
    return (decode_mixed, stretch_out)


def solution(mesh):
    return jax.shard_map(
        body,
        mesh=mesh,
        in_specs=(
            P("seq", "tp"),
            P("seq", "tp"),
            P("seq", "tp"),
            P("seq", None, "tp"),
            P("seq", None, "tp"),
            P("seq"),
            P(),
            P("tp", "seq"),
            P(None, "seq", "tp"),
            P(None, "seq", "tp"),
            P(None, "seq", "tp"),
            P(None, "seq", "tp"),
            P(None, "seq", "tp"),
            P(),
        ),
        out_specs=(P("tp", "seq"), P(None, "seq", "tp")),
        check_vma=False,
    )
```

```python
import functools
import math

import jax
import jax.numpy as jnp
from jax import lax
from jax.experimental import pallas as pl
from jax.experimental.pallas import tpu as pltpu
from jax.sharding import PartitionSpec as P

NEG_FILL = -1e30


def partial_attend(queries, keys, values, visible):
    factor = 1.0 / math.sqrt(queries.shape[-1])
    scores = jnp.dot(queries, keys.T, preferred_element_type=jnp.float32) * factor
    scores = jnp.where(visible, scores, NEG_FILL)
    row_top = jnp.max(scores, axis=1)
    weights = jnp.where(visible, jnp.exp(scores - row_top[:, None]), 0.0)
    weight_sum = jnp.sum(weights, axis=1)
    numerator = jnp.dot(weights.astype(jnp.bfloat16), values, preferred_element_type=jnp.float32)
    return (row_top, weight_sum, numerator)


def _prefill_kernel(
    info_ref, order_ref, q_hbm, k_ref, v_ref, sk_ref, sv_ref, o_ref, lse_ref, q_ref, sems,
    *, group_size, head_size, local_tok
):
    c = pl.program_id(0)
    stretch_count, src_count, tok_block, _ = q_ref.shape

    def query_copy(stretch, src):
        return pltpu.make_async_copy(
            q_hbm.at[order_ref[src], pl.ds(stretch * tok_block, tok_block)],
            q_ref.at[stretch, src],
            sems.at[stretch, src],
        )

    @pl.when(c == 0)
    def _():
        for stretch in range(stretch_count):
            for src in range(src_count):
                query_copy(stretch, src).start()

    for src in range(src_count):
        query_copy(c, src).wait()
    limit = info_ref[c]
    key_offset = info_ref[info_ref.shape[0] - 1]
    keys = k_ref[0]
    values = v_ref[0]
    own_keys = sk_ref[0]
    own_values = sv_ref[0]
    factor = 1.0 / math.sqrt(head_size)
    tokens = src_count * tok_block
    col = lax.broadcasted_iota(jnp.int32, (1, keys.shape[0]), 1)
    visible = col < limit
    key_token = key_offset + lax.broadcasted_iota(jnp.int32, (tokens, own_keys.shape[0]), 1)
    row = lax.broadcasted_iota(jnp.int32, (tokens, own_keys.shape[0]), 0)
    query_token = (row // tok_block) * local_tok + row % tok_block
    causal = key_token <= query_token
    dims = (((1,), (1,)), ((), ()))
    for h in range(group_size):
        q = q_ref[c, :, :, h * head_size : (h + 1) * head_size].reshape(tokens, head_size)
        s = lax.dot_general(q, keys, dims, preferred_element_type=jnp.float32) * factor
        s = jnp.where(visible, s, NEG_FILL)
        s_own = lax.dot_general(q, own_keys, dims, preferred_element_type=jnp.float32) * factor
        s_own = jnp.where(causal, s_own, NEG_FILL)
        m = jnp.maximum(
            jnp.max(s, axis=1, keepdims=True), jnp.max(s_own, axis=1, keepdims=True)
        )
        w = jnp.exp(s - m)
        w_own = jnp.exp(s_own - m)
        empty = m < 0.5 * NEG_FILL
        l = jnp.sum(w, axis=1, keepdims=True) + jnp.sum(w_own, axis=1, keepdims=True)
        num = jnp.dot(w.astype(jnp.bfloat16), values, preferred_element_type=jnp.float32)
        num = num + jnp.dot(
            w_own.astype(jnp.bfloat16), own_values, preferred_element_type=jnp.float32
        )
        l = jnp.where(empty, 0.0, l)
        num = jnp.where(empty, 0.0, num)
        safe = jnp.maximum(l, 1.0)
        o_ref[:, :, h * head_size : (h + 1) * head_size] = (
            (num / safe).astype(o_ref.dtype).reshape(src_count, tok_block, head_size)
        )
        lse_ref[0, :, h : h + 1] = m + jnp.log(safe)


def prefill_partial(
    info, order, queries, keys, values, own_keys, own_values, group_size, tok_block, local_tok,
    out_rows,
):
    src_count = order.shape[0]
    qw = queries.shape[2]
    n, p, hd = keys.shape
    own = own_keys.shape[1]
    tokens = src_count * tok_block
    kern = functools.partial(
        _prefill_kernel, group_size=group_size, head_size=hd, local_tok=local_tok
    )
    return pl.pallas_call(
        kern,
        grid_spec=pltpu.PrefetchScalarGridSpec(
            num_scalar_prefetch=2,
            grid=(n,),
            in_specs=[
                pl.BlockSpec(memory_space=pl.ANY),
                pl.BlockSpec((1, p, hd), lambda c, info, order: (c, 0, 0)),
                pl.BlockSpec((1, p, hd), lambda c, info, order: (c, 0, 0)),
                pl.BlockSpec((1, own, hd), lambda c, info, order: (c, 0, 0)),
                pl.BlockSpec((1, own, hd), lambda c, info, order: (c, 0, 0)),
            ],
            out_specs=[
                pl.BlockSpec((src_count, tok_block, qw), lambda c, info, order: (0, c, 0)),
                pl.BlockSpec((1, tokens, group_size), lambda c, info, order: (c, 0, 0)),
            ],
            scratch_shapes=[
                pltpu.VMEM((n, src_count, tok_block, qw), jnp.bfloat16),
                pltpu.SemaphoreType.DMA((n, src_count)),
            ],
        ),
        out_shape=[
            jax.ShapeDtypeStruct((src_count, out_rows, qw), jnp.bfloat16),
            jax.ShapeDtypeStruct((n, tokens, group_size), jnp.float32),
        ],
    )(info, order, queries, keys, values, own_keys, own_values)


def _combine_kernel(o_ref, lse_ref, out_ref, *, group_size, head_size):
    stretch_count, local_tok, _ = out_ref.shape
    for c in range(stretch_count):
        lse = lse_ref[:, c]
        top = jnp.max(lse, axis=0, keepdims=True)
        weights = jnp.exp(lse - top)
        total = jnp.sum(weights, axis=0)
        for h in range(group_size):
            part = o_ref[
                :, c * local_tok : (c + 1) * local_tok, h * head_size : (h + 1) * head_size
            ].astype(jnp.float32)
            num = jnp.sum(part * weights[:, :, h : h + 1], axis=0)
            out_ref[c, :, h * head_size : (h + 1) * head_size] = (
                num / total[:, h : h + 1]
            ).astype(out_ref.dtype)


def combine_partials(received, lse, group_size, head_size):
    _, stretch_count, local_tok, _ = lse.shape
    kern = functools.partial(_combine_kernel, group_size=group_size, head_size=head_size)
    return pl.pallas_call(
        kern,
        out_shape=jax.ShapeDtypeStruct(
            (stretch_count, local_tok, group_size * head_size), jnp.bfloat16
        ),
    )(received, lse)


def broadcast_over_seq(pack, seq_rank, seq_count):
    if seq_count > 16 or seq_count % 2:
        every = lax.all_to_all(
            jnp.broadcast_to(pack[None], (seq_count,) + pack.shape), "seq", 0, 0, tiled=True
        )
        return every, jnp.arange(seq_count, dtype=jnp.int32)
    half = seq_count // 2
    partner = lax.ppermute(pack, "seq", [(i, (i + half) % seq_count) for i in range(seq_count)])
    perms = [
        [(i, (i // half) * half + (i % half + shift) % half) for i in range(seq_count)]
        for shift in range(1, half)
    ]
    near_pieces = [lax.ppermute(pack, "seq", perm) for perm in perms]
    far_pieces = [lax.ppermute(partner, "seq", perm) for perm in perms]
    every = jnp.stack([pack, partner] + near_pieces + far_pieces)
    sources = jnp.arange(seq_count, dtype=jnp.int32)
    far = (sources // half) != (seq_rank // half)
    near = jnp.where(far, (sources + half) % seq_count, sources)
    shift_of = (seq_rank % half - near % half) % half
    order = jnp.where(
        far,
        jnp.where(shift_of == 0, 1, half + shift_of),
        jnp.where(shift_of == 0, 0, 1 + shift_of),
    )
    return every, order.astype(jnp.int32)


def exchange_over_seq(payload, seq_rank, seq_count):
    if seq_count > 16 or seq_count % 2:
        return lax.all_to_all(payload, "seq", 0, 0, tiled=True)
    half = seq_count // 2
    mine = lax.dynamic_index_in_dim(payload, seq_rank, 0, keepdims=False)
    partner_of = (seq_rank + half) % seq_count
    direct = lax.ppermute(
        lax.dynamic_index_in_dim(payload, partner_of, 0, keepdims=False),
        "seq",
        [(i, (i + half) % seq_count) for i in range(seq_count)],
    )
    near_pieces, far_pieces = [], []
    for shift in range(1, half):
        perm = [(i, (i // half) * half + (i % half + shift) % half) for i in range(seq_count)]
        target = (seq_rank // half) * half + (seq_rank % half + shift) % half
        pair = jnp.stack(
            [
                lax.dynamic_index_in_dim(payload, target, 0, keepdims=False),
                lax.dynamic_index_in_dim(payload, (target + half) % seq_count, 0, keepdims=False),
            ]
        )
        got = lax.ppermute(pair, "seq", perm)
        near_pieces.append(got[0])
        far_pieces.append(
            lax.ppermute(got[1], "seq", [(i, (i + half) % seq_count) for i in range(seq_count)])
        )
    return jnp.stack([mine, direct] + near_pieces + far_pieces)


def body(
    new_query,
    new_key,
    new_value,
    cache_keys,
    cache_values,
    cache_length,
    dealing,
    out_weight,
    stretch_query,
    stretch_key,
    stretch_value,
    prior_keys,
    prior_values,
    stretch_start,
):
    head_size = cache_keys.shape[2]
    group_size = new_query.shape[1] // head_size
    local_dec = new_query.shape[0]
    seq_rank = lax.axis_index("seq")
    seq_count = lax.axis_size("seq")
    total_dec = local_dec * seq_count
    stretch_count, local_tok, query_width = stretch_query.shape
    key_width = stretch_key.shape[2]
    stretch_rows = stretch_count * local_tok

    decode_kv = jnp.concatenate([new_key, new_value], axis=1)
    decode_kv = jnp.pad(decode_kv, ((0, 0), (0, query_width - 2 * key_width)))
    pack = jnp.concatenate(
        [stretch_query.reshape(stretch_rows, query_width), new_query, decode_kv], axis=0
    )
    every, order = broadcast_over_seq(pack, seq_rank, seq_count)
    decode_rows = jnp.take(every[:, stretch_rows:, :], order, axis=0)
    every_query = decode_rows[:, :local_dec, :].reshape(total_dec, query_width)
    every_kv = decode_rows[:, local_dec:, :].reshape(total_dec, query_width)
    every_key = every_kv[:, :key_width]
    every_value = every_kv[:, key_width : 2 * key_width]
    slot_ids = seq_rank * local_dec + jnp.arange(local_dec, dtype=jnp.int32)
    arrival_ids = jnp.arange(total_dec, dtype=jnp.int32)
    sources = jnp.sum(
        jnp.where(dealing[None, :] == slot_ids[:, None], arrival_ids[None, :], 0), axis=1
    )
    home_query = jnp.take(every_query, sources, axis=0)
    home_key = jnp.take(every_key, sources, axis=0)
    home_value = jnp.take(every_value, sources, axis=0)
    cache_span = cache_keys.shape[1]
    cache_pos = jnp.arange(cache_span, dtype=jnp.int32)

    def decode_slot(query_row, own_key, own_value, cached_keys, cached_values, length):
        key_all = jnp.concatenate([cached_keys, own_key[None, :]], axis=0)
        value_all = jnp.concatenate([cached_values, own_value[None, :]], axis=0)
        visible = jnp.concatenate([cache_pos < length, jnp.ones((1,), dtype=jnp.bool_)])
        visible = jnp.broadcast_to(visible[None, :], (group_size, cache_span + 1))
        row_top, weight_sum, numerator = partial_attend(
            query_row.reshape(group_size, head_size), key_all, value_all, visible
        )
        return (
            (numerator / weight_sum[:, None]).astype(jnp.bfloat16).reshape(group_size * head_size)
        )

    home_out = jax.vmap(decode_slot)(
        home_query, home_key, home_value, cache_keys, cache_values, cache_length
    )
    all_out = lax.all_to_all(
        jnp.broadcast_to(home_out[None], (seq_count,) + home_out.shape), "seq", 0, 0, tiled=True
    ).reshape(total_dec, group_size * head_size)
    arrival_out = jnp.take(all_out, dealing, axis=0)
    arrival_terms = jnp.dot(arrival_out, out_weight, preferred_element_type=jnp.float32)
    decode_mixed = lax.psum_scatter(arrival_terms, "tp", scatter_dimension=0, tiled=True).astype(
        jnp.bfloat16
    )

    prior_span = prior_keys.shape[1]
    direct = local_tok % 16 == 0
    stat_count = 3 * stretch_count * local_tok * group_size
    stat_rows = -(-stat_count // query_width)
    out_rows = stretch_rows
    limits = jnp.clip(stretch_start - seq_rank * prior_span, 0, prior_span).astype(jnp.int32)
    info = jnp.concatenate([limits, (seq_rank * local_tok).astype(jnp.int32)[None]])
    if direct:
        payload, part_lse = prefill_partial(
            info, order, every, prior_keys, prior_values, stretch_key, stretch_value, group_size,
            local_tok, local_tok, out_rows + stat_rows,
        )
    else:
        token_count = seq_count * local_tok
        queries_all = (
            jnp.take(every, order, axis=0)[:, :stretch_rows, :]
            .reshape(seq_count, stretch_count, local_tok, query_width)
            .transpose(1, 0, 2, 3)
            .reshape(1, stretch_rows * seq_count, query_width)
        )
        flat_out, part_lse = prefill_partial(
            info, jnp.zeros((1,), jnp.int32), queries_all, prior_keys, prior_values, stretch_key, stretch_value, group_size,
            token_count, token_count, stretch_rows * seq_count,
        )
        payload = jnp.pad(
            flat_out.reshape(stretch_count, seq_count, local_tok, query_width)
            .transpose(1, 0, 2, 3)
            .reshape(seq_count, out_rows, query_width),
            ((0, 0), (0, stat_rows), (0, 0)),
        )
    part_lse = part_lse.reshape(stretch_count, seq_count, local_tok, group_size)
    lse_hi = lax.reduce_precision(part_lse, exponent_bits=8, mantissa_bits=7)
    lse_rest = part_lse - lse_hi
    lse_mid = lax.reduce_precision(lse_rest, exponent_bits=8, mantissa_bits=7)
    lse_lo = lse_rest - lse_mid
    stats = (
        jnp.stack([lse_hi, lse_mid, lse_lo])
        .transpose(2, 0, 1, 3, 4)
        .reshape(seq_count, stat_count)
    )
    stats = jnp.pad(stats, ((0, 0), (0, stat_rows * query_width - stat_count)))
    payload = lax.dynamic_update_slice(
        payload,
        stats.astype(jnp.bfloat16).reshape(seq_count, stat_rows, query_width),
        (0, out_rows, 0),
    )

    received = exchange_over_seq(payload, seq_rank, seq_count)
    got_stats = (
        received[:, out_rows:, :]
        .reshape(seq_count, stat_rows * query_width)[:, :stat_count]
        .astype(jnp.float32)
        .reshape(seq_count, 3, stretch_count, local_tok, group_size)
    )
    got_lse = (got_stats[:, 0] + got_stats[:, 1]) + got_stats[:, 2]
    stretch_out = combine_partials(received, got_lse, group_size, head_size)
    return (decode_mixed, stretch_out)


def solution(mesh):
    return jax.shard_map(
        body,
        mesh=mesh,
        in_specs=(
            P("seq", "tp"),
            P("seq", "tp"),
            P("seq", "tp"),
            P("seq", None, "tp"),
            P("seq", None, "tp"),
            P("seq"),
            P(),
            P("tp", "seq"),
            P(None, "seq", "tp"),
            P(None, "seq", "tp"),
            P(None, "seq", "tp"),
            P(None, "seq", "tp"),
            P(None, "seq", "tp"),
            P(),
        ),
        out_specs=(P("tp", "seq"), P(None, "seq", "tp")),
        check_vma=False,
    )
```

```python
import functools
import math

import jax
import jax.numpy as jnp
from jax import lax
from jax.experimental import pallas as pl
from jax.experimental.pallas import tpu as pltpu
from jax.sharding import PartitionSpec as P

NEG_FILL = -1e30


def partial_attend(queries, keys, values, visible):
    factor = 1.0 / math.sqrt(queries.shape[-1])
    scores = jnp.dot(queries, keys.T, preferred_element_type=jnp.float32) * factor
    scores = jnp.where(visible, scores, NEG_FILL)
    row_top = jnp.max(scores, axis=1)
    weights = jnp.where(visible, jnp.exp(scores - row_top[:, None]), 0.0)
    weight_sum = jnp.sum(weights, axis=1)
    numerator = jnp.dot(weights.astype(jnp.bfloat16), values, preferred_element_type=jnp.float32)
    return (row_top, weight_sum, numerator)


def _prefill_kernel(
    info_ref, order_ref, q_hbm, k_ref, v_ref, sk_ref, sv_ref, o_ref, lse_ref, q_ref, sems,
    *, group_size, head_size, local_tok
):
    c = pl.program_id(0)
    stretch_count, src_count, tok_block, _ = q_ref.shape

    def query_copy(stretch, src):
        return pltpu.make_async_copy(
            q_hbm.at[order_ref[src], pl.ds(stretch * tok_block, tok_block)],
            q_ref.at[stretch, src],
            sems.at[stretch, src],
        )

    @pl.when(c == 0)
    def _():
        for stretch in range(stretch_count):
            for src in range(src_count):
                query_copy(stretch, src).start()

    for src in range(src_count):
        query_copy(c, src).wait()
    limit = info_ref[c]
    key_offset = info_ref[info_ref.shape[0] - 1]
    keys = k_ref[0]
    values = v_ref[0]
    own_keys = sk_ref[0]
    own_values = sv_ref[0]
    factor = 1.0 / math.sqrt(head_size)
    tokens = src_count * tok_block
    col = lax.broadcasted_iota(jnp.int32, (1, keys.shape[0]), 1)
    visible = col < limit
    key_token = key_offset + lax.broadcasted_iota(jnp.int32, (tokens, own_keys.shape[0]), 1)
    row = lax.broadcasted_iota(jnp.int32, (tokens, own_keys.shape[0]), 0)
    query_token = (row // tok_block) * local_tok + row % tok_block
    causal = key_token <= query_token
    dims = (((1,), (1,)), ((), ()))
    for h in range(group_size):
        q = q_ref[c, :, :, h * head_size : (h + 1) * head_size].reshape(tokens, head_size)
        s = lax.dot_general(q, keys, dims, preferred_element_type=jnp.float32) * factor
        s = jnp.where(visible, s, NEG_FILL)
        s_own = lax.dot_general(q, own_keys, dims, preferred_element_type=jnp.float32) * factor
        s_own = jnp.where(causal, s_own, NEG_FILL)
        m = jnp.maximum(
            jnp.max(s, axis=1, keepdims=True), jnp.max(s_own, axis=1, keepdims=True)
        )
        w = jnp.exp(s - m)
        w_own = jnp.exp(s_own - m)
        empty = m < 0.5 * NEG_FILL
        l = jnp.sum(w, axis=1, keepdims=True) + jnp.sum(w_own, axis=1, keepdims=True)
        num = jnp.dot(w.astype(jnp.bfloat16), values, preferred_element_type=jnp.float32)
        num = num + jnp.dot(
            w_own.astype(jnp.bfloat16), own_values, preferred_element_type=jnp.float32
        )
        l = jnp.where(empty, 0.0, l)
        num = jnp.where(empty, 0.0, num)
        safe = jnp.maximum(l, 1.0)
        o_ref[:, :, h * head_size : (h + 1) * head_size] = (
            (num / safe).astype(o_ref.dtype).reshape(src_count, tok_block, head_size)
        )
        lse_ref[:, 0, :, h : h + 1] = (m + jnp.log(safe)).reshape(src_count, tok_block, 1)


def prefill_partial(
    info, order, queries, keys, values, own_keys, own_values, group_size, tok_block, local_tok,
    out_rows,
):
    src_count = order.shape[0]
    qw = queries.shape[2]
    n, p, hd = keys.shape
    own = own_keys.shape[1]
    tokens = src_count * tok_block
    kern = functools.partial(
        _prefill_kernel, group_size=group_size, head_size=hd, local_tok=local_tok
    )
    return pl.pallas_call(
        kern,
        grid_spec=pltpu.PrefetchScalarGridSpec(
            num_scalar_prefetch=2,
            grid=(n,),
            in_specs=[
                pl.BlockSpec(memory_space=pl.ANY),
                pl.BlockSpec((1, p, hd), lambda c, info, order: (c, 0, 0)),
                pl.BlockSpec((1, p, hd), lambda c, info, order: (c, 0, 0)),
                pl.BlockSpec((1, own, hd), lambda c, info, order: (c, 0, 0)),
                pl.BlockSpec((1, own, hd), lambda c, info, order: (c, 0, 0)),
            ],
            out_specs=[
                pl.BlockSpec((src_count, tok_block, qw), lambda c, info, order: (0, c, 0)),
                pl.BlockSpec(
                    (src_count, 1, tok_block, group_size), lambda c, info, order: (0, c, 0, 0)
                ),
            ],
            scratch_shapes=[
                pltpu.VMEM((n, src_count, tok_block, qw), jnp.bfloat16),
                pltpu.SemaphoreType.DMA((n, src_count)),
            ],
        ),
        out_shape=[
            jax.ShapeDtypeStruct((src_count, out_rows, qw), jnp.bfloat16),
            jax.ShapeDtypeStruct((src_count, n, tok_block, group_size), jnp.float32),
        ],
    )(info, order, queries, keys, values, own_keys, own_values)


def _combine_kernel(o_ref, lse_ref, out_ref, *, group_size, head_size):
    stretch_count, local_tok, _ = out_ref.shape
    for c in range(stretch_count):
        lse = lse_ref[:, c]
        top = jnp.max(lse, axis=0, keepdims=True)
        weights = jnp.exp(lse - top)
        total = jnp.sum(weights, axis=0)
        for h in range(group_size):
            part = o_ref[
                :, c * local_tok : (c + 1) * local_tok, h * head_size : (h + 1) * head_size
            ].astype(jnp.float32)
            num = jnp.sum(part * weights[:, :, h : h + 1], axis=0)
            out_ref[c, :, h * head_size : (h + 1) * head_size] = (
                num / total[:, h : h + 1]
            ).astype(out_ref.dtype)


def combine_partials(received, lse, group_size, head_size):
    _, stretch_count, local_tok, _ = lse.shape
    kern = functools.partial(_combine_kernel, group_size=group_size, head_size=head_size)
    return pl.pallas_call(
        kern,
        out_shape=jax.ShapeDtypeStruct(
            (stretch_count, local_tok, group_size * head_size), jnp.bfloat16
        ),
    )(received, lse)


def broadcast_over_seq(pack, seq_rank, seq_count):
    if seq_count > 16 or seq_count % 2:
        every = lax.all_to_all(
            jnp.broadcast_to(pack[None], (seq_count,) + pack.shape), "seq", 0, 0, tiled=True
        )
        return every, jnp.arange(seq_count, dtype=jnp.int32)
    half = seq_count // 2
    partner = lax.ppermute(pack, "seq", [(i, (i + half) % seq_count) for i in range(seq_count)])
    perms = [
        [(i, (i // half) * half + (i % half + shift) % half) for i in range(seq_count)]
        for shift in range(1, half)
    ]
    near_pieces = [lax.ppermute(pack, "seq", perm) for perm in perms]
    far_pieces = [lax.ppermute(partner, "seq", perm) for perm in perms]
    every = jnp.stack([pack, partner] + near_pieces + far_pieces)
    sources = jnp.arange(seq_count, dtype=jnp.int32)
    far = (sources // half) != (seq_rank // half)
    near = jnp.where(far, (sources + half) % seq_count, sources)
    shift_of = (seq_rank % half - near % half) % half
    order = jnp.where(
        far,
        jnp.where(shift_of == 0, 1, half + shift_of),
        jnp.where(shift_of == 0, 0, 1 + shift_of),
    )
    return every, order.astype(jnp.int32)


def body(
    new_query,
    new_key,
    new_value,
    cache_keys,
    cache_values,
    cache_length,
    dealing,
    out_weight,
    stretch_query,
    stretch_key,
    stretch_value,
    prior_keys,
    prior_values,
    stretch_start,
):
    head_size = cache_keys.shape[2]
    group_size = new_query.shape[1] // head_size
    local_dec = new_query.shape[0]
    seq_rank = lax.axis_index("seq")
    seq_count = lax.axis_size("seq")
    total_dec = local_dec * seq_count
    stretch_count, local_tok, query_width = stretch_query.shape
    key_width = stretch_key.shape[2]
    stretch_rows = stretch_count * local_tok

    decode_kv = jnp.concatenate([new_key, new_value], axis=1)
    decode_kv = jnp.pad(decode_kv, ((0, 0), (0, query_width - 2 * key_width)))
    pack = jnp.concatenate(
        [stretch_query.reshape(stretch_rows, query_width), new_query, decode_kv], axis=0
    )
    every, order = broadcast_over_seq(pack, seq_rank, seq_count)
    decode_rows = jnp.take(every[:, stretch_rows:, :], order, axis=0)
    every_query = decode_rows[:, :local_dec, :].reshape(total_dec, query_width)
    every_kv = decode_rows[:, local_dec:, :].reshape(total_dec, query_width)
    every_key = every_kv[:, :key_width]
    every_value = every_kv[:, key_width : 2 * key_width]
    slot_ids = seq_rank * local_dec + jnp.arange(local_dec, dtype=jnp.int32)
    arrival_ids = jnp.arange(total_dec, dtype=jnp.int32)
    sources = jnp.sum(
        jnp.where(dealing[None, :] == slot_ids[:, None], arrival_ids[None, :], 0), axis=1
    )
    home_query = jnp.take(every_query, sources, axis=0)
    home_key = jnp.take(every_key, sources, axis=0)
    home_value = jnp.take(every_value, sources, axis=0)
    cache_span = cache_keys.shape[1]
    cache_pos = jnp.arange(cache_span, dtype=jnp.int32)

    def decode_slot(query_row, own_key, own_value, cached_keys, cached_values, length):
        key_all = jnp.concatenate([cached_keys, own_key[None, :]], axis=0)
        value_all = jnp.concatenate([cached_values, own_value[None, :]], axis=0)
        visible = jnp.concatenate([cache_pos < length, jnp.ones((1,), dtype=jnp.bool_)])
        visible = jnp.broadcast_to(visible[None, :], (group_size, cache_span + 1))
        row_top, weight_sum, numerator = partial_attend(
            query_row.reshape(group_size, head_size), key_all, value_all, visible
        )
        return (
            (numerator / weight_sum[:, None]).astype(jnp.bfloat16).reshape(group_size * head_size)
        )

    home_out = jax.vmap(decode_slot)(
        home_query, home_key, home_value, cache_keys, cache_values, cache_length
    )
    all_out = lax.all_to_all(
        jnp.broadcast_to(home_out[None], (seq_count,) + home_out.shape), "seq", 0, 0, tiled=True
    ).reshape(total_dec, group_size * head_size)
    arrival_out = jnp.take(all_out, dealing, axis=0)
    arrival_terms = jnp.dot(arrival_out, out_weight, preferred_element_type=jnp.float32)
    decode_mixed = lax.psum_scatter(arrival_terms, "tp", scatter_dimension=0, tiled=True).astype(
        jnp.bfloat16
    )

    prior_span = prior_keys.shape[1]
    direct = local_tok % 16 == 0
    stat_count = 3 * stretch_count * local_tok * group_size
    stat_rows = -(-stat_count // query_width)
    out_rows = stretch_rows
    limits = jnp.clip(stretch_start - seq_rank * prior_span, 0, prior_span).astype(jnp.int32)
    info = jnp.concatenate([limits, (seq_rank * local_tok).astype(jnp.int32)[None]])
    if direct:
        payload, part_lse = prefill_partial(
            info, order, every, prior_keys, prior_values, stretch_key, stretch_value, group_size,
            local_tok, local_tok, out_rows + stat_rows,
        )
    else:
        token_count = seq_count * local_tok
        queries_all = (
            jnp.take(every, order, axis=0)[:, :stretch_rows, :]
            .reshape(seq_count, stretch_count, local_tok, query_width)
            .transpose(1, 0, 2, 3)
            .reshape(1, stretch_rows * seq_count, query_width)
        )
        flat_out, part_lse = prefill_partial(
            info, jnp.zeros((1,), jnp.int32), queries_all, prior_keys, prior_values, stretch_key, stretch_value, group_size,
            token_count, token_count, stretch_rows * seq_count,
        )
        payload = jnp.pad(
            flat_out.reshape(stretch_count, seq_count, local_tok, query_width)
            .transpose(1, 0, 2, 3)
            .reshape(seq_count, out_rows, query_width),
            ((0, 0), (0, stat_rows), (0, 0)),
        )
    if not direct:
        part_lse = part_lse.reshape(stretch_count, seq_count, local_tok, group_size).transpose(
            1, 0, 2, 3
        )
    lse_hi = lax.reduce_precision(part_lse, exponent_bits=8, mantissa_bits=7)
    lse_rest = part_lse - lse_hi
    lse_mid = lax.reduce_precision(lse_rest, exponent_bits=8, mantissa_bits=7)
    lse_lo = lse_rest - lse_mid
    stats = jnp.stack([lse_hi, lse_mid, lse_lo], axis=1).reshape(seq_count, stat_count)
    stats = jnp.pad(stats, ((0, 0), (0, stat_rows * query_width - stat_count)))
    payload = lax.dynamic_update_slice(
        payload,
        stats.astype(jnp.bfloat16).reshape(seq_count, stat_rows, query_width),
        (0, out_rows, 0),
    )

    received = lax.all_to_all(payload, "seq", 0, 0, tiled=True)
    got_stats = (
        received[:, out_rows:, :]
        .reshape(seq_count, stat_rows * query_width)[:, :stat_count]
        .astype(jnp.float32)
        .reshape(seq_count, 3, stretch_count, local_tok, group_size)
    )
    got_lse = (got_stats[:, 0] + got_stats[:, 1]) + got_stats[:, 2]
    stretch_out = combine_partials(received, got_lse, group_size, head_size)
    return (decode_mixed, stretch_out)


def solution(mesh):
    return jax.shard_map(
        body,
        mesh=mesh,
        in_specs=(
            P("seq", "tp"),
            P("seq", "tp"),
            P("seq", "tp"),
            P("seq", None, "tp"),
            P("seq", None, "tp"),
            P("seq"),
            P(),
            P("tp", "seq"),
            P(None, "seq", "tp"),
            P(None, "seq", "tp"),
            P(None, "seq", "tp"),
            P(None, "seq", "tp"),
            P(None, "seq", "tp"),
            P(),
        ),
        out_specs=(P("tp", "seq"), P(None, "seq", "tp")),
        check_vma=False,
    )
```

```python
import functools
import math

import jax
import jax.numpy as jnp
from jax import lax
from jax.experimental import pallas as pl
from jax.experimental.pallas import tpu as pltpu
from jax.sharding import PartitionSpec as P

NEG_FILL = -1e30


def partial_attend(queries, keys, values, visible):
    factor = 1.0 / math.sqrt(queries.shape[-1])
    scores = jnp.dot(queries, keys.T, preferred_element_type=jnp.float32) * factor
    scores = jnp.where(visible, scores, NEG_FILL)
    row_top = jnp.max(scores, axis=1)
    weights = jnp.where(visible, jnp.exp(scores - row_top[:, None]), 0.0)
    weight_sum = jnp.sum(weights, axis=1)
    numerator = jnp.dot(weights.astype(jnp.bfloat16), values, preferred_element_type=jnp.float32)
    return (row_top, weight_sum, numerator)


def _prefill_kernel(
    info_ref, order_ref, q_hbm, k_ref, v_ref, sk_ref, sv_ref, o_ref, lse_ref, q_ref, sems,
    *, group_size, head_size, local_tok
):
    c = pl.program_id(0)
    stretch_count, src_count, tok_block, _ = q_ref.shape

    def query_copy(stretch, src):
        return pltpu.make_async_copy(
            q_hbm.at[order_ref[src], pl.ds(stretch * tok_block, tok_block)],
            q_ref.at[stretch, src],
            sems.at[stretch, src],
        )

    @pl.when(c == 0)
    def _():
        for stretch in range(stretch_count):
            for src in range(src_count):
                query_copy(stretch, src).start()

    for src in range(src_count):
        query_copy(c, src).wait()
    limit = info_ref[c]
    key_offset = info_ref[info_ref.shape[0] - 1]
    keys = k_ref[0]
    values = v_ref[0]
    own_keys = sk_ref[0]
    own_values = sv_ref[0]
    factor = 1.0 / math.sqrt(head_size)
    tokens = src_count * tok_block
    col = lax.broadcasted_iota(jnp.int32, (1, keys.shape[0]), 1)
    visible = col < limit
    key_token = key_offset + lax.broadcasted_iota(jnp.int32, (tokens, own_keys.shape[0]), 1)
    row = lax.broadcasted_iota(jnp.int32, (tokens, own_keys.shape[0]), 0)
    query_token = (row // tok_block) * local_tok + row % tok_block
    causal = key_token <= query_token
    dims = (((1,), (1,)), ((), ()))
    for h in range(group_size):
        q = q_ref[c, :, :, h * head_size : (h + 1) * head_size].reshape(tokens, head_size)
        s = lax.dot_general(q, keys, dims, preferred_element_type=jnp.float32) * factor
        s = jnp.where(visible, s, NEG_FILL)
        s_own = lax.dot_general(q, own_keys, dims, preferred_element_type=jnp.float32) * factor
        s_own = jnp.where(causal, s_own, NEG_FILL)
        m = jnp.maximum(
            jnp.max(s, axis=1, keepdims=True), jnp.max(s_own, axis=1, keepdims=True)
        )
        w = jnp.exp(s - m)
        w_own = jnp.exp(s_own - m)
        empty = m < 0.5 * NEG_FILL
        l = jnp.sum(w, axis=1, keepdims=True) + jnp.sum(w_own, axis=1, keepdims=True)
        num = jnp.dot(w.astype(jnp.bfloat16), values, preferred_element_type=jnp.float32)
        num = num + jnp.dot(
            w_own.astype(jnp.bfloat16), own_values, preferred_element_type=jnp.float32
        )
        l = jnp.where(empty, 0.0, l)
        num = jnp.where(empty, 0.0, num)
        safe = jnp.maximum(l, 1.0)
        o_ref[:, :, h * head_size : (h + 1) * head_size] = (
            (num / safe).astype(o_ref.dtype).reshape(src_count, tok_block, head_size)
        )
        lse_ref[:, 0, :, h : h + 1] = (m + jnp.log(safe)).reshape(src_count, tok_block, 1)


def prefill_partial(
    info, order, queries, keys, values, own_keys, own_values, group_size, tok_block, local_tok,
    out_rows,
):
    src_count = order.shape[0]
    qw = queries.shape[2]
    n, p, hd = keys.shape
    own = own_keys.shape[1]
    tokens = src_count * tok_block
    kern = functools.partial(
        _prefill_kernel, group_size=group_size, head_size=hd, local_tok=local_tok
    )
    return pl.pallas_call(
        kern,
        grid_spec=pltpu.PrefetchScalarGridSpec(
            num_scalar_prefetch=2,
            grid=(n,),
            in_specs=[
                pl.BlockSpec(memory_space=pl.ANY),
                pl.BlockSpec((1, p, hd), lambda c, info, order: (c, 0, 0)),
                pl.BlockSpec((1, p, hd), lambda c, info, order: (c, 0, 0)),
                pl.BlockSpec((1, own, hd), lambda c, info, order: (c, 0, 0)),
                pl.BlockSpec((1, own, hd), lambda c, info, order: (c, 0, 0)),
            ],
            out_specs=[
                pl.BlockSpec((src_count, tok_block, qw), lambda c, info, order: (0, c, 0)),
                pl.BlockSpec(
                    (src_count, 1, tok_block, group_size), lambda c, info, order: (0, c, 0, 0)
                ),
            ],
            scratch_shapes=[
                pltpu.VMEM((n, src_count, tok_block, qw), jnp.bfloat16),
                pltpu.SemaphoreType.DMA((n, src_count)),
            ],
        ),
        out_shape=[
            jax.ShapeDtypeStruct((src_count, out_rows, qw), jnp.bfloat16),
            jax.ShapeDtypeStruct((src_count, n, tok_block, group_size), jnp.float32),
        ],
    )(info, order, queries, keys, values, own_keys, own_values)


def _combine_kernel(o_ref, lse_ref, out_ref, *, group_size, head_size):
    stretch_count, local_tok, _ = out_ref.shape
    for c in range(stretch_count):
        parts = [lse_ref[:, p, c].astype(jnp.float32) for p in range(3)]
        lse = (parts[0] + parts[1]) + parts[2]
        top = jnp.max(lse, axis=0, keepdims=True)
        weights = jnp.exp(lse - top)
        total = jnp.sum(weights, axis=0)
        for h in range(group_size):
            part = o_ref[
                :, c * local_tok : (c + 1) * local_tok, h * head_size : (h + 1) * head_size
            ].astype(jnp.float32)
            num = jnp.sum(part * weights[:, :, h : h + 1], axis=0)
            out_ref[c, :, h * head_size : (h + 1) * head_size] = (
                num / total[:, h : h + 1]
            ).astype(out_ref.dtype)


def combine_partials(received, lse, group_size, head_size):
    _, _, stretch_count, local_tok, _ = lse.shape
    kern = functools.partial(_combine_kernel, group_size=group_size, head_size=head_size)
    return pl.pallas_call(
        kern,
        out_shape=jax.ShapeDtypeStruct(
            (stretch_count, local_tok, group_size * head_size), jnp.bfloat16
        ),
    )(received, lse)


def broadcast_over_seq(pack, seq_rank, seq_count):
    if seq_count > 16 or seq_count % 2:
        every = lax.all_to_all(
            jnp.broadcast_to(pack[None], (seq_count,) + pack.shape), "seq", 0, 0, tiled=True
        )
        return every, jnp.arange(seq_count, dtype=jnp.int32)
    half = seq_count // 2
    partner = lax.ppermute(pack, "seq", [(i, (i + half) % seq_count) for i in range(seq_count)])
    perms = [
        [(i, (i // half) * half + (i % half + shift) % half) for i in range(seq_count)]
        for shift in range(1, half)
    ]
    near_pieces = [lax.ppermute(pack, "seq", perm) for perm in perms]
    far_pieces = [lax.ppermute(partner, "seq", perm) for perm in perms]
    every = jnp.stack([pack, partner] + near_pieces + far_pieces)
    sources = jnp.arange(seq_count, dtype=jnp.int32)
    far = (sources // half) != (seq_rank // half)
    near = jnp.where(far, (sources + half) % seq_count, sources)
    shift_of = (seq_rank % half - near % half) % half
    order = jnp.where(
        far,
        jnp.where(shift_of == 0, 1, half + shift_of),
        jnp.where(shift_of == 0, 0, 1 + shift_of),
    )
    return every, order.astype(jnp.int32)


def body(
    new_query,
    new_key,
    new_value,
    cache_keys,
    cache_values,
    cache_length,
    dealing,
    out_weight,
    stretch_query,
    stretch_key,
    stretch_value,
    prior_keys,
    prior_values,
    stretch_start,
):
    head_size = cache_keys.shape[2]
    group_size = new_query.shape[1] // head_size
    local_dec = new_query.shape[0]
    seq_rank = lax.axis_index("seq")
    seq_count = lax.axis_size("seq")
    total_dec = local_dec * seq_count
    stretch_count, local_tok, query_width = stretch_query.shape
    key_width = stretch_key.shape[2]
    stretch_rows = stretch_count * local_tok

    decode_kv = jnp.concatenate([new_key, new_value], axis=1)
    decode_kv = jnp.pad(decode_kv, ((0, 0), (0, query_width - 2 * key_width)))
    pack = jnp.concatenate(
        [stretch_query.reshape(stretch_rows, query_width), new_query, decode_kv], axis=0
    )
    every, order = broadcast_over_seq(pack, seq_rank, seq_count)
    decode_rows = jnp.take(every[:, stretch_rows:, :], order, axis=0)
    every_query = decode_rows[:, :local_dec, :].reshape(total_dec, query_width)
    every_kv = decode_rows[:, local_dec:, :].reshape(total_dec, query_width)
    every_key = every_kv[:, :key_width]
    every_value = every_kv[:, key_width : 2 * key_width]
    slot_ids = seq_rank * local_dec + jnp.arange(local_dec, dtype=jnp.int32)
    arrival_ids = jnp.arange(total_dec, dtype=jnp.int32)
    sources = jnp.sum(
        jnp.where(dealing[None, :] == slot_ids[:, None], arrival_ids[None, :], 0), axis=1
    )
    home_query = jnp.take(every_query, sources, axis=0)
    home_key = jnp.take(every_key, sources, axis=0)
    home_value = jnp.take(every_value, sources, axis=0)
    cache_span = cache_keys.shape[1]
    cache_pos = jnp.arange(cache_span, dtype=jnp.int32)

    def decode_slot(query_row, own_key, own_value, cached_keys, cached_values, length):
        key_all = jnp.concatenate([cached_keys, own_key[None, :]], axis=0)
        value_all = jnp.concatenate([cached_values, own_value[None, :]], axis=0)
        visible = jnp.concatenate([cache_pos < length, jnp.ones((1,), dtype=jnp.bool_)])
        visible = jnp.broadcast_to(visible[None, :], (group_size, cache_span + 1))
        row_top, weight_sum, numerator = partial_attend(
            query_row.reshape(group_size, head_size), key_all, value_all, visible
        )
        return (
            (numerator / weight_sum[:, None]).astype(jnp.bfloat16).reshape(group_size * head_size)
        )

    home_out = jax.vmap(decode_slot)(
        home_query, home_key, home_value, cache_keys, cache_values, cache_length
    )
    all_out = lax.all_to_all(
        jnp.broadcast_to(home_out[None], (seq_count,) + home_out.shape), "seq", 0, 0, tiled=True
    ).reshape(total_dec, group_size * head_size)
    arrival_out = jnp.take(all_out, dealing, axis=0)
    arrival_terms = jnp.dot(arrival_out, out_weight, preferred_element_type=jnp.float32)
    decode_mixed = lax.psum_scatter(arrival_terms, "tp", scatter_dimension=0, tiled=True).astype(
        jnp.bfloat16
    )

    prior_span = prior_keys.shape[1]
    direct = local_tok % 16 == 0
    stat_count = 3 * stretch_count * local_tok * group_size
    stat_rows = -(-stat_count // query_width)
    out_rows = stretch_rows
    limits = jnp.clip(stretch_start - seq_rank * prior_span, 0, prior_span).astype(jnp.int32)
    info = jnp.concatenate([limits, (seq_rank * local_tok).astype(jnp.int32)[None]])
    if direct:
        payload, part_lse = prefill_partial(
            info, order, every, prior_keys, prior_values, stretch_key, stretch_value, group_size,
            local_tok, local_tok, out_rows + stat_rows,
        )
    else:
        token_count = seq_count * local_tok
        queries_all = (
            jnp.take(every, order, axis=0)[:, :stretch_rows, :]
            .reshape(seq_count, stretch_count, local_tok, query_width)
            .transpose(1, 0, 2, 3)
            .reshape(1, stretch_rows * seq_count, query_width)
        )
        flat_out, part_lse = prefill_partial(
            info, jnp.zeros((1,), jnp.int32), queries_all, prior_keys, prior_values, stretch_key, stretch_value, group_size,
            token_count, token_count, stretch_rows * seq_count,
        )
        payload = jnp.pad(
            flat_out.reshape(stretch_count, seq_count, local_tok, query_width)
            .transpose(1, 0, 2, 3)
            .reshape(seq_count, out_rows, query_width),
            ((0, 0), (0, stat_rows), (0, 0)),
        )
    if not direct:
        part_lse = part_lse.reshape(stretch_count, seq_count, local_tok, group_size).transpose(
            1, 0, 2, 3
        )
    lse_hi = lax.reduce_precision(part_lse, exponent_bits=8, mantissa_bits=7)
    lse_rest = part_lse - lse_hi
    lse_mid = lax.reduce_precision(lse_rest, exponent_bits=8, mantissa_bits=7)
    lse_lo = lse_rest - lse_mid
    stats = jnp.stack([lse_hi, lse_mid, lse_lo], axis=1).reshape(seq_count, stat_count)
    stats = jnp.pad(stats, ((0, 0), (0, stat_rows * query_width - stat_count)))
    payload = lax.dynamic_update_slice(
        payload,
        stats.astype(jnp.bfloat16).reshape(seq_count, stat_rows, query_width),
        (0, out_rows, 0),
    )

    received = lax.all_to_all(payload, "seq", 0, 0, tiled=True)
    got_stats = (
        received[:, out_rows:, :]
        .reshape(seq_count, stat_rows * query_width)[:, :stat_count]
        .reshape(seq_count, 3, stretch_count, local_tok, group_size)
    )
    stretch_out = combine_partials(received, got_stats, group_size, head_size)
    return (decode_mixed, stretch_out)


def solution(mesh):
    return jax.shard_map(
        body,
        mesh=mesh,
        in_specs=(
            P("seq", "tp"),
            P("seq", "tp"),
            P("seq", "tp"),
            P("seq", None, "tp"),
            P("seq", None, "tp"),
            P("seq"),
            P(),
            P("tp", "seq"),
            P(None, "seq", "tp"),
            P(None, "seq", "tp"),
            P(None, "seq", "tp"),
            P(None, "seq", "tp"),
            P(None, "seq", "tp"),
            P(),
        ),
        out_specs=(P("tp", "seq"), P(None, "seq", "tp")),
        check_vma=False,
    )
```

```python
import functools
import math

import jax
import jax.numpy as jnp
from jax import lax
from jax.experimental import pallas as pl
from jax.experimental.pallas import tpu as pltpu
from jax.sharding import PartitionSpec as P

NEG_FILL = -1e30


def partial_attend(queries, keys, values, visible):
    factor = 1.0 / math.sqrt(queries.shape[-1])
    scores = jnp.dot(queries, keys.T, preferred_element_type=jnp.float32) * factor
    scores = jnp.where(visible, scores, NEG_FILL)
    row_top = jnp.max(scores, axis=1)
    weights = jnp.where(visible, jnp.exp(scores - row_top[:, None]), 0.0)
    weight_sum = jnp.sum(weights, axis=1)
    numerator = jnp.dot(weights.astype(jnp.bfloat16), values, preferred_element_type=jnp.float32)
    return (row_top, weight_sum, numerator)


def _prefill_kernel(
    info_ref, order_ref, q_hbm, k_ref, v_ref, sk_ref, sv_ref, o_ref, lse_ref, q_ref, sems,
    *, group_size, head_size, local_tok
):
    c = pl.program_id(0)
    stretch_count, src_count, tok_block, _ = q_ref.shape

    def query_copy(stretch, src):
        return pltpu.make_async_copy(
            q_hbm.at[order_ref[src], pl.ds(stretch * tok_block, tok_block)],
            q_ref.at[stretch, src],
            sems.at[stretch, src],
        )

    @pl.when(c == 0)
    def _():
        for stretch in range(stretch_count):
            for src in range(src_count):
                query_copy(stretch, src).start()

    for src in range(src_count):
        query_copy(c, src).wait()
    limit = info_ref[c]
    key_offset = info_ref[info_ref.shape[0] - 1]
    keys = k_ref[0]
    values = v_ref[0]
    own_keys = sk_ref[0]
    own_values = sv_ref[0]
    factor = 1.0 / math.sqrt(head_size)
    tokens = src_count * tok_block
    col = lax.broadcasted_iota(jnp.int32, (1, keys.shape[0]), 1)
    visible = col < limit
    key_token = key_offset + lax.broadcasted_iota(jnp.int32, (tokens, own_keys.shape[0]), 1)
    row = lax.broadcasted_iota(jnp.int32, (tokens, own_keys.shape[0]), 0)
    query_token = (row // tok_block) * local_tok + row % tok_block
    causal = key_token <= query_token
    dims = (((1,), (1,)), ((), ()))
    for h in range(group_size):
        q = q_ref[c, :, :, h * head_size : (h + 1) * head_size].reshape(tokens, head_size)
        s = lax.dot_general(q, keys, dims, preferred_element_type=jnp.float32) * factor
        s = jnp.where(visible, s, NEG_FILL)
        s_own = lax.dot_general(q, own_keys, dims, preferred_element_type=jnp.float32) * factor
        s_own = jnp.where(causal, s_own, NEG_FILL)
        m = jnp.maximum(
            jnp.max(s, axis=1, keepdims=True), jnp.max(s_own, axis=1, keepdims=True)
        )
        w = jnp.exp(s - m)
        w_own = jnp.exp(s_own - m)
        empty = m < 0.5 * NEG_FILL
        l = jnp.sum(w, axis=1, keepdims=True) + jnp.sum(w_own, axis=1, keepdims=True)
        num = jnp.dot(w.astype(jnp.bfloat16), values, preferred_element_type=jnp.float32)
        num = num + jnp.dot(
            w_own.astype(jnp.bfloat16), own_values, preferred_element_type=jnp.float32
        )
        l = jnp.where(empty, 0.0, l)
        num = jnp.where(empty, 0.0, num)
        safe = jnp.maximum(l, 1.0)
        o_ref[:, :, h * head_size : (h + 1) * head_size] = (
            (num / safe).astype(o_ref.dtype).reshape(src_count, tok_block, head_size)
        )
        lse_ref[:, 0, :, h : h + 1] = (m + jnp.log(safe)).reshape(src_count, tok_block, 1)


def prefill_partial(
    info, order, queries, keys, values, own_keys, own_values, group_size, tok_block, local_tok,
    out_rows,
):
    src_count = order.shape[0]
    qw = queries.shape[2]
    n, p, hd = keys.shape
    own = own_keys.shape[1]
    tokens = src_count * tok_block
    kern = functools.partial(
        _prefill_kernel, group_size=group_size, head_size=hd, local_tok=local_tok
    )
    return pl.pallas_call(
        kern,
        grid_spec=pltpu.PrefetchScalarGridSpec(
            num_scalar_prefetch=2,
            grid=(n,),
            in_specs=[
                pl.BlockSpec(memory_space=pl.ANY),
                pl.BlockSpec((1, p, hd), lambda c, info, order: (c, 0, 0)),
                pl.BlockSpec((1, p, hd), lambda c, info, order: (c, 0, 0)),
                pl.BlockSpec((1, own, hd), lambda c, info, order: (c, 0, 0)),
                pl.BlockSpec((1, own, hd), lambda c, info, order: (c, 0, 0)),
            ],
            out_specs=[
                pl.BlockSpec((src_count, tok_block, qw), lambda c, info, order: (0, c, 0)),
                pl.BlockSpec(
                    (src_count, 1, tok_block, group_size), lambda c, info, order: (0, c, 0, 0)
                ),
            ],
            scratch_shapes=[
                pltpu.VMEM((n, src_count, tok_block, qw), jnp.bfloat16),
                pltpu.SemaphoreType.DMA((n, src_count)),
            ],
        ),
        out_shape=[
            jax.ShapeDtypeStruct((src_count, out_rows, qw), jnp.bfloat16),
            jax.ShapeDtypeStruct((src_count, n, tok_block, group_size), jnp.float32),
        ],
    )(info, order, queries, keys, values, own_keys, own_values)


def _combine_kernel(o_ref, lse_ref, out_ref, *, group_size, head_size):
    stretch_count, local_tok, _ = out_ref.shape
    for c in range(stretch_count):
        lse = lse_ref[:, c]
        top = jnp.max(lse, axis=0, keepdims=True)
        weights = jnp.exp(lse - top)
        total = jnp.sum(weights, axis=0)
        for h in range(group_size):
            part = o_ref[
                :, c * local_tok : (c + 1) * local_tok, h * head_size : (h + 1) * head_size
            ].astype(jnp.float32)
            num = jnp.sum(part * weights[:, :, h : h + 1], axis=0)
            out_ref[c, :, h * head_size : (h + 1) * head_size] = (
                num / total[:, h : h + 1]
            ).astype(out_ref.dtype)


def combine_partials(received, lse, group_size, head_size):
    _, stretch_count, local_tok, _ = lse.shape
    kern = functools.partial(_combine_kernel, group_size=group_size, head_size=head_size)
    return pl.pallas_call(
        kern,
        out_shape=jax.ShapeDtypeStruct(
            (stretch_count, local_tok, group_size * head_size), jnp.bfloat16
        ),
    )(received, lse)


def broadcast_over_seq(pack, seq_rank, seq_count):
    if seq_count > 16 or seq_count % 2:
        every = lax.all_to_all(
            jnp.broadcast_to(pack[None], (seq_count,) + pack.shape), "seq", 0, 0, tiled=True
        )
        return every, jnp.arange(seq_count, dtype=jnp.int32)
    half = seq_count // 2
    partner = lax.ppermute(pack, "seq", [(i, (i + half) % seq_count) for i in range(seq_count)])
    perms = [
        [(i, (i // half) * half + (i % half + shift) % half) for i in range(seq_count)]
        for shift in range(1, half)
    ]
    near_pieces = [lax.ppermute(pack, "seq", perm) for perm in perms]
    far_pieces = [lax.ppermute(partner, "seq", perm) for perm in perms]
    every = jnp.stack([pack, partner] + near_pieces + far_pieces)
    sources = jnp.arange(seq_count, dtype=jnp.int32)
    far = (sources // half) != (seq_rank // half)
    near = jnp.where(far, (sources + half) % seq_count, sources)
    shift_of = (seq_rank % half - near % half) % half
    order = jnp.where(
        far,
        jnp.where(shift_of == 0, 1, half + shift_of),
        jnp.where(shift_of == 0, 0, 1 + shift_of),
    )
    return every, order.astype(jnp.int32)


def body(
    new_query,
    new_key,
    new_value,
    cache_keys,
    cache_values,
    cache_length,
    dealing,
    out_weight,
    stretch_query,
    stretch_key,
    stretch_value,
    prior_keys,
    prior_values,
    stretch_start,
):
    head_size = cache_keys.shape[2]
    group_size = new_query.shape[1] // head_size
    local_dec = new_query.shape[0]
    seq_rank = lax.axis_index("seq")
    seq_count = lax.axis_size("seq")
    total_dec = local_dec * seq_count
    stretch_count, local_tok, query_width = stretch_query.shape
    key_width = stretch_key.shape[2]
    stretch_rows = stretch_count * local_tok

    decode_kv = jnp.concatenate([new_key, new_value], axis=1)
    decode_kv = jnp.pad(decode_kv, ((0, 0), (0, query_width - 2 * key_width)))
    pack = jnp.concatenate(
        [stretch_query.reshape(stretch_rows, query_width), new_query, decode_kv], axis=0
    )
    every, order = broadcast_over_seq(pack, seq_rank, seq_count)
    decode_rows = jnp.take(every[:, stretch_rows:, :], order, axis=0)
    every_query = decode_rows[:, :local_dec, :].reshape(total_dec, query_width)
    every_kv = decode_rows[:, local_dec:, :].reshape(total_dec, query_width)
    every_key = every_kv[:, :key_width]
    every_value = every_kv[:, key_width : 2 * key_width]
    slot_ids = seq_rank * local_dec + jnp.arange(local_dec, dtype=jnp.int32)
    arrival_ids = jnp.arange(total_dec, dtype=jnp.int32)
    sources = jnp.sum(
        jnp.where(dealing[None, :] == slot_ids[:, None], arrival_ids[None, :], 0), axis=1
    )
    home_query = jnp.take(every_query, sources, axis=0)
    home_key = jnp.take(every_key, sources, axis=0)
    home_value = jnp.take(every_value, sources, axis=0)
    cache_span = cache_keys.shape[1]
    cache_pos = jnp.arange(cache_span, dtype=jnp.int32)

    def decode_slot(query_row, own_key, own_value, cached_keys, cached_values, length):
        factor = 1.0 / math.sqrt(head_size)
        queries = query_row.reshape(group_size, head_size)
        visible = (cache_pos < length)[None, :]
        scores = jnp.dot(queries, cached_keys.T, preferred_element_type=jnp.float32) * factor
        scores = jnp.where(visible, scores, NEG_FILL)
        own_score = (
            jnp.dot(queries, own_key[:, None], preferred_element_type=jnp.float32) * factor
        )
        row_top = jnp.maximum(jnp.max(scores, axis=1, keepdims=True), own_score)
        weights = jnp.where(visible, jnp.exp(scores - row_top), 0.0)
        own_weight = jnp.exp(own_score - row_top)
        weight_sum = jnp.sum(weights, axis=1, keepdims=True) + own_weight
        numerator = jnp.dot(
            weights.astype(jnp.bfloat16), cached_values, preferred_element_type=jnp.float32
        ) + lax.reduce_precision(own_weight, exponent_bits=8, mantissa_bits=7) * own_value.astype(
            jnp.float32
        )
        return (numerator / weight_sum).astype(jnp.bfloat16).reshape(group_size * head_size)

    home_out = jax.vmap(decode_slot)(
        home_query, home_key, home_value, cache_keys, cache_values, cache_length
    )
    all_out = lax.all_to_all(
        jnp.broadcast_to(home_out[None], (seq_count,) + home_out.shape), "seq", 0, 0, tiled=True
    ).reshape(total_dec, group_size * head_size)
    arrival_out = jnp.take(all_out, dealing, axis=0)
    arrival_terms = jnp.dot(arrival_out, out_weight, preferred_element_type=jnp.float32)
    decode_mixed = lax.psum_scatter(arrival_terms, "tp", scatter_dimension=0, tiled=True).astype(
        jnp.bfloat16
    )

    prior_span = prior_keys.shape[1]
    direct = local_tok % 16 == 0
    stat_count = 3 * stretch_count * local_tok * group_size
    stat_rows = -(-stat_count // query_width)
    out_rows = stretch_rows
    limits = jnp.clip(stretch_start - seq_rank * prior_span, 0, prior_span).astype(jnp.int32)
    info = jnp.concatenate([limits, (seq_rank * local_tok).astype(jnp.int32)[None]])
    if direct:
        payload, part_lse = prefill_partial(
            info, order, every, prior_keys, prior_values, stretch_key, stretch_value, group_size,
            local_tok, local_tok, out_rows + stat_rows,
        )
    else:
        token_count = seq_count * local_tok
        queries_all = (
            jnp.take(every, order, axis=0)[:, :stretch_rows, :]
            .reshape(seq_count, stretch_count, local_tok, query_width)
            .transpose(1, 0, 2, 3)
            .reshape(1, stretch_rows * seq_count, query_width)
        )
        flat_out, part_lse = prefill_partial(
            info, jnp.zeros((1,), jnp.int32), queries_all, prior_keys, prior_values, stretch_key, stretch_value, group_size,
            token_count, token_count, stretch_rows * seq_count,
        )
        payload = jnp.pad(
            flat_out.reshape(stretch_count, seq_count, local_tok, query_width)
            .transpose(1, 0, 2, 3)
            .reshape(seq_count, out_rows, query_width),
            ((0, 0), (0, stat_rows), (0, 0)),
        )
    if not direct:
        part_lse = part_lse.reshape(stretch_count, seq_count, local_tok, group_size).transpose(
            1, 0, 2, 3
        )
    lse_hi = lax.reduce_precision(part_lse, exponent_bits=8, mantissa_bits=7)
    lse_rest = part_lse - lse_hi
    lse_mid = lax.reduce_precision(lse_rest, exponent_bits=8, mantissa_bits=7)
    lse_lo = lse_rest - lse_mid
    stats = jnp.stack([lse_hi, lse_mid, lse_lo], axis=1).reshape(seq_count, stat_count)
    stats = jnp.pad(stats, ((0, 0), (0, stat_rows * query_width - stat_count)))
    payload = lax.dynamic_update_slice(
        payload,
        stats.astype(jnp.bfloat16).reshape(seq_count, stat_rows, query_width),
        (0, out_rows, 0),
    )

    received = lax.all_to_all(payload, "seq", 0, 0, tiled=True)
    got_stats = (
        received[:, out_rows:, :]
        .reshape(seq_count, stat_rows * query_width)[:, :stat_count]
        .astype(jnp.float32)
        .reshape(seq_count, 3, stretch_count, local_tok, group_size)
    )
    got_lse = (got_stats[:, 0] + got_stats[:, 1]) + got_stats[:, 2]
    stretch_out = combine_partials(received, got_lse, group_size, head_size)
    return (decode_mixed, stretch_out)


def solution(mesh):
    return jax.shard_map(
        body,
        mesh=mesh,
        in_specs=(
            P("seq", "tp"),
            P("seq", "tp"),
            P("seq", "tp"),
            P("seq", None, "tp"),
            P("seq", None, "tp"),
            P("seq"),
            P(),
            P("tp", "seq"),
            P(None, "seq", "tp"),
            P(None, "seq", "tp"),
            P(None, "seq", "tp"),
            P(None, "seq", "tp"),
            P(None, "seq", "tp"),
            P(),
        ),
        out_specs=(P("tp", "seq"), P(None, "seq", "tp")),
        check_vma=False,
    )
```

```python
import functools
import math

import jax
import jax.numpy as jnp
from jax import lax
from jax.experimental import pallas as pl
from jax.experimental.pallas import tpu as pltpu
from jax.sharding import PartitionSpec as P

NEG_FILL = -1e30


def partial_attend(queries, keys, values, visible):
    factor = 1.0 / math.sqrt(queries.shape[-1])
    scores = jnp.dot(queries, keys.T, preferred_element_type=jnp.float32) * factor
    scores = jnp.where(visible, scores, NEG_FILL)
    row_top = jnp.max(scores, axis=1)
    weights = jnp.where(visible, jnp.exp(scores - row_top[:, None]), 0.0)
    weight_sum = jnp.sum(weights, axis=1)
    numerator = jnp.dot(weights.astype(jnp.bfloat16), values, preferred_element_type=jnp.float32)
    return (row_top, weight_sum, numerator)


def _prefill_kernel(
    info_ref, order_ref, q_hbm, k_ref, v_ref, sk_ref, sv_ref, o_ref, lse_ref, q_ref, sems,
    *, group_size, head_size, local_tok
):
    c = pl.program_id(0)
    stretch_count, src_count, tok_block, _ = q_ref.shape

    def query_copy(stretch, src):
        return pltpu.make_async_copy(
            q_hbm.at[order_ref[src], pl.ds(stretch * tok_block, tok_block)],
            q_ref.at[stretch, src],
            sems.at[stretch, src],
        )

    @pl.when(c == 0)
    def _():
        for stretch in range(stretch_count):
            for src in range(src_count):
                query_copy(stretch, src).start()

    for src in range(src_count):
        query_copy(c, src).wait()
    limit = info_ref[c]
    key_offset = info_ref[info_ref.shape[0] - 1]
    keys = k_ref[0]
    values = v_ref[0]
    own_keys = sk_ref[0]
    own_values = sv_ref[0]
    factor = 1.0 / math.sqrt(head_size)
    tokens = src_count * tok_block
    col = lax.broadcasted_iota(jnp.int32, (1, keys.shape[0]), 1)
    visible = col < limit
    key_token = key_offset + lax.broadcasted_iota(jnp.int32, (tokens, own_keys.shape[0]), 1)
    row = lax.broadcasted_iota(jnp.int32, (tokens, own_keys.shape[0]), 0)
    query_token = (row // tok_block) * local_tok + row % tok_block
    causal = key_token <= query_token
    dims = (((1,), (1,)), ((), ()))
    for h in range(group_size):
        q = q_ref[c, :, :, h * head_size : (h + 1) * head_size].reshape(tokens, head_size)
        s = lax.dot_general(q, keys, dims, preferred_element_type=jnp.float32) * factor
        s = jnp.where(visible, s, NEG_FILL)
        s_own = lax.dot_general(q, own_keys, dims, preferred_element_type=jnp.float32) * factor
        s_own = jnp.where(causal, s_own, NEG_FILL)
        m = jnp.maximum(
            jnp.max(s, axis=1, keepdims=True), jnp.max(s_own, axis=1, keepdims=True)
        )
        w = jnp.exp(s - m)
        w_own = jnp.exp(s_own - m)
        empty = m < 0.5 * NEG_FILL
        l = jnp.sum(w, axis=1, keepdims=True) + jnp.sum(w_own, axis=1, keepdims=True)
        num = jnp.dot(w.astype(jnp.bfloat16), values, preferred_element_type=jnp.float32)
        num = num + jnp.dot(
            w_own.astype(jnp.bfloat16), own_values, preferred_element_type=jnp.float32
        )
        l = jnp.where(empty, 0.0, l)
        num = jnp.where(empty, 0.0, num)
        safe = jnp.maximum(l, 1.0)
        o_ref[:, :, h * head_size : (h + 1) * head_size] = (
            (num / safe).astype(o_ref.dtype).reshape(src_count, tok_block, head_size)
        )
        lse_ref[:, 0, :, h : h + 1] = (m + jnp.log(safe)).reshape(src_count, tok_block, 1)


def prefill_partial(
    info, order, queries, keys, values, own_keys, own_values, group_size, tok_block, local_tok,
    out_rows,
):
    src_count = order.shape[0]
    qw = queries.shape[2]
    n, p, hd = keys.shape
    own = own_keys.shape[1]
    tokens = src_count * tok_block
    kern = functools.partial(
        _prefill_kernel, group_size=group_size, head_size=hd, local_tok=local_tok
    )
    return pl.pallas_call(
        kern,
        grid_spec=pltpu.PrefetchScalarGridSpec(
            num_scalar_prefetch=2,
            grid=(n,),
            in_specs=[
                pl.BlockSpec(memory_space=pl.ANY),
                pl.BlockSpec((1, p, hd), lambda c, info, order: (c, 0, 0)),
                pl.BlockSpec((1, p, hd), lambda c, info, order: (c, 0, 0)),
                pl.BlockSpec((1, own, hd), lambda c, info, order: (c, 0, 0)),
                pl.BlockSpec((1, own, hd), lambda c, info, order: (c, 0, 0)),
            ],
            out_specs=[
                pl.BlockSpec((src_count, tok_block, qw), lambda c, info, order: (0, c, 0)),
                pl.BlockSpec(
                    (src_count, 1, tok_block, group_size), lambda c, info, order: (0, c, 0, 0)
                ),
            ],
            scratch_shapes=[
                pltpu.VMEM((n, src_count, tok_block, qw), jnp.bfloat16),
                pltpu.SemaphoreType.DMA((n, src_count)),
            ],
        ),
        out_shape=[
            jax.ShapeDtypeStruct((src_count, out_rows, qw), jnp.bfloat16),
            jax.ShapeDtypeStruct((src_count, n, tok_block, group_size), jnp.float32),
        ],
    )(info, order, queries, keys, values, own_keys, own_values)


def _combine_kernel(o_ref, lse_ref, out_ref, *, group_size, head_size):
    stretch_count, local_tok, _ = out_ref.shape
    for c in range(stretch_count):
        lse = lse_ref[:, c]
        top = jnp.max(lse, axis=0, keepdims=True)
        weights = jnp.exp(lse - top)
        total = jnp.sum(weights, axis=0)
        for h in range(group_size):
            part = o_ref[
                :, c * local_tok : (c + 1) * local_tok, h * head_size : (h + 1) * head_size
            ].astype(jnp.float32)
            num = jnp.sum(part * weights[:, :, h : h + 1], axis=0)
            out_ref[c, :, h * head_size : (h + 1) * head_size] = (
                num / total[:, h : h + 1]
            ).astype(out_ref.dtype)


def combine_partials(received, lse, group_size, head_size):
    src_count, stretch_count, local_tok, _ = lse.shape
    kern = functools.partial(_combine_kernel, group_size=group_size, head_size=head_size)
    out_shape = jax.ShapeDtypeStruct(
        (stretch_count, local_tok, group_size * head_size), jnp.bfloat16
    )
    if local_tok % 16:
        return pl.pallas_call(kern, out_shape=out_shape)(received, lse)
    width = received.shape[2]
    return pl.pallas_call(
        kern,
        grid=(stretch_count,),
        in_specs=[
            pl.BlockSpec((src_count, local_tok, width), lambda c: (0, c, 0)),
            pl.BlockSpec((src_count, 1, local_tok, group_size), lambda c: (0, c, 0, 0)),
        ],
        out_specs=pl.BlockSpec((1, local_tok, width), lambda c: (c, 0, 0)),
        out_shape=out_shape,
    )(received, lse)


def broadcast_over_seq(pack, seq_rank, seq_count):
    if seq_count > 16 or seq_count % 2:
        every = lax.all_to_all(
            jnp.broadcast_to(pack[None], (seq_count,) + pack.shape), "seq", 0, 0, tiled=True
        )
        return every, jnp.arange(seq_count, dtype=jnp.int32)
    half = seq_count // 2
    partner = lax.ppermute(pack, "seq", [(i, (i + half) % seq_count) for i in range(seq_count)])
    perms = [
        [(i, (i // half) * half + (i % half + shift) % half) for i in range(seq_count)]
        for shift in range(1, half)
    ]
    near_pieces = [lax.ppermute(pack, "seq", perm) for perm in perms]
    far_pieces = [lax.ppermute(partner, "seq", perm) for perm in perms]
    every = jnp.stack([pack, partner] + near_pieces + far_pieces)
    sources = jnp.arange(seq_count, dtype=jnp.int32)
    far = (sources // half) != (seq_rank // half)
    near = jnp.where(far, (sources + half) % seq_count, sources)
    shift_of = (seq_rank % half - near % half) % half
    order = jnp.where(
        far,
        jnp.where(shift_of == 0, 1, half + shift_of),
        jnp.where(shift_of == 0, 0, 1 + shift_of),
    )
    return every, order.astype(jnp.int32)


def body(
    new_query,
    new_key,
    new_value,
    cache_keys,
    cache_values,
    cache_length,
    dealing,
    out_weight,
    stretch_query,
    stretch_key,
    stretch_value,
    prior_keys,
    prior_values,
    stretch_start,
):
    head_size = cache_keys.shape[2]
    group_size = new_query.shape[1] // head_size
    local_dec = new_query.shape[0]
    seq_rank = lax.axis_index("seq")
    seq_count = lax.axis_size("seq")
    total_dec = local_dec * seq_count
    stretch_count, local_tok, query_width = stretch_query.shape
    key_width = stretch_key.shape[2]
    stretch_rows = stretch_count * local_tok

    decode_kv = jnp.concatenate([new_key, new_value], axis=1)
    decode_kv = jnp.pad(decode_kv, ((0, 0), (0, query_width - 2 * key_width)))
    pack = jnp.concatenate(
        [stretch_query.reshape(stretch_rows, query_width), new_query, decode_kv], axis=0
    )
    every, order = broadcast_over_seq(pack, seq_rank, seq_count)
    decode_rows = jnp.take(every[:, stretch_rows:, :], order, axis=0)
    every_query = decode_rows[:, :local_dec, :].reshape(total_dec, query_width)
    every_kv = decode_rows[:, local_dec:, :].reshape(total_dec, query_width)
    every_key = every_kv[:, :key_width]
    every_value = every_kv[:, key_width : 2 * key_width]
    slot_ids = seq_rank * local_dec + jnp.arange(local_dec, dtype=jnp.int32)
    arrival_ids = jnp.arange(total_dec, dtype=jnp.int32)
    sources = jnp.sum(
        jnp.where(dealing[None, :] == slot_ids[:, None], arrival_ids[None, :], 0), axis=1
    )
    home_query = jnp.take(every_query, sources, axis=0)
    home_key = jnp.take(every_key, sources, axis=0)
    home_value = jnp.take(every_value, sources, axis=0)
    cache_span = cache_keys.shape[1]
    cache_pos = jnp.arange(cache_span, dtype=jnp.int32)

    def decode_slot(query_row, own_key, own_value, cached_keys, cached_values, length):
        key_all = jnp.concatenate([cached_keys, own_key[None, :]], axis=0)
        value_all = jnp.concatenate([cached_values, own_value[None, :]], axis=0)
        visible = jnp.concatenate([cache_pos < length, jnp.ones((1,), dtype=jnp.bool_)])
        visible = jnp.broadcast_to(visible[None, :], (group_size, cache_span + 1))
        row_top, weight_sum, numerator = partial_attend(
            query_row.reshape(group_size, head_size), key_all, value_all, visible
        )
        return (
            (numerator / weight_sum[:, None]).astype(jnp.bfloat16).reshape(group_size * head_size)
        )

    home_out = jax.vmap(decode_slot)(
        home_query, home_key, home_value, cache_keys, cache_values, cache_length
    )
    all_out = lax.all_to_all(
        jnp.broadcast_to(home_out[None], (seq_count,) + home_out.shape), "seq", 0, 0, tiled=True
    ).reshape(total_dec, group_size * head_size)
    arrival_out = jnp.take(all_out, dealing, axis=0)
    arrival_terms = jnp.dot(arrival_out, out_weight, preferred_element_type=jnp.float32)
    decode_mixed = lax.psum_scatter(arrival_terms, "tp", scatter_dimension=0, tiled=True).astype(
        jnp.bfloat16
    )

    prior_span = prior_keys.shape[1]
    direct = local_tok % 16 == 0
    stat_count = 3 * stretch_count * local_tok * group_size
    stat_rows = -(-stat_count // query_width)
    out_rows = stretch_rows
    limits = jnp.clip(stretch_start - seq_rank * prior_span, 0, prior_span).astype(jnp.int32)
    info = jnp.concatenate([limits, (seq_rank * local_tok).astype(jnp.int32)[None]])
    if direct:
        payload, part_lse = prefill_partial(
            info, order, every, prior_keys, prior_values, stretch_key, stretch_value, group_size,
            local_tok, local_tok, out_rows + stat_rows,
        )
    else:
        token_count = seq_count * local_tok
        queries_all = (
            jnp.take(every, order, axis=0)[:, :stretch_rows, :]
            .reshape(seq_count, stretch_count, local_tok, query_width)
            .transpose(1, 0, 2, 3)
            .reshape(1, stretch_rows * seq_count, query_width)
        )
        flat_out, part_lse = prefill_partial(
            info, jnp.zeros((1,), jnp.int32), queries_all, prior_keys, prior_values, stretch_key, stretch_value, group_size,
            token_count, token_count, stretch_rows * seq_count,
        )
        payload = jnp.pad(
            flat_out.reshape(stretch_count, seq_count, local_tok, query_width)
            .transpose(1, 0, 2, 3)
            .reshape(seq_count, out_rows, query_width),
            ((0, 0), (0, stat_rows), (0, 0)),
        )
    if not direct:
        part_lse = part_lse.reshape(stretch_count, seq_count, local_tok, group_size).transpose(
            1, 0, 2, 3
        )
    lse_hi = lax.reduce_precision(part_lse, exponent_bits=8, mantissa_bits=7)
    lse_rest = part_lse - lse_hi
    lse_mid = lax.reduce_precision(lse_rest, exponent_bits=8, mantissa_bits=7)
    lse_lo = lse_rest - lse_mid
    stats = jnp.stack([lse_hi, lse_mid, lse_lo], axis=1).reshape(seq_count, stat_count)
    stats = jnp.pad(stats, ((0, 0), (0, stat_rows * query_width - stat_count)))
    payload = lax.dynamic_update_slice(
        payload,
        stats.astype(jnp.bfloat16).reshape(seq_count, stat_rows, query_width),
        (0, out_rows, 0),
    )

    received = lax.all_to_all(payload, "seq", 0, 0, tiled=True)
    got_stats = (
        received[:, out_rows:, :]
        .reshape(seq_count, stat_rows * query_width)[:, :stat_count]
        .astype(jnp.float32)
        .reshape(seq_count, 3, stretch_count, local_tok, group_size)
    )
    got_lse = (got_stats[:, 0] + got_stats[:, 1]) + got_stats[:, 2]
    stretch_out = combine_partials(received, got_lse, group_size, head_size)
    return (decode_mixed, stretch_out)


def solution(mesh):
    return jax.shard_map(
        body,
        mesh=mesh,
        in_specs=(
            P("seq", "tp"),
            P("seq", "tp"),
            P("seq", "tp"),
            P("seq", None, "tp"),
            P("seq", None, "tp"),
            P("seq"),
            P(),
            P("tp", "seq"),
            P(None, "seq", "tp"),
            P(None, "seq", "tp"),
            P(None, "seq", "tp"),
            P(None, "seq", "tp"),
            P(None, "seq", "tp"),
            P(),
        ),
        out_specs=(P("tp", "seq"), P(None, "seq", "tp")),
        check_vma=False,
    )
```

```python
import functools
import math

import jax
import jax.numpy as jnp
from jax import lax
from jax.experimental import pallas as pl
from jax.experimental.pallas import tpu as pltpu
from jax.sharding import PartitionSpec as P

NEG_FILL = -1e30


def partial_attend(queries, keys, values, visible):
    factor = 1.0 / math.sqrt(queries.shape[-1])
    scores = jnp.dot(queries, keys.T, preferred_element_type=jnp.float32) * factor
    scores = jnp.where(visible, scores, NEG_FILL)
    row_top = jnp.max(scores, axis=1)
    weights = jnp.where(visible, jnp.exp(scores - row_top[:, None]), 0.0)
    weight_sum = jnp.sum(weights, axis=1)
    numerator = jnp.dot(weights.astype(jnp.bfloat16), values, preferred_element_type=jnp.float32)
    return (row_top, weight_sum, numerator)


def _prefill_kernel(
    info_ref, order_ref, q_hbm, k_ref, v_ref, sk_ref, sv_ref, o_ref, lse_ref, q_ref, sems,
    *, group_size, head_size, local_tok
):
    c = pl.program_id(0)
    stretch_count, src_count, tok_block, _ = q_ref.shape

    def query_copy(stretch, src):
        return pltpu.make_async_copy(
            q_hbm.at[order_ref[src], pl.ds(stretch * tok_block, tok_block)],
            q_ref.at[stretch, src],
            sems.at[stretch, src],
        )

    @pl.when(c == 0)
    def _():
        for src in range(src_count):
            query_copy(0, src).start()

    for src in range(src_count):
        query_copy(c, src).wait()

    @pl.when(c == 0)
    def _():
        for stretch in range(1, stretch_count):
            for src in range(src_count):
                query_copy(stretch, src).start()
    limit = info_ref[c]
    key_offset = info_ref[info_ref.shape[0] - 1]
    keys = k_ref[0]
    values = v_ref[0]
    own_keys = sk_ref[0]
    own_values = sv_ref[0]
    factor = 1.0 / math.sqrt(head_size)
    tokens = src_count * tok_block
    col = lax.broadcasted_iota(jnp.int32, (1, keys.shape[0]), 1)
    visible = col < limit
    key_token = key_offset + lax.broadcasted_iota(jnp.int32, (tokens, own_keys.shape[0]), 1)
    row = lax.broadcasted_iota(jnp.int32, (tokens, own_keys.shape[0]), 0)
    query_token = (row // tok_block) * local_tok + row % tok_block
    causal = key_token <= query_token
    dims = (((1,), (1,)), ((), ()))
    for h in range(group_size):
        q = q_ref[c, :, :, h * head_size : (h + 1) * head_size].reshape(tokens, head_size)
        s = lax.dot_general(q, keys, dims, preferred_element_type=jnp.float32) * factor
        s = jnp.where(visible, s, NEG_FILL)
        s_own = lax.dot_general(q, own_keys, dims, preferred_element_type=jnp.float32) * factor
        s_own = jnp.where(causal, s_own, NEG_FILL)
        m = jnp.maximum(
            jnp.max(s, axis=1, keepdims=True), jnp.max(s_own, axis=1, keepdims=True)
        )
        w = jnp.exp(s - m)
        w_own = jnp.exp(s_own - m)
        empty = m < 0.5 * NEG_FILL
        l = jnp.sum(w, axis=1, keepdims=True) + jnp.sum(w_own, axis=1, keepdims=True)
        num = jnp.dot(w.astype(jnp.bfloat16), values, preferred_element_type=jnp.float32)
        num = num + jnp.dot(
            w_own.astype(jnp.bfloat16), own_values, preferred_element_type=jnp.float32
        )
        l = jnp.where(empty, 0.0, l)
        num = jnp.where(empty, 0.0, num)
        safe = jnp.maximum(l, 1.0)
        o_ref[:, :, h * head_size : (h + 1) * head_size] = (
            (num / safe).astype(o_ref.dtype).reshape(src_count, tok_block, head_size)
        )
        lse_ref[:, 0, :, h : h + 1] = (m + jnp.log(safe)).reshape(src_count, tok_block, 1)


def prefill_partial(
    info, order, queries, keys, values, own_keys, own_values, group_size, tok_block, local_tok,
    out_rows,
):
    src_count = order.shape[0]
    qw = queries.shape[2]
    n, p, hd = keys.shape
    own = own_keys.shape[1]
    tokens = src_count * tok_block
    kern = functools.partial(
        _prefill_kernel, group_size=group_size, head_size=hd, local_tok=local_tok
    )
    return pl.pallas_call(
        kern,
        grid_spec=pltpu.PrefetchScalarGridSpec(
            num_scalar_prefetch=2,
            grid=(n,),
            in_specs=[
                pl.BlockSpec(memory_space=pl.ANY),
                pl.BlockSpec((1, p, hd), lambda c, info, order: (c, 0, 0)),
                pl.BlockSpec((1, p, hd), lambda c, info, order: (c, 0, 0)),
                pl.BlockSpec((1, own, hd), lambda c, info, order: (c, 0, 0)),
                pl.BlockSpec((1, own, hd), lambda c, info, order: (c, 0, 0)),
            ],
            out_specs=[
                pl.BlockSpec((src_count, tok_block, qw), lambda c, info, order: (0, c, 0)),
                pl.BlockSpec(
                    (src_count, 1, tok_block, group_size), lambda c, info, order: (0, c, 0, 0)
                ),
            ],
            scratch_shapes=[
                pltpu.VMEM((n, src_count, tok_block, qw), jnp.bfloat16),
                pltpu.SemaphoreType.DMA((n, src_count)),
            ],
        ),
        out_shape=[
            jax.ShapeDtypeStruct((src_count, out_rows, qw), jnp.bfloat16),
            jax.ShapeDtypeStruct((src_count, n, tok_block, group_size), jnp.float32),
        ],
    )(info, order, queries, keys, values, own_keys, own_values)


def _combine_kernel(o_ref, lse_ref, out_ref, *, group_size, head_size):
    stretch_count, local_tok, _ = out_ref.shape
    for c in range(stretch_count):
        lse = lse_ref[:, c]
        top = jnp.max(lse, axis=0, keepdims=True)
        weights = jnp.exp(lse - top)
        total = jnp.sum(weights, axis=0)
        for h in range(group_size):
            part = o_ref[
                :, c * local_tok : (c + 1) * local_tok, h * head_size : (h + 1) * head_size
            ].astype(jnp.float32)
            num = jnp.sum(part * weights[:, :, h : h + 1], axis=0)
            out_ref[c, :, h * head_size : (h + 1) * head_size] = (
                num / total[:, h : h + 1]
            ).astype(out_ref.dtype)


def combine_partials(received, lse, group_size, head_size):
    _, stretch_count, local_tok, _ = lse.shape
    kern = functools.partial(_combine_kernel, group_size=group_size, head_size=head_size)
    return pl.pallas_call(
        kern,
        out_shape=jax.ShapeDtypeStruct(
            (stretch_count, local_tok, group_size * head_size), jnp.bfloat16
        ),
    )(received, lse)


def broadcast_over_seq(pack, seq_rank, seq_count):
    if seq_count > 16 or seq_count % 2:
        every = lax.all_to_all(
            jnp.broadcast_to(pack[None], (seq_count,) + pack.shape), "seq", 0, 0, tiled=True
        )
        return every, jnp.arange(seq_count, dtype=jnp.int32)
    half = seq_count // 2
    partner = lax.ppermute(pack, "seq", [(i, (i + half) % seq_count) for i in range(seq_count)])
    perms = [
        [(i, (i // half) * half + (i % half + shift) % half) for i in range(seq_count)]
        for shift in range(1, half)
    ]
    near_pieces = [lax.ppermute(pack, "seq", perm) for perm in perms]
    far_pieces = [lax.ppermute(partner, "seq", perm) for perm in perms]
    every = jnp.stack([pack, partner] + near_pieces + far_pieces)
    sources = jnp.arange(seq_count, dtype=jnp.int32)
    far = (sources // half) != (seq_rank // half)
    near = jnp.where(far, (sources + half) % seq_count, sources)
    shift_of = (seq_rank % half - near % half) % half
    order = jnp.where(
        far,
        jnp.where(shift_of == 0, 1, half + shift_of),
        jnp.where(shift_of == 0, 0, 1 + shift_of),
    )
    return every, order.astype(jnp.int32)


def body(
    new_query,
    new_key,
    new_value,
    cache_keys,
    cache_values,
    cache_length,
    dealing,
    out_weight,
    stretch_query,
    stretch_key,
    stretch_value,
    prior_keys,
    prior_values,
    stretch_start,
):
    head_size = cache_keys.shape[2]
    group_size = new_query.shape[1] // head_size
    local_dec = new_query.shape[0]
    seq_rank = lax.axis_index("seq")
    seq_count = lax.axis_size("seq")
    total_dec = local_dec * seq_count
    stretch_count, local_tok, query_width = stretch_query.shape
    key_width = stretch_key.shape[2]
    stretch_rows = stretch_count * local_tok

    decode_kv = jnp.concatenate([new_key, new_value], axis=1)
    decode_kv = jnp.pad(decode_kv, ((0, 0), (0, query_width - 2 * key_width)))
    pack = jnp.concatenate(
        [stretch_query.reshape(stretch_rows, query_width), new_query, decode_kv], axis=0
    )
    every, order = broadcast_over_seq(pack, seq_rank, seq_count)
    decode_rows = jnp.take(every[:, stretch_rows:, :], order, axis=0)
    every_query = decode_rows[:, :local_dec, :].reshape(total_dec, query_width)
    every_kv = decode_rows[:, local_dec:, :].reshape(total_dec, query_width)
    every_key = every_kv[:, :key_width]
    every_value = every_kv[:, key_width : 2 * key_width]
    slot_ids = seq_rank * local_dec + jnp.arange(local_dec, dtype=jnp.int32)
    arrival_ids = jnp.arange(total_dec, dtype=jnp.int32)
    sources = jnp.sum(
        jnp.where(dealing[None, :] == slot_ids[:, None], arrival_ids[None, :], 0), axis=1
    )
    home_query = jnp.take(every_query, sources, axis=0)
    home_key = jnp.take(every_key, sources, axis=0)
    home_value = jnp.take(every_value, sources, axis=0)
    cache_span = cache_keys.shape[1]
    cache_pos = jnp.arange(cache_span, dtype=jnp.int32)

    def decode_slot(query_row, own_key, own_value, cached_keys, cached_values, length):
        key_all = jnp.concatenate([cached_keys, own_key[None, :]], axis=0)
        value_all = jnp.concatenate([cached_values, own_value[None, :]], axis=0)
        visible = jnp.concatenate([cache_pos < length, jnp.ones((1,), dtype=jnp.bool_)])
        visible = jnp.broadcast_to(visible[None, :], (group_size, cache_span + 1))
        row_top, weight_sum, numerator = partial_attend(
            query_row.reshape(group_size, head_size), key_all, value_all, visible
        )
        return (
            (numerator / weight_sum[:, None]).astype(jnp.bfloat16).reshape(group_size * head_size)
        )

    home_out = jax.vmap(decode_slot)(
        home_query, home_key, home_value, cache_keys, cache_values, cache_length
    )
    all_out = lax.all_to_all(
        jnp.broadcast_to(home_out[None], (seq_count,) + home_out.shape), "seq", 0, 0, tiled=True
    ).reshape(total_dec, group_size * head_size)
    arrival_out = jnp.take(all_out, dealing, axis=0)
    arrival_terms = jnp.dot(arrival_out, out_weight, preferred_element_type=jnp.float32)
    decode_mixed = lax.psum_scatter(arrival_terms, "tp", scatter_dimension=0, tiled=True).astype(
        jnp.bfloat16
    )

    prior_span = prior_keys.shape[1]
    direct = local_tok % 16 == 0
    stat_count = 3 * stretch_count * local_tok * group_size
    stat_rows = -(-stat_count // query_width)
    out_rows = stretch_rows
    limits = jnp.clip(stretch_start - seq_rank * prior_span, 0, prior_span).astype(jnp.int32)
    info = jnp.concatenate([limits, (seq_rank * local_tok).astype(jnp.int32)[None]])
    if direct:
        payload, part_lse = prefill_partial(
            info, order, every, prior_keys, prior_values, stretch_key, stretch_value, group_size,
            local_tok, local_tok, out_rows + stat_rows,
        )
    else:
        token_count = seq_count * local_tok
        queries_all = (
            jnp.take(every, order, axis=0)[:, :stretch_rows, :]
            .reshape(seq_count, stretch_count, local_tok, query_width)
            .transpose(1, 0, 2, 3)
            .reshape(1, stretch_rows * seq_count, query_width)
        )
        flat_out, part_lse = prefill_partial(
            info, jnp.zeros((1,), jnp.int32), queries_all, prior_keys, prior_values, stretch_key, stretch_value, group_size,
            token_count, token_count, stretch_rows * seq_count,
        )
        payload = jnp.pad(
            flat_out.reshape(stretch_count, seq_count, local_tok, query_width)
            .transpose(1, 0, 2, 3)
            .reshape(seq_count, out_rows, query_width),
            ((0, 0), (0, stat_rows), (0, 0)),
        )
    if not direct:
        part_lse = part_lse.reshape(stretch_count, seq_count, local_tok, group_size).transpose(
            1, 0, 2, 3
        )
    lse_hi = lax.reduce_precision(part_lse, exponent_bits=8, mantissa_bits=7)
    lse_rest = part_lse - lse_hi
    lse_mid = lax.reduce_precision(lse_rest, exponent_bits=8, mantissa_bits=7)
    lse_lo = lse_rest - lse_mid
    stats = jnp.stack([lse_hi, lse_mid, lse_lo], axis=1).reshape(seq_count, stat_count)
    stats = jnp.pad(stats, ((0, 0), (0, stat_rows * query_width - stat_count)))
    payload = lax.dynamic_update_slice(
        payload,
        stats.astype(jnp.bfloat16).reshape(seq_count, stat_rows, query_width),
        (0, out_rows, 0),
    )

    received = lax.all_to_all(payload, "seq", 0, 0, tiled=True)
    got_stats = (
        received[:, out_rows:, :]
        .reshape(seq_count, stat_rows * query_width)[:, :stat_count]
        .astype(jnp.float32)
        .reshape(seq_count, 3, stretch_count, local_tok, group_size)
    )
    got_lse = (got_stats[:, 0] + got_stats[:, 1]) + got_stats[:, 2]
    stretch_out = combine_partials(received, got_lse, group_size, head_size)
    return (decode_mixed, stretch_out)


def solution(mesh):
    return jax.shard_map(
        body,
        mesh=mesh,
        in_specs=(
            P("seq", "tp"),
            P("seq", "tp"),
            P("seq", "tp"),
            P("seq", None, "tp"),
            P("seq", None, "tp"),
            P("seq"),
            P(),
            P("tp", "seq"),
            P(None, "seq", "tp"),
            P(None, "seq", "tp"),
            P(None, "seq", "tp"),
            P(None, "seq", "tp"),
            P(None, "seq", "tp"),
            P(),
        ),
        out_specs=(P("tp", "seq"), P(None, "seq", "tp")),
        check_vma=False,
    )
```
